32 devices in a mesh: section: 4 (over y, core), seq: 8 (over z, x).
Axes of the slice: x: 2, y: 2, z: 4, core: 2. Of those that a mesh axis runs over, the one named last changes fastest.
Arguments:
- queries: bfloat16 [4, 2048, 4096], P('section', 'seq'), may hold values from -42 to 42
- keys: bfloat16 [4, 2048, 512], P('section', 'seq'), may hold values from -6 to 6
- values: bfloat16 [4, 2048, 512], P('section', 'seq'), may hold values from -6 to 6
- out_grads: bfloat16 [4, 2048, 4096], P('section', 'seq'), may hold values from -6 to 6
- random_blocks: int32 [4, 32, 3], P('section'), may hold values from 0 to 31, as said below
- global_blocks: int32 [4, 2], P('section'), may hold values from 0 to 31, as said below
- pad_lengths: int32 [4, 8], P('section'), may hold values from 0 to 63, as said below
Outputs:
- passed_query_grad: bfloat16 [4, 2048, 4096], P('section', 'seq')
- passed_key_grad: bfloat16 [4, 2048, 512], P('section', 'seq')
- passed_value_grad: bfloat16 [4, 2048, 512], P('section', 'seq')
The draws below stay inside these ranges and needn't reach their ends.
Inputs may be any that keep to these rules, and one draw needn't show every extreme that they name: `random_blocks`: over the 12 random blocks named by one shard's query blocks, the blocks of any one shard are named at most 2 times, and on every shard some shard's blocks exactly 2 times; within one random slot (one column) at most 1 times, and exactly 1 times for some shard. `global_blocks`: the 2 global blocks of a section are distinct. `pad_lengths`: every section has a shard with exactly 63 padding tokens.
All inputs are finite; a program needn't handle non-finite values.
Results may differ from the reference program's by a relative error of at most 0.007.
Values may be sent and summed in bfloat16 or wider, within the bound.
No kernel may reach another device: no remote copies, remote signals or barrier semaphores. Data moves between devices by JAX's collectives and lax.ppermute only.
A program may use at most 128 MiB of HBM per device.

```python
import math
import jax
import jax.numpy as jnp
from jax import lax

QHEADS = 32
KVHEADS = 4
HDIM = 128
BLK = 64
GLOB = 2
RAND = 3
TOK_DEV = 256
SECTIONS = 4
SHARDS = 8
TOKENS = 2048
QBLK = 4
NBLK = 32
QW = 4096
KW = 512


def query_key_pair(key):
    base = jax.random.fold_in(key, 7)
    query_seed, key_seed = jax.random.split(base)
    query_draw = jnp.clip(jax.random.normal(query_seed, (SECTIONS, TOKENS, QW), jnp.float32), -6.0, 6.0)
    key_draw = jnp.clip(jax.random.normal(key_seed, (SECTIONS, TOKENS, KW), jnp.float32), -6.0, 6.0)
    return (query_draw, key_draw)


def draw_queries(key, part):
    return query_key_pair(key)[0].astype(jnp.bfloat16)


def draw_keys(key, part):
    return query_key_pair(key)[1].astype(jnp.bfloat16)


def draw_random_blocks(key, part):
    perm_seed, local_seed = jax.random.split(jax.random.fold_in(key, 11))
    perm_seeds = jax.random.split(perm_seed, SECTIONS * SHARDS)
    orders = jax.vmap(lambda one_seed: jax.random.permutation(one_seed, SHARDS))(perm_seeds).reshape(SECTIONS, SHARDS, SHARDS)
    request = jnp.arange(QBLK)[:, None] + QBLK * jnp.arange(RAND)[None, :]
    owners = orders[:, :, request % SHARDS]
    local_blocks = jax.random.randint(local_seed, (SECTIONS, SHARDS, QBLK, RAND), 0, QBLK)
    return (owners * QBLK + local_blocks).reshape(SECTIONS, NBLK, RAND).astype(jnp.int32)


def draw_global_blocks(key, part):
    section_seeds = jax.random.split(jax.random.fold_in(key, 13), SECTIONS)
    return jax.vmap(lambda one_seed: jax.random.permutation(one_seed, NBLK)[:GLOB])(section_seeds).astype(jnp.int32)


def draw_pad_lengths(key, part):
    size_seed, pick_seed = jax.random.split(jax.random.fold_in(key, 17))
    sizes_drawn = jax.random.randint(size_seed, (SECTIONS, SHARDS), 0, BLK)
    fullest = jax.random.randint(pick_seed, (SECTIONS,), 0, SHARDS)
    return sizes_drawn.at[jnp.arange(SECTIONS), fullest].set(BLK - 1).astype(jnp.int32)


def shard_levels(own_key, extent, pieces, least, high):
    factor_of, own = 1.0, jax.random.fold_in(own_key, 6)
    for axis_at, shards_of in pieces:
        heights = jnp.exp(jax.random.uniform(jax.random.fold_in(own, axis_at), (shards_of,), jnp.float32, least / len(pieces), high / len(pieces)))
        factor_of = factor_of * jnp.repeat(heights, extent[axis_at] // shards_of).reshape([-1 if axis == axis_at else 1 for axis in range(len(extent))])
    return factor_of


def gaussian(stream_key, dims, spread, reach, shards=(), kind=jnp.bfloat16):
    gain = shard_levels(stream_key, dims, shards, -0.22, 0.18) if shards else 1.0
    values = jax.random.normal(stream_key, dims, jnp.float32) * spread * gain
    return jnp.minimum(jnp.maximum(values, -reach), reach).astype(kind)


def setup_inputs(seed: int = 0) -> dict:
    key_of = jax.random.split(jax.random.key(seed), 8)
    return {
        "queries": draw_queries(jax.random.fold_in(key_of[7], 71), 0),
        "keys": draw_keys(jax.random.fold_in(key_of[7], 71), 0),
        "values": gaussian(key_of[2], (SECTIONS, TOKENS, KW), 1.0, 6.0, ((0, 4), (1, 8))),
        "out_grads": gaussian(key_of[3], (SECTIONS, TOKENS, QW), 1.0, 6.0, ((0, 4), (1, 8))),
        "random_blocks": draw_random_blocks(jax.random.fold_in(key_of[7], 71), 0),
        "global_blocks": draw_global_blocks(jax.random.fold_in(key_of[7], 71), 0),
        "pad_lengths": draw_pad_lengths(jax.random.fold_in(key_of[7], 71), 0),
    }


def lowered(source):
    return lax.optimization_barrier(source.astype(jnp.bfloat16)).astype(jnp.float32)

def block_backward(query_rows, grad_rows, key_tiles, value_tiles, key_live):
    nblocks = query_rows.shape[0]
    ntiles = key_tiles.shape[1]
    group = QHEADS // KVHEADS
    score_scale = 1.0 / math.sqrt(HDIM)
    query_five = query_rows.astype(jnp.float32).reshape(nblocks, BLK, KVHEADS, group, HDIM)
    grad_five = grad_rows.astype(jnp.float32).reshape(nblocks, BLK, KVHEADS, group, HDIM)
    key_five = key_tiles.astype(jnp.float32).reshape(nblocks, ntiles, BLK, KVHEADS, HDIM)
    value_five = value_tiles.astype(jnp.float32).reshape(nblocks, ntiles, BLK, KVHEADS, HDIM)
    scores = jnp.einsum('bqhgd,btkhd->bhgqtk', query_five, key_five) * score_scale
    scores = jnp.where(key_live[:, None, None, None, :, :], scores, -1e+30)
    row_max = lax.optimization_barrier(jnp.max(scores, axis=(4, 5), keepdims=True))
    log_total = row_max + jnp.log(lax.optimization_barrier(jnp.sum(jnp.exp(scores - row_max), axis=(4, 5), keepdims=True)))
    probs = jnp.exp(scores - log_total)
    probs_low = lowered(probs)
    output = jnp.einsum('bhgqtk,btkhd->bqhgd', probs_low, value_five)
    row_dot = lax.optimization_barrier(jnp.sum(grad_five * output, axis=-1))
    prob_grad = jnp.einsum('bqhgd,btkhd->bhgqtk', grad_five, value_five)
    score_grad = lowered(probs * (prob_grad - jnp.transpose(row_dot, (0, 2, 3, 1))[:, :, :, :, None, None]))
    query_grad = jnp.einsum('bhgqtk,btkhd->bqhgd', score_grad, key_five) * score_scale
    key_grad = jnp.einsum('bhgqtk,bqhgd->btkhd', score_grad, query_five) * score_scale
    value_grad = jnp.einsum('bhgqtk,bqhgd->btkhd', probs_low, grad_five)
    return (query_grad.reshape(nblocks, BLK, QW), key_grad.reshape(nblocks, ntiles, BLK, KW), value_grad.reshape(nblocks, ntiles, BLK, KW))

def section_backward(queries, keys, values, out_grads, random_blocks, global_blocks, pad_lengths):
    ntiles = 3 + GLOB + RAND
    near = 3 + GLOB
    block_ids = jnp.arange(NBLK, dtype=jnp.int32)
    window_ids = block_ids[:, None] + jnp.arange(-1, 2, dtype=jnp.int32)[None, :]
    tile_ids = jnp.concatenate([window_ids, jnp.broadcast_to(global_blocks[None, :], (NBLK, GLOB)), random_blocks], axis=1)
    valid = (tile_ids >= 0) & (tile_ids < NBLK)
    safe_ids = jnp.clip(tile_ids, 0, NBLK - 1).astype(jnp.int32)
    owner_shard = safe_ids // QBLK
    within = (safe_ids % QBLK)[:, :, None] * BLK + jnp.arange(BLK, dtype=jnp.int32)[None, None, :]
    key_live = valid[:, :, None] & (within < (TOK_DEV - pad_lengths[owner_shard])[:, :, None])
    key_blocks = keys.reshape(NBLK, BLK, KW)
    value_blocks = values.reshape(NBLK, BLK, KW)

    def group_step(carry, inputs):
        key_sum, value_sum = carry
        query_rows, grad_rows, group_ids, group_live = inputs
        query_grad, key_grad, value_grad = block_backward(query_rows, grad_rows, key_blocks[group_ids], value_blocks[group_ids], group_live)
        key_grad = jnp.concatenate([key_grad[:, :near], lowered(key_grad[:, near:])], axis=1)
        value_grad = jnp.concatenate([value_grad[:, :near], lowered(value_grad[:, near:])], axis=1)
        flat_ids = group_ids.reshape(-1)
        key_sum = key_sum.at[flat_ids].add(key_grad.reshape(-1, BLK, KW))
        value_sum = value_sum.at[flat_ids].add(value_grad.reshape(-1, BLK, KW))
        return ((key_sum, value_sum), query_grad)
    inputs = (queries.reshape(SHARDS, QBLK, BLK, QW), out_grads.reshape(SHARDS, QBLK, BLK, QW), safe_ids.reshape(SHARDS, QBLK, ntiles), key_live.reshape(SHARDS, QBLK, ntiles, BLK))
    zeros = jnp.zeros((NBLK, BLK, KW), jnp.float32)
    (key_sum, value_sum), query_grads = lax.scan(group_step, (zeros, zeros), inputs)
    return (query_grads.reshape(TOKENS, QW).astype(jnp.bfloat16), key_sum.reshape(TOKENS, KW).astype(jnp.bfloat16), value_sum.reshape(TOKENS, KW).astype(jnp.bfloat16))

def reference(queries, keys, values, out_grads, random_blocks, global_blocks, pad_lengths):
    query_list = []
    key_list = []
    value_list = []
    for section_num in range(SECTIONS):
        query_grad, key_grad, value_grad = section_backward(queries[section_num], keys[section_num], values[section_num], out_grads[section_num], random_blocks[section_num], global_blocks[section_num], pad_lengths[section_num])
        query_list.append(query_grad)
        key_list.append(key_grad)
        value_list.append(value_grad)
    return (jnp.roll(jnp.stack(query_list), -1, axis=0), jnp.roll(jnp.stack(key_list), -1, axis=0), jnp.roll(jnp.stack(value_list), -1, axis=0))
```

```python
import math

import jax
import jax.numpy as jnp
from jax import lax
from jax.experimental import pallas as pl
from jax.sharding import PartitionSpec as P

HDIM = 128
BLK = 64
GLOB = 2
RAND = 3


def extended_2(array, sides, width):
    for axis, dim in sides:
        devices, length = (lax.axis_size(axis), array.shape[dim])
        up = [(i, (i + 1) % devices) for i in range(devices - 1)]
        down = [(j, i) for i, j in up]
        last = lax.slice_in_dim(array, length - width, length, axis=dim)
        leading = lax.slice_in_dim(array, 0, width, axis=dim)
        before = lax.ppermute(last, axis, up)
        after = lax.ppermute(leading, axis, down)
        array = jnp.concatenate([before, array, after], axis=dim)
    return array


def broadcast(array, axis, root):
    mine = lax.axis_index(axis) == root
    return lax.psum(jnp.where(mine, array, jnp.zeros_like(array)), axis)


def from_behind(block, axis, distance):
    devices = range(lax.axis_size(axis))
    route = [((i - distance) % len(devices), i) for i in devices]
    return lax.ppermute(block, axis, route)


def attention_kernel(q_ref, g_ref, k_ref, v_ref, live_ref, dq_ref, dk_ref, dv_ref):
    block_len, width = q_ref.shape
    group = width // HDIM
    ntiles = k_ref.shape[0]
    score_scale = 1.0 / math.sqrt(HDIM)
    query = q_ref[...]
    grad = g_ref[...]
    query_rows = jnp.concatenate(
        [query[:, g * HDIM : (g + 1) * HDIM] for g in range(group)], axis=0
    )
    grad_rows = jnp.concatenate([grad[:, g * HDIM : (g + 1) * HDIM] for g in range(group)], axis=0)
    key_rows = k_ref[...].reshape(ntiles * block_len, HDIM)
    value_rows = v_ref[...].reshape(ntiles * block_len, HDIM)
    live = live_ref[...] > 0.5
    contract_last = (((1,), (1,)), ((), ()))
    contract_first = (((0,), (0,)), ((), ()))
    scores = (
        lax.dot_general(query_rows, key_rows, contract_last, preferred_element_type=jnp.float32)
        * score_scale
    )
    scores = jnp.where(live, scores, -1e30)
    row_max = jnp.max(scores, axis=1, keepdims=True)
    shifted = jnp.exp(scores - row_max)
    total = jnp.sum(shifted, axis=1, keepdims=True)
    probs = shifted * (1.0 / total)
    probs_low = probs.astype(jnp.bfloat16)
    output = jnp.dot(probs_low, value_rows, preferred_element_type=jnp.float32)
    row_dot = jnp.sum(grad_rows.astype(jnp.float32) * output, axis=1, keepdims=True)
    prob_grad = lax.dot_general(
        grad_rows, value_rows, contract_last, preferred_element_type=jnp.float32
    )
    score_grad = (probs * (prob_grad - row_dot)).astype(jnp.bfloat16)
    query_grad = jnp.dot(score_grad, key_rows, preferred_element_type=jnp.float32) * score_scale
    key_grad = (
        lax.dot_general(score_grad, query_rows, contract_first, preferred_element_type=jnp.float32)
        * score_scale
    )
    value_grad = lax.dot_general(
        probs_low, grad_rows, contract_first, preferred_element_type=jnp.float32
    )
    for g in range(group):
        dq_ref[:, g * HDIM : (g + 1) * HDIM] = query_grad[g * block_len : (g + 1) * block_len].astype(
            dq_ref.dtype
        )
    dk_ref[...] = key_grad.reshape(ntiles, block_len, HDIM)
    dv_ref[...] = value_grad.reshape(ntiles, block_len, HDIM)


def block_backward(query_rows, grad_rows, key_tiles, value_tiles, key_live):
    nblocks, block_len, qwidth = query_rows.shape
    ntiles = key_tiles.shape[1]
    kwidth = key_tiles.shape[-1]
    heads_kv = kwidth // HDIM
    group_width = qwidth // heads_kv
    live = key_live.reshape(nblocks, 1, ntiles * block_len).astype(jnp.float32)
    row_spec = pl.BlockSpec((block_len, group_width), lambda b, h: (b, h))
    tile_spec = pl.BlockSpec((None, ntiles, block_len, HDIM), lambda b, h: (b, 0, 0, h))
    live_spec = pl.BlockSpec((None, 1, ntiles * block_len), lambda b, h: (b, 0, 0))
    flops = 12 * nblocks * heads_kv * (group_width // HDIM) * block_len * ntiles * block_len * HDIM
    query_grad, key_grad, value_grad = pl.pallas_call(
        attention_kernel,
        grid=(nblocks, heads_kv),
        in_specs=[row_spec, row_spec, tile_spec, tile_spec, live_spec],
        out_specs=[row_spec, tile_spec, tile_spec],
        out_shape=[
            jax.ShapeDtypeStruct((nblocks * block_len, qwidth), jnp.bfloat16),
            jax.ShapeDtypeStruct((nblocks, ntiles, block_len, kwidth), jnp.float32),
            jax.ShapeDtypeStruct((nblocks, ntiles, block_len, kwidth), jnp.float32),
        ],
        cost_estimate=pl.CostEstimate(
            flops=flops,
            transcendentals=nblocks * qwidth // HDIM * block_len * ntiles * block_len,
            bytes_accessed=nblocks * block_len * qwidth * 6 + nblocks * ntiles * block_len * kwidth * 12,
        ),
    )(
        query_rows.reshape(nblocks * block_len, qwidth),
        grad_rows.reshape(nblocks * block_len, qwidth),
        key_tiles,
        value_tiles,
        live,
    )
    return (query_grad, key_grad, value_grad)


def request_plan(request_lists, this_shard, query_blocks):
    shards, count = request_lists.shape
    capacity = -(-count // shards)
    owner_ids = request_lists // query_blocks
    local_ids = request_lists % query_blocks
    order = jnp.arange(count, dtype=jnp.int32)
    earlier = order[None, :] < order[:, None]
    same_owner = owner_ids[:, :, None] == owner_ids[:, None, :]
    slot_rank = jnp.sum(same_owner & earlier[None], axis=2)
    slot_ids = jnp.arange(capacity, dtype=jnp.int32)
    chosen = (owner_ids[:, None, :] == this_shard) & (
        slot_rank[:, None, :] == slot_ids[None, :, None]
    )
    serve_block = jnp.sum(jnp.where(chosen, local_ids[:, None, :], 0), axis=2)
    slot_used = jnp.any(chosen, axis=2)
    owner_mine = lax.dynamic_index_in_dim(owner_ids, this_shard, 0, keepdims=False)
    rank_mine = lax.dynamic_index_in_dim(slot_rank, this_shard, 0, keepdims=False)
    return (serve_block, slot_used, owner_mine, rank_mine)


def serve_tiles(own_blocks, request_info):
    serve_block, slot_used = (request_info[0], request_info[1])
    shards, capacity = serve_block.shape
    gathered = jnp.take(own_blocks, serve_block.reshape(-1), axis=1)
    gathered = gathered.reshape(2, shards, capacity, own_blocks.shape[2], own_blocks.shape[3])
    return jnp.where(slot_used[None, :, :, None, None], gathered, jnp.zeros((), own_blocks.dtype))


def pick_tiles(received, request_info):
    return received[:, request_info[2], request_info[3]]


def place_terms(terms, request_info):
    serve_block = request_info[0]
    shards, capacity = serve_block.shape
    holder = jnp.zeros((2, shards, capacity, terms.shape[2], terms.shape[3]), terms.dtype)
    return holder.at[:, request_info[2], request_info[3]].set(terms)


def absorb_terms(received, request_info, query_blocks):
    serve_block, slot_used = (request_info[0], request_info[1])
    onehot = (
        slot_used[:, :, None]
        & (serve_block[:, :, None] == jnp.arange(query_blocks, dtype=jnp.int32)[None, None, :])
    ).astype(jnp.bfloat16)
    return jnp.einsum("ncq,xncsk->xqsk", onehot, received, preferred_element_type=jnp.float32)


def token_live(tile_ids, pad_sizes, query_blocks, shard_tokens, total_blocks):
    valid = (tile_ids >= 0) & (tile_ids < total_blocks)
    safe_ids = jnp.clip(tile_ids, 0, total_blocks - 1)
    owner_shard = safe_ids // query_blocks
    shards = pad_sizes.shape[0]
    pad_of = jnp.sum(
        jnp.where(owner_shard[..., None] == jnp.arange(shards, dtype=jnp.int32), pad_sizes, 0),
        axis=-1,
    )
    within = (safe_ids % query_blocks)[..., None] * BLK + jnp.arange(BLK, dtype=jnp.int32)
    return valid[..., None] & (within < (shard_tokens - pad_of)[..., None])


def body(queries, keys, values, out_grads, random_blocks, global_blocks, pad_lengths):
    query_rows = queries[0]
    key_rows = keys[0]
    value_rows = values[0]
    grad_rows = out_grads[0]
    random_table = random_blocks[0]
    global_ids = global_blocks[0]
    pad_sizes = pad_lengths[0]
    shards = lax.axis_size("seq")
    this_shard = lax.axis_index("seq")
    shard_tokens, qwidth = query_rows.shape
    kwidth = key_rows.shape[1]
    query_blocks = shard_tokens // BLK
    total_blocks = query_blocks * shards
    near = 3 + GLOB
    kvpair = jnp.stack([key_rows, value_rows])
    extended = extended_2(kvpair, (("seq", 1),), BLK)
    ext_blocks = extended.reshape(2, query_blocks + 2, BLK, kwidth)
    window = jnp.stack(
        [ext_blocks[:, offset : offset + query_blocks] for offset in range(3)], axis=2
    )
    own_blocks = kvpair.reshape(2, query_blocks, BLK, kwidth)
    global_list = []
    for glob_num in range(GLOB):
        owner_dev = global_ids[glob_num] // query_blocks
        local_tile = lax.dynamic_index_in_dim(
            own_blocks, global_ids[glob_num] % query_blocks, 1, keepdims=False
        )
        global_list.append(broadcast(local_tile, "seq", owner_dev))
    global_tiles = jnp.stack(global_list, axis=1)
    random_three = random_table.reshape(shards, query_blocks, RAND)
    slot_plans = []
    pieces = []
    for slot_num in range(RAND):
        slot_plan = request_plan(random_three[:, :, slot_num], this_shard, query_blocks)
        received = lax.all_to_all(
            serve_tiles(own_blocks, slot_plan), "seq", split_axis=1, concat_axis=1, tiled=True
        )
        pieces.append(pick_tiles(received, slot_plan))
        slot_plans.append(slot_plan)
    fetched = jnp.stack(pieces, axis=2)
    spread_global = jnp.broadcast_to(global_tiles[:, None], (2, query_blocks, GLOB, BLK, kwidth))
    all_tiles = jnp.concatenate([window, spread_global, fetched], axis=2)
    base_ids = this_shard * query_blocks + jnp.arange(query_blocks, dtype=jnp.int32)
    window_ids = base_ids[:, None] + jnp.arange(-1, 2, dtype=jnp.int32)[None, :]
    my_random = lax.dynamic_index_in_dim(random_three, this_shard, 0, keepdims=False)
    tile_ids = jnp.concatenate(
        [window_ids, jnp.broadcast_to(global_ids[None, :], (query_blocks, GLOB)), my_random], axis=1
    )
    key_live = token_live(tile_ids, pad_sizes, query_blocks, shard_tokens, total_blocks)
    query_grad, key_terms, value_terms = block_backward(
        query_rows.reshape(query_blocks, BLK, qwidth),
        grad_rows.reshape(query_blocks, BLK, qwidth),
        all_tiles[0],
        all_tiles[1],
        key_live,
    )
    contrib = jnp.stack([key_terms, value_terms])
    local_sum = contrib[:, :, 1]
    local_sum = local_sum + jnp.pad(contrib[:, 1:, 0], ((0, 0), (0, 1), (0, 0), (0, 0)))
    local_sum = local_sum + jnp.pad(contrib[:, :-1, 2], ((0, 0), (1, 0), (0, 0), (0, 0)))
    edge_out = jnp.concatenate([contrib[:, 0, 0], contrib[:, query_blocks - 1, 2]], axis=1)
    edge_in = extended_2(edge_out.astype(jnp.bfloat16), (("seq", 1),), BLK).astype(edge_out.dtype)
    local_sum = local_sum.at[:, 0].add(edge_in[:, :BLK])
    local_sum = local_sum.at[:, query_blocks - 1].add(edge_in[:, 3 * BLK :])
    global_part = jnp.sum(contrib[:, :, 3:near], axis=1)
    global_total = lax.psum(global_part, "seq")
    global_pick = (
        (global_ids[:, None] // query_blocks == this_shard)
        & (global_ids[:, None] % query_blocks == jnp.arange(query_blocks, dtype=jnp.int32)[None, :])
    ).astype(jnp.float32)
    local_sum = local_sum + jnp.einsum(
        "gq,xgsk->xqsk", global_pick, global_total, precision=lax.Precision.HIGHEST
    )
    random_terms = contrib[:, :, near:].astype(jnp.bfloat16)
    for slot_num in range(RAND):
        returned = lax.all_to_all(
            place_terms(random_terms[:, :, slot_num], slot_plans[slot_num]),
            "seq",
            split_axis=1,
            concat_axis=1,
            tiled=True,
        )
        local_sum = local_sum + absorb_terms(returned, slot_plans[slot_num], query_blocks)
    key_grad = local_sum[0].reshape(shard_tokens, kwidth).astype(jnp.bfloat16)
    value_grad = local_sum[1].reshape(shard_tokens, kwidth).astype(jnp.bfloat16)
    query_low = query_grad
    packed = jnp.concatenate([query_low, key_grad, value_grad], axis=-1)
    handed = from_behind(packed, "section", -1)
    return (
        handed[None, :, :qwidth],
        handed[None, :, qwidth : qwidth + kwidth],
        handed[None, :, qwidth + kwidth :],
    )


def solution(mesh):
    in_specs = (
        P("section", "seq", None),
        P("section", "seq", None),
        P("section", "seq", None),
        P("section", "seq", None),
        P("section", None, None),
        P("section", None),
        P("section", None),
    )
    out_specs = (P("section", "seq", None), P("section", "seq", None), P("section", "seq", None))
    return jax.shard_map(body, mesh=mesh, in_specs=in_specs, out_specs=out_specs, check_vma=False)
```

```python
import math

import jax
import jax.numpy as jnp
from jax import lax
from jax.experimental import pallas as pl
from jax.sharding import PartitionSpec as P

HDIM = 128
BLK = 64
GLOB = 2
RAND = 3


def extended_2(array, sides, width):
    for axis, dim in sides:
        devices, length = (lax.axis_size(axis), array.shape[dim])
        up = [(i, (i + 1) % devices) for i in range(devices - 1)]
        down = [(j, i) for i, j in up]
        last = lax.slice_in_dim(array, length - width, length, axis=dim)
        leading = lax.slice_in_dim(array, 0, width, axis=dim)
        before = lax.ppermute(last, axis, up)
        after = lax.ppermute(leading, axis, down)
        array = jnp.concatenate([before, array, after], axis=dim)
    return array


def broadcast(array, axis, root):
    mine = lax.axis_index(axis) == root
    return lax.psum(jnp.where(mine, array, jnp.zeros_like(array)), axis)


def from_behind(block, axis, distance):
    devices = range(lax.axis_size(axis))
    route = [((i - distance) % len(devices), i) for i in devices]
    return lax.ppermute(block, axis, route)


def attention_kernel(q_ref, g_ref, k_ref, v_ref, live_ref, dq_ref, dkv_ref):
    block_len, width = q_ref.shape
    group = width // HDIM
    ntiles = k_ref.shape[0]
    score_scale = 1.0 / math.sqrt(HDIM)
    query = q_ref[...]
    grad = g_ref[...]
    query_rows = jnp.concatenate(
        [query[:, g * HDIM : (g + 1) * HDIM] for g in range(group)], axis=0
    )
    grad_rows = jnp.concatenate([grad[:, g * HDIM : (g + 1) * HDIM] for g in range(group)], axis=0)
    key_rows = k_ref[...].reshape(ntiles * block_len, HDIM)
    value_rows = v_ref[...].reshape(ntiles * block_len, HDIM)
    live = live_ref[...] > 0.5
    contract_last = (((1,), (1,)), ((), ()))
    contract_first = (((0,), (0,)), ((), ()))
    scores = (
        lax.dot_general(query_rows, key_rows, contract_last, preferred_element_type=jnp.float32)
        * score_scale
    )
    scores = jnp.where(live, scores, -1e30)
    row_max = jnp.max(scores, axis=1, keepdims=True)
    shifted = jnp.exp(scores - row_max)
    total = jnp.sum(shifted, axis=1, keepdims=True)
    probs = shifted * (1.0 / total)
    probs_low = probs.astype(jnp.bfloat16)
    output = jnp.dot(probs_low, value_rows, preferred_element_type=jnp.float32)
    row_dot = jnp.sum(grad_rows.astype(jnp.float32) * output, axis=1, keepdims=True)
    prob_grad = lax.dot_general(
        grad_rows, value_rows, contract_last, preferred_element_type=jnp.float32
    )
    score_grad = (probs * (prob_grad - row_dot)).astype(jnp.bfloat16)
    query_grad = jnp.dot(score_grad, key_rows, preferred_element_type=jnp.float32) * score_scale
    key_grad = (
        lax.dot_general(score_grad, query_rows, contract_first, preferred_element_type=jnp.float32)
        * score_scale
    )
    value_grad = lax.dot_general(
        probs_low, grad_rows, contract_first, preferred_element_type=jnp.float32
    )
    for g in range(group):
        dq_ref[:, g * HDIM : (g + 1) * HDIM] = query_grad[g * block_len : (g + 1) * block_len].astype(
            dq_ref.dtype
        )
    dkv_ref[:, 0] = key_grad.reshape(ntiles, block_len, HDIM)
    dkv_ref[:, 1] = value_grad.reshape(ntiles, block_len, HDIM)


def block_backward(query_rows, grad_rows, kv_tiles, key_live):
    shard_tokens, qwidth = query_rows.shape
    nblocks, ntiles, _, block_len, kwidth = kv_tiles.shape
    heads_kv = kwidth // HDIM
    group_width = qwidth // heads_kv
    live = key_live.reshape(nblocks, 1, ntiles * block_len).astype(jnp.float32)
    row_spec = pl.BlockSpec((block_len, group_width), lambda b, h: (b, h))
    key_spec = pl.BlockSpec((None, ntiles, None, block_len, HDIM), lambda b, h: (b, 0, 0, 0, h))
    value_spec = pl.BlockSpec((None, ntiles, None, block_len, HDIM), lambda b, h: (b, 0, 1, 0, h))
    term_spec = pl.BlockSpec((None, ntiles, 2, block_len, HDIM), lambda b, h: (b, 0, 0, 0, h))
    live_spec = pl.BlockSpec((None, 1, ntiles * block_len), lambda b, h: (b, 0, 0))
    flops = 12 * nblocks * heads_kv * (group_width // HDIM) * block_len * ntiles * block_len * HDIM
    query_grad, terms = pl.pallas_call(
        attention_kernel,
        grid=(nblocks, heads_kv),
        in_specs=[row_spec, row_spec, key_spec, value_spec, live_spec],
        out_specs=[row_spec, term_spec],
        out_shape=[
            jax.ShapeDtypeStruct((shard_tokens, qwidth), jnp.bfloat16),
            jax.ShapeDtypeStruct((nblocks, ntiles, 2, block_len, kwidth), jnp.float32),
        ],
        cost_estimate=pl.CostEstimate(
            flops=flops,
            transcendentals=nblocks * qwidth // HDIM * block_len * ntiles * block_len,
            bytes_accessed=shard_tokens * qwidth * 6 + nblocks * ntiles * block_len * kwidth * 12,
        ),
    )(query_rows, grad_rows, kv_tiles, kv_tiles, live)
    return (query_grad, terms)


def request_plan(request_lists, this_shard, query_blocks):
    shards, count = request_lists.shape
    capacity = -(-count // shards)
    owner_ids = request_lists // query_blocks
    local_ids = request_lists % query_blocks
    order = jnp.arange(count, dtype=jnp.int32)
    earlier = order[None, :] < order[:, None]
    same_owner = owner_ids[:, :, None] == owner_ids[:, None, :]
    slot_rank = jnp.sum(same_owner & earlier[None], axis=2)
    slot_ids = jnp.arange(capacity, dtype=jnp.int32)
    chosen = (owner_ids[:, None, :] == this_shard) & (
        slot_rank[:, None, :] == slot_ids[None, :, None]
    )
    serve_block = jnp.sum(jnp.where(chosen, local_ids[:, None, :], 0), axis=2)
    slot_used = jnp.any(chosen, axis=2)
    owner_mine = lax.dynamic_index_in_dim(owner_ids, this_shard, 0, keepdims=False)
    rank_mine = lax.dynamic_index_in_dim(slot_rank, this_shard, 0, keepdims=False)
    return (serve_block, slot_used, owner_mine, rank_mine)


def serve_tiles(own_blocks, request_info):
    serve_block, slot_used = (request_info[0], request_info[1])
    shards, capacity = serve_block.shape
    gathered = jnp.take(own_blocks, serve_block.reshape(-1), axis=1)
    gathered = gathered.reshape(2, shards, capacity, own_blocks.shape[2], own_blocks.shape[3])
    return jnp.where(slot_used[None, :, :, None, None], gathered, jnp.zeros((), own_blocks.dtype))


def pick_tiles(received, request_info):
    return received[:, request_info[2], request_info[3]]


def place_terms(terms, request_info):
    serve_block = request_info[0]
    shards, capacity = serve_block.shape
    holder = jnp.zeros((2, shards, capacity, terms.shape[2], terms.shape[3]), terms.dtype)
    return holder.at[:, request_info[2], request_info[3]].set(terms)


def absorb_terms(received, request_info, query_blocks):
    serve_block, slot_used = (request_info[0], request_info[1])
    onehot = (
        slot_used[:, :, None]
        & (serve_block[:, :, None] == jnp.arange(query_blocks, dtype=jnp.int32)[None, None, :])
    ).astype(jnp.bfloat16)
    return jnp.einsum("ncq,xncsk->xqsk", onehot, received, preferred_element_type=jnp.float32)


def token_live(tile_ids, pad_sizes, query_blocks, shard_tokens, total_blocks):
    valid = (tile_ids >= 0) & (tile_ids < total_blocks)
    safe_ids = jnp.clip(tile_ids, 0, total_blocks - 1)
    owner_shard = safe_ids // query_blocks
    shards = pad_sizes.shape[0]
    pad_of = jnp.sum(
        jnp.where(owner_shard[..., None] == jnp.arange(shards, dtype=jnp.int32), pad_sizes, 0),
        axis=-1,
    )
    within = (safe_ids % query_blocks)[..., None] * BLK + jnp.arange(BLK, dtype=jnp.int32)
    return valid[..., None] & (within < (shard_tokens - pad_of)[..., None])


def body(queries, keys, values, out_grads, random_blocks, global_blocks, pad_lengths):
    query_rows = queries[0]
    key_rows = keys[0]
    value_rows = values[0]
    grad_rows = out_grads[0]
    random_table = random_blocks[0]
    global_ids = global_blocks[0]
    pad_sizes = pad_lengths[0]
    shards = lax.axis_size("seq")
    this_shard = lax.axis_index("seq")
    shard_tokens, qwidth = query_rows.shape
    kwidth = key_rows.shape[1]
    query_blocks = shard_tokens // BLK
    total_blocks = query_blocks * shards
    near = 3 + GLOB
    kvpair = jnp.stack(
        [key_rows.reshape(query_blocks, BLK, kwidth), value_rows.reshape(query_blocks, BLK, kwidth)],
        axis=1,
    )
    all_blocks = lax.all_gather(kvpair, "seq", axis=0, tiled=True)
    random_three = random_table.reshape(shards, query_blocks, RAND)
    base_ids = this_shard * query_blocks + jnp.arange(query_blocks, dtype=jnp.int32)
    window_ids = base_ids[:, None] + jnp.arange(-1, 2, dtype=jnp.int32)[None, :]
    my_random = lax.dynamic_index_in_dim(random_three, this_shard, 0, keepdims=False)
    tile_ids = jnp.concatenate(
        [window_ids, jnp.broadcast_to(global_ids[None, :], (query_blocks, GLOB)), my_random], axis=1
    )
    ntiles = tile_ids.shape[1]
    safe_ids = jnp.clip(tile_ids, 0, total_blocks - 1)
    kv_tiles = jnp.take(all_blocks, safe_ids.reshape(-1), axis=0).reshape(
        query_blocks, ntiles, 2, BLK, kwidth
    )
    key_live = token_live(tile_ids, pad_sizes, query_blocks, shard_tokens, total_blocks)
    query_grad, terms = block_backward(query_rows, grad_rows, kv_tiles, key_live)
    handed_query = from_behind(query_grad, "section", -1)
    local_sum = terms[:, 1]
    local_sum = local_sum + jnp.pad(terms[1:, 0], ((0, 1), (0, 0), (0, 0), (0, 0)))
    local_sum = local_sum + jnp.pad(terms[:-1, 2], ((1, 0), (0, 0), (0, 0), (0, 0)))
    global_part = jnp.sum(terms[:, 3:near], axis=0)
    random_part = terms[:, near:].astype(jnp.bfloat16).astype(jnp.float32)
    foreign = jnp.concatenate(
        [
            terms[0:1, 0],
            terms[query_blocks - 1 : query_blocks, 2],
            global_part,
            random_part.reshape(query_blocks * RAND, 2, BLK, kwidth),
        ],
        axis=0,
    )
    foreign_ids = jnp.concatenate(
        [
            safe_ids[0:1, 0],
            safe_ids[query_blocks - 1 : query_blocks, 2],
            global_ids,
            my_random.reshape(-1),
        ]
    )
    partial = jnp.zeros((total_blocks, 2, BLK, kwidth), jnp.float32).at[foreign_ids].add(foreign)
    returned = lax.psum_scatter(
        partial.astype(jnp.bfloat16), "seq", scatter_dimension=0, tiled=True
    )
    kv_sum = local_sum + returned.astype(jnp.float32)
    kv_grad = jnp.concatenate(
        [
            kv_sum[:, 0].reshape(shard_tokens, kwidth).astype(jnp.bfloat16),
            kv_sum[:, 1].reshape(shard_tokens, kwidth).astype(jnp.bfloat16),
        ],
        axis=-1,
    )
    handed_kv = from_behind(kv_grad, "section", -1)
    return (
        handed_query[None],
        handed_kv[None, :, :kwidth],
        handed_kv[None, :, kwidth:],
    )


def solution(mesh):
    in_specs = (
        P("section", "seq", None),
        P("section", "seq", None),
        P("section", "seq", None),
        P("section", "seq", None),
        P("section", None, None),
        P("section", None),
        P("section", None),
    )
    out_specs = (P("section", "seq", None), P("section", "seq", None), P("section", "seq", None))
    return jax.shard_map(body, mesh=mesh, in_specs=in_specs, out_specs=out_specs, check_vma=False)
```

```python
import math

import jax
import jax.numpy as jnp
from jax import lax
from jax.experimental import pallas as pl
from jax.experimental.pallas import tpu as pltpu
from jax.sharding import PartitionSpec as P

HDIM = 128
BLK = 64
GLOB = 2
RAND = 3


def extended_2(array, sides, width):
    for axis, dim in sides:
        devices, length = (lax.axis_size(axis), array.shape[dim])
        up = [(i, (i + 1) % devices) for i in range(devices - 1)]
        down = [(j, i) for i, j in up]
        last = lax.slice_in_dim(array, length - width, length, axis=dim)
        leading = lax.slice_in_dim(array, 0, width, axis=dim)
        before = lax.ppermute(last, axis, up)
        after = lax.ppermute(leading, axis, down)
        array = jnp.concatenate([before, array, after], axis=dim)
    return array


def broadcast(array, axis, root):
    mine = lax.axis_index(axis) == root
    return lax.psum(jnp.where(mine, array, jnp.zeros_like(array)), axis)


def from_behind(block, axis, distance):
    devices = range(lax.axis_size(axis))
    route = [((i - distance) % len(devices), i) for i in devices]
    return lax.ppermute(block, axis, route)


def attention_kernel(ids_ref, q_ref, g_ref, *refs):
    del ids_ref
    ntiles = len(refs) - 6
    tile_refs = refs[:ntiles]
    live_ref = refs[ntiles]
    dq_ref, own_ref, edge_ref, glob_ref, rand_ref = refs[ntiles + 1 :]
    nblocks = own_ref.shape[0]
    block_len, width = q_ref.shape
    group = width // HDIM
    near = 3 + GLOB
    b = pl.program_id(1)
    score_scale = 1.0 / math.sqrt(HDIM)
    query = q_ref[...]
    grad = g_ref[...]
    query_rows = jnp.concatenate(
        [query[:, g * HDIM : (g + 1) * HDIM] for g in range(group)], axis=0
    )
    grad_rows = jnp.concatenate([grad[:, g * HDIM : (g + 1) * HDIM] for g in range(group)], axis=0)
    key_rows = jnp.concatenate([tile_refs[t][0] for t in range(ntiles)], axis=0)
    value_rows = jnp.concatenate([tile_refs[t][1] for t in range(ntiles)], axis=0)
    live = live_ref[...] > 0.5
    contract_last = (((1,), (1,)), ((), ()))
    contract_first = (((0,), (0,)), ((), ()))
    scores = (
        lax.dot_general(query_rows, key_rows, contract_last, preferred_element_type=jnp.float32)
        * score_scale
    )
    scores = jnp.where(live, scores, -1e30)
    row_max = jnp.max(scores, axis=1, keepdims=True)
    shifted = jnp.exp(scores - row_max)
    total = jnp.sum(shifted, axis=1, keepdims=True)
    probs = shifted * (1.0 / total)
    probs_low = probs.astype(jnp.bfloat16)
    output = jnp.dot(probs_low, value_rows, preferred_element_type=jnp.float32)
    row_dot = jnp.sum(grad_rows.astype(jnp.float32) * output, axis=1, keepdims=True)
    prob_grad = lax.dot_general(
        grad_rows, value_rows, contract_last, preferred_element_type=jnp.float32
    )
    score_grad = (probs * (prob_grad - row_dot)).astype(jnp.bfloat16)
    query_grad = jnp.dot(score_grad, key_rows, preferred_element_type=jnp.float32) * score_scale
    key_grad = (
        lax.dot_general(score_grad, query_rows, contract_first, preferred_element_type=jnp.float32)
        * score_scale
    )
    value_grad = lax.dot_general(
        probs_low, grad_rows, contract_first, preferred_element_type=jnp.float32
    )
    for g in range(group):
        dq_ref[:, g * HDIM : (g + 1) * HDIM] = query_grad[g * block_len : (g + 1) * block_len].astype(
            dq_ref.dtype
        )
    terms = jnp.stack(
        [key_grad.reshape(ntiles, block_len, HDIM), value_grad.reshape(ntiles, block_len, HDIM)],
        axis=1,
    )

    @pl.when(b == 0)
    def _():
        own_ref[...] = jnp.zeros_like(own_ref)
        glob_ref[...] = jnp.zeros_like(glob_ref)
        edge_ref[0] = terms[0]

    @pl.when(b > 0)
    def _():
        before = jnp.maximum(b - 1, 0)
        own_ref[before] = own_ref[before] + terms[0]

    own_ref[b] = own_ref[b] + terms[1]

    @pl.when(b < nblocks - 1)
    def _():
        after = jnp.minimum(b + 1, nblocks - 1)
        own_ref[after] = own_ref[after] + terms[2]

    @pl.when(b == nblocks - 1)
    def _():
        edge_ref[1] = terms[2]

    glob_ref[...] = glob_ref[...] + terms[3:near]
    rand_ref[...] = terms[near:].astype(rand_ref.dtype)


def block_backward(query_rows, grad_rows, all_blocks, tile_ids, key_live):
    shard_tokens, qwidth = query_rows.shape
    _, _, block_len, kwidth = all_blocks.shape
    nblocks, ntiles = tile_ids.shape
    heads_kv = kwidth // HDIM
    group_width = qwidth // heads_kv
    near = 3 + GLOB
    nrand = ntiles - near
    live = key_live.reshape(nblocks, 1, ntiles * block_len).astype(jnp.float32)
    row_spec = pl.BlockSpec((block_len, group_width), lambda h, b, ids: (b, h))
    tile_specs = [
        pl.BlockSpec(
            (None, 2, block_len, HDIM), lambda h, b, ids, t=t: (ids[b * ntiles + t], 0, 0, h)
        )
        for t in range(ntiles)
    ]
    live_spec = pl.BlockSpec((None, 1, ntiles * block_len), lambda h, b, ids: (b, 0, 0))
    own_spec = pl.BlockSpec((nblocks, 2, block_len, HDIM), lambda h, b, ids: (0, 0, 0, h))
    edge_spec = pl.BlockSpec((2, 2, block_len, HDIM), lambda h, b, ids: (0, 0, 0, h))
    glob_spec = pl.BlockSpec((GLOB, 2, block_len, HDIM), lambda h, b, ids: (0, 0, 0, h))
    rand_spec = pl.BlockSpec((None, nrand, 2, block_len, HDIM), lambda h, b, ids: (b, 0, 0, 0, h))
    flops = 12 * nblocks * heads_kv * (group_width // HDIM) * block_len * ntiles * block_len * HDIM
    grid_spec = pltpu.PrefetchScalarGridSpec(
        num_scalar_prefetch=1,
        grid=(heads_kv, nblocks),
        in_specs=[row_spec, row_spec, *tile_specs, live_spec],
        out_specs=[row_spec, own_spec, edge_spec, glob_spec, rand_spec],
    )
    outs = pl.pallas_call(
        attention_kernel,
        grid_spec=grid_spec,
        out_shape=[
            jax.ShapeDtypeStruct((shard_tokens, qwidth), jnp.bfloat16),
            jax.ShapeDtypeStruct((nblocks, 2, block_len, kwidth), jnp.float32),
            jax.ShapeDtypeStruct((2, 2, block_len, kwidth), jnp.float32),
            jax.ShapeDtypeStruct((GLOB, 2, block_len, kwidth), jnp.float32),
            jax.ShapeDtypeStruct((nblocks, nrand, 2, block_len, kwidth), jnp.bfloat16),
        ],
        compiler_params=pltpu.CompilerParams(
            dimension_semantics=("arbitrary", "arbitrary")
        ),
        cost_estimate=pl.CostEstimate(
            flops=flops,
            transcendentals=nblocks * qwidth // HDIM * block_len * ntiles * block_len,
            bytes_accessed=shard_tokens * qwidth * 6 + nblocks * ntiles * block_len * kwidth * 6,
        ),
    )(tile_ids.reshape(-1), query_rows, grad_rows, *([all_blocks] * ntiles), live)
    return outs


def request_plan(request_lists, this_shard, query_blocks):
    shards, count = request_lists.shape
    capacity = -(-count // shards)
    owner_ids = request_lists // query_blocks
    local_ids = request_lists % query_blocks
    order = jnp.arange(count, dtype=jnp.int32)
    earlier = order[None, :] < order[:, None]
    same_owner = owner_ids[:, :, None] == owner_ids[:, None, :]
    slot_rank = jnp.sum(same_owner & earlier[None], axis=2)
    slot_ids = jnp.arange(capacity, dtype=jnp.int32)
    chosen = (owner_ids[:, None, :] == this_shard) & (
        slot_rank[:, None, :] == slot_ids[None, :, None]
    )
    serve_block = jnp.sum(jnp.where(chosen, local_ids[:, None, :], 0), axis=2)
    slot_used = jnp.any(chosen, axis=2)
    owner_mine = lax.dynamic_index_in_dim(owner_ids, this_shard, 0, keepdims=False)
    rank_mine = lax.dynamic_index_in_dim(slot_rank, this_shard, 0, keepdims=False)
    return (serve_block, slot_used, owner_mine, rank_mine)


def serve_tiles(own_blocks, request_info):
    serve_block, slot_used = (request_info[0], request_info[1])
    shards, capacity = serve_block.shape
    gathered = jnp.take(own_blocks, serve_block.reshape(-1), axis=1)
    gathered = gathered.reshape(2, shards, capacity, own_blocks.shape[2], own_blocks.shape[3])
    return jnp.where(slot_used[None, :, :, None, None], gathered, jnp.zeros((), own_blocks.dtype))


def pick_tiles(received, request_info):
    return received[:, request_info[2], request_info[3]]


def place_terms(terms, request_info):
    serve_block = request_info[0]
    shards, capacity = serve_block.shape
    holder = jnp.zeros((2, shards, capacity, terms.shape[2], terms.shape[3]), terms.dtype)
    return holder.at[:, request_info[2], request_info[3]].set(terms)


def absorb_terms(received, request_info, query_blocks):
    serve_block, slot_used = (request_info[0], request_info[1])
    onehot = (
        slot_used[:, :, None]
        & (serve_block[:, :, None] == jnp.arange(query_blocks, dtype=jnp.int32)[None, None, :])
    ).astype(jnp.bfloat16)
    return jnp.einsum("ncq,xncsk->xqsk", onehot, received, preferred_element_type=jnp.float32)


def token_live(tile_ids, pad_sizes, query_blocks, shard_tokens, total_blocks):
    valid = (tile_ids >= 0) & (tile_ids < total_blocks)
    safe_ids = jnp.clip(tile_ids, 0, total_blocks - 1)
    owner_shard = safe_ids // query_blocks
    shards = pad_sizes.shape[0]
    pad_of = jnp.sum(
        jnp.where(owner_shard[..., None] == jnp.arange(shards, dtype=jnp.int32), pad_sizes, 0),
        axis=-1,
    )
    within = (safe_ids % query_blocks)[..., None] * BLK + jnp.arange(BLK, dtype=jnp.int32)
    return valid[..., None] & (within < (shard_tokens - pad_of)[..., None])


def body(queries, keys, values, out_grads, random_blocks, global_blocks, pad_lengths):
    query_rows = queries[0]
    key_rows = keys[0]
    value_rows = values[0]
    grad_rows = out_grads[0]
    random_table = random_blocks[0]
    global_ids = global_blocks[0]
    pad_sizes = pad_lengths[0]
    shards = lax.axis_size("seq")
    this_shard = lax.axis_index("seq")
    shard_tokens, qwidth = query_rows.shape
    kwidth = key_rows.shape[1]
    query_blocks = shard_tokens // BLK
    total_blocks = query_blocks * shards
    near = 3 + GLOB
    kvpair = jnp.stack(
        [key_rows.reshape(query_blocks, BLK, kwidth), value_rows.reshape(query_blocks, BLK, kwidth)],
        axis=1,
    )
    all_blocks = lax.all_gather(kvpair, "seq", axis=0, tiled=True)
    random_three = random_table.reshape(shards, query_blocks, RAND)
    base_ids = this_shard * query_blocks + jnp.arange(query_blocks, dtype=jnp.int32)
    window_ids = base_ids[:, None] + jnp.arange(-1, 2, dtype=jnp.int32)[None, :]
    my_random = lax.dynamic_index_in_dim(random_three, this_shard, 0, keepdims=False)
    tile_ids = jnp.concatenate(
        [window_ids, jnp.broadcast_to(global_ids[None, :], (query_blocks, GLOB)), my_random], axis=1
    )
    safe_ids = jnp.clip(tile_ids, 0, total_blocks - 1)
    key_live = token_live(tile_ids, pad_sizes, query_blocks, shard_tokens, total_blocks)
    query_grad, local_sum, edge_terms, global_part, random_part = block_backward(
        query_rows, grad_rows, all_blocks, safe_ids, key_live
    )
    handed_query = from_behind(query_grad, "section", -1)
    foreign = jnp.concatenate(
        [
            edge_terms.astype(jnp.bfloat16),
            global_part.astype(jnp.bfloat16),
            random_part.reshape(query_blocks * RAND, 2, BLK, kwidth),
        ],
        axis=0,
    )
    foreign_ids = jnp.concatenate(
        [
            safe_ids[0:1, 0],
            safe_ids[query_blocks - 1 : query_blocks, 2],
            global_ids,
            my_random.reshape(-1),
        ]
    )
    onehot = (
        foreign_ids[None, :] == jnp.arange(total_blocks, dtype=jnp.int32)[:, None]
    ).astype(jnp.bfloat16)
    partial = jnp.einsum(
        "nf,fxsk->nxsk", onehot, foreign, preferred_element_type=jnp.float32
    ).astype(jnp.bfloat16)
    returned = lax.psum_scatter(
        partial, "seq", scatter_dimension=0, tiled=True
    )
    kv_sum = local_sum + returned.astype(jnp.float32)
    kv_grad = jnp.concatenate(
        [
            kv_sum[:, 0].reshape(shard_tokens, kwidth).astype(jnp.bfloat16),
            kv_sum[:, 1].reshape(shard_tokens, kwidth).astype(jnp.bfloat16),
        ],
        axis=-1,
    )
    handed_kv = from_behind(kv_grad, "section", -1)
    return (
        handed_query[None],
        handed_kv[None, :, :kwidth],
        handed_kv[None, :, kwidth:],
    )


def solution(mesh):
    in_specs = (
        P("section", "seq", None),
        P("section", "seq", None),
        P("section", "seq", None),
        P("section", "seq", None),
        P("section", None, None),
        P("section", None),
        P("section", None),
    )
    out_specs = (P("section", "seq", None), P("section", "seq", None), P("section", "seq", None))
    return jax.shard_map(body, mesh=mesh, in_specs=in_specs, out_specs=out_specs, check_vma=False)
```

```python
import math

import jax
import jax.numpy as jnp
from jax import lax
from jax.experimental import pallas as pl
from jax.experimental.pallas import tpu as pltpu
from jax.sharding import PartitionSpec as P

HDIM = 128
BLK = 64
GLOB = 2
RAND = 3


def extended_2(array, sides, width):
    for axis, dim in sides:
        devices, length = (lax.axis_size(axis), array.shape[dim])
        up = [(i, (i + 1) % devices) for i in range(devices - 1)]
        down = [(j, i) for i, j in up]
        last = lax.slice_in_dim(array, length - width, length, axis=dim)
        leading = lax.slice_in_dim(array, 0, width, axis=dim)
        before = lax.ppermute(last, axis, up)
        after = lax.ppermute(leading, axis, down)
        array = jnp.concatenate([before, array, after], axis=dim)
    return array


def broadcast(array, axis, root):
    mine = lax.axis_index(axis) == root
    return lax.psum(jnp.where(mine, array, jnp.zeros_like(array)), axis)


def from_behind(block, axis, distance):
    devices = range(lax.axis_size(axis))
    route = [((i - distance) % len(devices), i) for i in devices]
    return lax.ppermute(block, axis, route)


def tree_sum(array, axis):
    devices = lax.axis_size(axis)
    if devices & (devices - 1):
        return lax.psum(array, axis)
    step = 1
    while step < devices:
        array = array + lax.ppermute(array, axis, [(i, i ^ step) for i in range(devices)])
        step *= 2
    return array


def attention_kernel(ids_ref, q_ref, g_ref, *refs):
    del ids_ref
    ntiles = len(refs) - 6
    tile_refs = refs[:ntiles]
    live_ref = refs[ntiles]
    dq_ref, own_ref, edge_ref, glob_ref, rand_ref = refs[ntiles + 1 :]
    nblocks = own_ref.shape[0]
    block_len, width = q_ref.shape
    group = width // HDIM
    near = 3 + GLOB
    b = pl.program_id(1)
    score_scale = 1.0 / math.sqrt(HDIM)
    query = q_ref[...]
    grad = g_ref[...]
    query_rows = jnp.concatenate(
        [query[:, g * HDIM : (g + 1) * HDIM] for g in range(group)], axis=0
    )
    grad_rows = jnp.concatenate([grad[:, g * HDIM : (g + 1) * HDIM] for g in range(group)], axis=0)
    key_rows = jnp.concatenate([tile_refs[t][0] for t in range(ntiles)], axis=0)
    value_rows = jnp.concatenate([tile_refs[t][1] for t in range(ntiles)], axis=0)
    live = live_ref[...] > 0.5
    contract_last = (((1,), (1,)), ((), ()))
    contract_first = (((0,), (0,)), ((), ()))
    scores = (
        lax.dot_general(query_rows, key_rows, contract_last, preferred_element_type=jnp.float32)
        * score_scale
    )
    scores = jnp.where(live, scores, -1e30)
    row_max = jnp.max(scores, axis=1, keepdims=True)
    shifted = jnp.exp(scores - row_max)
    total = jnp.sum(shifted, axis=1, keepdims=True)
    probs = shifted * (1.0 / total)
    probs_low = probs.astype(jnp.bfloat16)
    output = jnp.dot(probs_low, value_rows, preferred_element_type=jnp.float32)
    row_dot = jnp.sum(grad_rows.astype(jnp.float32) * output, axis=1, keepdims=True)
    prob_grad = lax.dot_general(
        grad_rows, value_rows, contract_last, preferred_element_type=jnp.float32
    )
    score_grad = (probs * (prob_grad - row_dot)).astype(jnp.bfloat16)
    query_grad = jnp.dot(score_grad, key_rows, preferred_element_type=jnp.float32) * score_scale
    key_grad = (
        lax.dot_general(score_grad, query_rows, contract_first, preferred_element_type=jnp.float32)
        * score_scale
    )
    value_grad = lax.dot_general(
        probs_low, grad_rows, contract_first, preferred_element_type=jnp.float32
    )
    for g in range(group):
        dq_ref[:, g * HDIM : (g + 1) * HDIM] = query_grad[g * block_len : (g + 1) * block_len].astype(
            dq_ref.dtype
        )
    terms = jnp.stack(
        [key_grad.reshape(ntiles, block_len, HDIM), value_grad.reshape(ntiles, block_len, HDIM)],
        axis=1,
    )

    @pl.when(b == 0)
    def _():
        own_ref[...] = jnp.zeros_like(own_ref)
        glob_ref[...] = jnp.zeros_like(glob_ref)
        edge_ref[0] = terms[0]

    @pl.when(b > 0)
    def _():
        before = jnp.maximum(b - 1, 0)
        own_ref[before] = own_ref[before] + terms[0]

    own_ref[b] = own_ref[b] + terms[1]

    @pl.when(b < nblocks - 1)
    def _():
        after = jnp.minimum(b + 1, nblocks - 1)
        own_ref[after] = own_ref[after] + terms[2]

    @pl.when(b == nblocks - 1)
    def _():
        edge_ref[1] = terms[2]

    glob_ref[...] = glob_ref[...] + terms[3:near]
    rand_ref[...] = terms[near:].astype(rand_ref.dtype)


def block_backward(query_rows, grad_rows, all_blocks, tile_ids, key_live):
    shard_tokens, qwidth = query_rows.shape
    _, _, block_len, kwidth = all_blocks.shape
    nblocks, ntiles = tile_ids.shape
    heads_kv = kwidth // HDIM
    group_width = qwidth // heads_kv
    near = 3 + GLOB
    nrand = ntiles - near
    live = key_live.reshape(nblocks, 1, ntiles * block_len).astype(jnp.float32)
    row_spec = pl.BlockSpec((block_len, group_width), lambda h, b, ids: (b, h))
    tile_specs = [
        pl.BlockSpec(
            (None, 2, block_len, HDIM), lambda h, b, ids, t=t: (ids[b * ntiles + t], 0, 0, h)
        )
        for t in range(ntiles)
    ]
    live_spec = pl.BlockSpec((None, 1, ntiles * block_len), lambda h, b, ids: (b, 0, 0))
    own_spec = pl.BlockSpec((nblocks, 2, block_len, HDIM), lambda h, b, ids: (0, 0, 0, h))
    edge_spec = pl.BlockSpec((2, 2, block_len, HDIM), lambda h, b, ids: (0, 0, 0, h))
    glob_spec = pl.BlockSpec((GLOB, 2, block_len, HDIM), lambda h, b, ids: (0, 0, 0, h))
    rand_spec = pl.BlockSpec((None, nrand, 2, block_len, HDIM), lambda h, b, ids: (b, 0, 0, 0, h))
    flops = 12 * nblocks * heads_kv * (group_width // HDIM) * block_len * ntiles * block_len * HDIM
    grid_spec = pltpu.PrefetchScalarGridSpec(
        num_scalar_prefetch=1,
        grid=(heads_kv, nblocks),
        in_specs=[row_spec, row_spec, *tile_specs, live_spec],
        out_specs=[row_spec, own_spec, edge_spec, glob_spec, rand_spec],
    )
    outs = pl.pallas_call(
        attention_kernel,
        grid_spec=grid_spec,
        out_shape=[
            jax.ShapeDtypeStruct((shard_tokens, qwidth), jnp.bfloat16),
            jax.ShapeDtypeStruct((nblocks, 2, block_len, kwidth), jnp.float32),
            jax.ShapeDtypeStruct((2, 2, block_len, kwidth), jnp.float32),
            jax.ShapeDtypeStruct((GLOB, 2, block_len, kwidth), jnp.float32),
            jax.ShapeDtypeStruct((nblocks, nrand, 2, block_len, kwidth), jnp.bfloat16),
        ],
        compiler_params=pltpu.CompilerParams(
            dimension_semantics=("arbitrary", "arbitrary")
        ),
        cost_estimate=pl.CostEstimate(
            flops=flops,
            transcendentals=nblocks * qwidth // HDIM * block_len * ntiles * block_len,
            bytes_accessed=shard_tokens * qwidth * 6 + nblocks * ntiles * block_len * kwidth * 6,
        ),
    )(tile_ids.reshape(-1), query_rows, grad_rows, *([all_blocks] * ntiles), live)
    return outs


def request_plan(request_lists, this_shard, query_blocks):
    shards, count = request_lists.shape
    capacity = -(-count // shards)
    owner_ids = request_lists // query_blocks
    local_ids = request_lists % query_blocks
    order = jnp.arange(count, dtype=jnp.int32)
    earlier = order[None, :] < order[:, None]
    same_owner = owner_ids[:, :, None] == owner_ids[:, None, :]
    slot_rank = jnp.sum(same_owner & earlier[None], axis=2)
    slot_ids = jnp.arange(capacity, dtype=jnp.int32)
    chosen = (owner_ids[:, None, :] == this_shard) & (
        slot_rank[:, None, :] == slot_ids[None, :, None]
    )
    serve_block = jnp.sum(jnp.where(chosen, local_ids[:, None, :], 0), axis=2)
    slot_used = jnp.any(chosen, axis=2)
    owner_mine = lax.dynamic_index_in_dim(owner_ids, this_shard, 0, keepdims=False)
    rank_mine = lax.dynamic_index_in_dim(slot_rank, this_shard, 0, keepdims=False)
    return (serve_block, slot_used, owner_mine, rank_mine)


def serve_tiles(own_blocks, request_info):
    serve_block, slot_used = (request_info[0], request_info[1])
    shards, capacity = serve_block.shape
    gathered = jnp.take(own_blocks, serve_block.reshape(-1), axis=1)
    gathered = gathered.reshape(2, shards, capacity, own_blocks.shape[2], own_blocks.shape[3])
    return jnp.where(slot_used[None, :, :, None, None], gathered, jnp.zeros((), own_blocks.dtype))


def pick_tiles(received, request_info):
    return received[:, request_info[2], request_info[3]]


def place_terms(terms, request_info):
    serve_block = request_info[0]
    shards, capacity = serve_block.shape
    holder = jnp.zeros((2, shards, capacity, terms.shape[2], terms.shape[3]), terms.dtype)
    return holder.at[:, request_info[2], request_info[3]].set(terms)


def absorb_terms(received, request_info, query_blocks):
    serve_block, slot_used = (request_info[0], request_info[1])
    onehot = (
        slot_used[:, :, None]
        & (serve_block[:, :, None] == jnp.arange(query_blocks, dtype=jnp.int32)[None, None, :])
    ).astype(jnp.bfloat16)
    return jnp.einsum("ncq,xncsk->xqsk", onehot, received, preferred_element_type=jnp.float32)


def token_live(tile_ids, pad_sizes, query_blocks, shard_tokens, total_blocks):
    valid = (tile_ids >= 0) & (tile_ids < total_blocks)
    safe_ids = jnp.clip(tile_ids, 0, total_blocks - 1)
    owner_shard = safe_ids // query_blocks
    shards = pad_sizes.shape[0]
    pad_of = jnp.sum(
        jnp.where(owner_shard[..., None] == jnp.arange(shards, dtype=jnp.int32), pad_sizes, 0),
        axis=-1,
    )
    within = (safe_ids % query_blocks)[..., None] * BLK + jnp.arange(BLK, dtype=jnp.int32)
    return valid[..., None] & (within < (shard_tokens - pad_of)[..., None])


def body(queries, keys, values, out_grads, random_blocks, global_blocks, pad_lengths):
    query_rows = queries[0]
    key_rows = keys[0]
    value_rows = values[0]
    grad_rows = out_grads[0]
    random_table = random_blocks[0]
    global_ids = global_blocks[0]
    pad_sizes = pad_lengths[0]
    shards = lax.axis_size("seq")
    this_shard = lax.axis_index("seq")
    shard_tokens, qwidth = query_rows.shape
    kwidth = key_rows.shape[1]
    query_blocks = shard_tokens // BLK
    total_blocks = query_blocks * shards
    own_blocks = jnp.stack(
        [key_rows.reshape(query_blocks, BLK, kwidth), value_rows.reshape(query_blocks, BLK, kwidth)],
        axis=1,
    )
    up = [(i, (i + 1) % shards) for i in range(shards - 1)]
    down = [(j, i) for i, j in up]
    edge_before = lax.ppermute(own_blocks[query_blocks - 1 :], "seq", up)
    edge_after = lax.ppermute(own_blocks[:1], "seq", down)
    global_mine = [
        jnp.where(
            global_ids[g] // query_blocks == this_shard,
            lax.dynamic_index_in_dim(own_blocks, global_ids[g] % query_blocks, 0, keepdims=True),
            jnp.zeros((), own_blocks.dtype),
        )
        for g in range(GLOB)
    ]
    global_tiles = tree_sum(jnp.concatenate(global_mine, axis=0), "seq")
    requests = random_table.reshape(shards, query_blocks * RAND)
    plan = request_plan(requests, this_shard, query_blocks)
    serve_block, slot_used, owner_mine, rank_mine = plan
    capacity = serve_block.shape[1]
    served = jnp.take(own_blocks, serve_block.reshape(-1), axis=0)
    received = lax.all_to_all(served, "seq", 0, 0, tiled=True)
    sources = jnp.concatenate([own_blocks, edge_before, edge_after, global_tiles, received], axis=0)
    nb = query_blocks
    block_range = jnp.arange(nb, dtype=jnp.int32)
    source_ids = jnp.concatenate(
        [
            jnp.where(block_range == 0, nb, block_range - 1)[:, None],
            block_range[:, None],
            jnp.where(block_range == nb - 1, nb + 1, block_range + 1)[:, None],
            jnp.broadcast_to(nb + 2 + jnp.arange(GLOB, dtype=jnp.int32)[None, :], (nb, GLOB)),
            (nb + 2 + GLOB + owner_mine * capacity + rank_mine).reshape(nb, RAND),
        ],
        axis=1,
    )
    source_ids = jnp.clip(source_ids, 0, sources.shape[0] - 1)
    random_three = random_table.reshape(shards, query_blocks, RAND)
    base_ids = this_shard * query_blocks + block_range
    window_ids = base_ids[:, None] + jnp.arange(-1, 2, dtype=jnp.int32)[None, :]
    my_random = lax.dynamic_index_in_dim(random_three, this_shard, 0, keepdims=False)
    tile_ids = jnp.concatenate(
        [window_ids, jnp.broadcast_to(global_ids[None, :], (query_blocks, GLOB)), my_random], axis=1
    )
    key_live = token_live(tile_ids, pad_sizes, query_blocks, shard_tokens, total_blocks)
    query_grad, local_sum, edge_terms, global_part, random_part = block_backward(
        query_rows, grad_rows, sources, source_ids, key_live
    )
    handed_query = from_behind(query_grad, "section", -1)
    edge_low = edge_terms.astype(jnp.bfloat16)
    from_after = lax.ppermute(edge_low[:1], "seq", down)
    from_before = lax.ppermute(edge_low[1:], "seq", up)
    holder = jnp.zeros((shards, capacity, 2, BLK, kwidth), random_part.dtype)
    holder = holder.at[owner_mine, rank_mine].set(
        random_part.reshape(query_blocks * RAND, 2, BLK, kwidth)
    )
    returned = lax.all_to_all(
        holder.reshape(shards * capacity, 2, BLK, kwidth), "seq", 0, 0, tiled=True
    )
    onehot = (
        slot_used.reshape(-1)[None, :]
        & (serve_block.reshape(-1)[None, :] == block_range[:, None])
    ).astype(jnp.bfloat16)
    kv_sum = local_sum + jnp.einsum(
        "qf,fxsk->qxsk", onehot, returned, preferred_element_type=jnp.float32
    )
    kv_sum = kv_sum.at[nb - 1].add(from_after[0].astype(jnp.float32))
    kv_sum = kv_sum.at[0].add(from_before[0].astype(jnp.float32))
    global_total = tree_sum(global_part, "seq")
    global_pick = (
        (global_ids[:, None] // query_blocks == this_shard)
        & (global_ids[:, None] % query_blocks == block_range[None, :])
    ).astype(jnp.float32)
    kv_sum = kv_sum + jnp.einsum(
        "gq,gxsk->qxsk", global_pick, global_total, precision=lax.Precision.HIGHEST
    )
    kv_grad = jnp.concatenate(
        [
            kv_sum[:, 0].reshape(shard_tokens, kwidth).astype(jnp.bfloat16),
            kv_sum[:, 1].reshape(shard_tokens, kwidth).astype(jnp.bfloat16),
        ],
        axis=-1,
    )
    handed_kv = from_behind(kv_grad, "section", -1)
    return (
        handed_query[None],
        handed_kv[None, :, :kwidth],
        handed_kv[None, :, kwidth:],
    )


def solution(mesh):
    in_specs = (
        P("section", "seq", None),
        P("section", "seq", None),
        P("section", "seq", None),
        P("section", "seq", None),
        P("section", None, None),
        P("section", None),
        P("section", None),
    )
    out_specs = (P("section", "seq", None), P("section", "seq", None), P("section", "seq", None))
    return jax.shard_map(body, mesh=mesh, in_specs=in_specs, out_specs=out_specs, check_vma=False)
```

```python
import math

import jax
import jax.numpy as jnp
from jax import lax
from jax.experimental import pallas as pl
from jax.experimental.pallas import tpu as pltpu
from jax.sharding import PartitionSpec as P

HDIM = 128
BLK = 64
GLOB = 2
RAND = 3


def extended_2(array, sides, width):
    for axis, dim in sides:
        devices, length = (lax.axis_size(axis), array.shape[dim])
        up = [(i, (i + 1) % devices) for i in range(devices - 1)]
        down = [(j, i) for i, j in up]
        last = lax.slice_in_dim(array, length - width, length, axis=dim)
        leading = lax.slice_in_dim(array, 0, width, axis=dim)
        before = lax.ppermute(last, axis, up)
        after = lax.ppermute(leading, axis, down)
        array = jnp.concatenate([before, array, after], axis=dim)
    return array


def broadcast(array, axis, root):
    mine = lax.axis_index(axis) == root
    return lax.psum(jnp.where(mine, array, jnp.zeros_like(array)), axis)


def from_behind(block, axis, distance):
    devices = range(lax.axis_size(axis))
    route = [((i - distance) % len(devices), i) for i in devices]
    return lax.ppermute(block, axis, route)


def tree_sum(array, axis):
    devices = lax.axis_size(axis)
    rows = array.size // array.shape[-1]
    if devices & (devices - 1) or rows % devices:
        return lax.psum(array, axis)
    me = lax.axis_index(axis)
    pieces = array.reshape(rows, array.shape[-1])
    step = 1
    while step < devices:
        half = pieces.shape[0] // 2
        bit = (me // step) % 2
        keep = lax.dynamic_slice_in_dim(pieces, bit * half, half)
        send = lax.dynamic_slice_in_dim(pieces, (1 - bit) * half, half)
        pieces = keep + lax.ppermute(send, axis, [(i, i ^ step) for i in range(devices)])
        step *= 2
    while step > 1:
        step //= 2
        bit = (me // step) % 2
        other = lax.ppermute(pieces, axis, [(i, i ^ step) for i in range(devices)])
        both = jnp.concatenate([pieces, other], axis=0)
        pieces = jnp.where(bit == 0, both, jnp.concatenate([other, pieces], axis=0))
    return pieces.reshape(array.shape)


def attention_kernel(ids_ref, q_ref, g_ref, *refs):
    del ids_ref
    ntiles = len(refs) - 6
    tile_refs = refs[:ntiles]
    live_ref = refs[ntiles]
    dq_ref, own_ref, edge_ref, glob_ref, rand_ref = refs[ntiles + 1 :]
    nblocks = own_ref.shape[0]
    block_len, width = q_ref.shape
    group = width // HDIM
    near = 3 + GLOB
    b = pl.program_id(1)
    score_scale = 1.0 / math.sqrt(HDIM)
    query = q_ref[...]
    grad = g_ref[...]
    query_rows = jnp.concatenate(
        [query[:, g * HDIM : (g + 1) * HDIM] for g in range(group)], axis=0
    )
    grad_rows = jnp.concatenate([grad[:, g * HDIM : (g + 1) * HDIM] for g in range(group)], axis=0)
    key_rows = jnp.concatenate([tile_refs[t][0] for t in range(ntiles)], axis=0)
    value_rows = jnp.concatenate([tile_refs[t][1] for t in range(ntiles)], axis=0)
    live = live_ref[...] > 0.5
    contract_last = (((1,), (1,)), ((), ()))
    contract_first = (((0,), (0,)), ((), ()))
    scores = (
        lax.dot_general(query_rows, key_rows, contract_last, preferred_element_type=jnp.float32)
        * score_scale
    )
    scores = jnp.where(live, scores, -1e30)
    row_max = jnp.max(scores, axis=1, keepdims=True)
    shifted = jnp.exp(scores - row_max)
    total = jnp.sum(shifted, axis=1, keepdims=True)
    probs = shifted * (1.0 / total)
    probs_low = probs.astype(jnp.bfloat16)
    output = jnp.dot(probs_low, value_rows, preferred_element_type=jnp.float32)
    row_dot = jnp.sum(grad_rows.astype(jnp.float32) * output, axis=1, keepdims=True)
    prob_grad = lax.dot_general(
        grad_rows, value_rows, contract_last, preferred_element_type=jnp.float32
    )
    score_grad = (probs * (prob_grad - row_dot)).astype(jnp.bfloat16)
    query_grad = jnp.dot(score_grad, key_rows, preferred_element_type=jnp.float32) * score_scale
    key_grad = (
        lax.dot_general(score_grad, query_rows, contract_first, preferred_element_type=jnp.float32)
        * score_scale
    )
    value_grad = lax.dot_general(
        probs_low, grad_rows, contract_first, preferred_element_type=jnp.float32
    )
    for g in range(group):
        dq_ref[:, g * HDIM : (g + 1) * HDIM] = query_grad[g * block_len : (g + 1) * block_len].astype(
            dq_ref.dtype
        )
    terms = jnp.stack(
        [key_grad.reshape(ntiles, block_len, HDIM), value_grad.reshape(ntiles, block_len, HDIM)],
        axis=1,
    )

    @pl.when(b == 0)
    def _():
        own_ref[...] = jnp.zeros_like(own_ref)
        glob_ref[...] = jnp.zeros_like(glob_ref)
        edge_ref[0] = terms[0]

    @pl.when(b > 0)
    def _():
        before = jnp.maximum(b - 1, 0)
        own_ref[before] = own_ref[before] + terms[0]

    own_ref[b] = own_ref[b] + terms[1]

    @pl.when(b < nblocks - 1)
    def _():
        after = jnp.minimum(b + 1, nblocks - 1)
        own_ref[after] = own_ref[after] + terms[2]

    @pl.when(b == nblocks - 1)
    def _():
        edge_ref[1] = terms[2]

    glob_ref[...] = glob_ref[...] + terms[3:near]
    rand_ref[...] = terms[near:].astype(rand_ref.dtype)


def block_backward(query_rows, grad_rows, all_blocks, tile_ids, key_live):
    shard_tokens, qwidth = query_rows.shape
    _, _, block_len, kwidth = all_blocks.shape
    nblocks, ntiles = tile_ids.shape
    heads_kv = kwidth // HDIM
    group_width = qwidth // heads_kv
    near = 3 + GLOB
    nrand = ntiles - near
    live = key_live.reshape(nblocks, 1, ntiles * block_len).astype(jnp.float32)
    row_spec = pl.BlockSpec((block_len, group_width), lambda h, b, ids: (b, h))
    tile_specs = [
        pl.BlockSpec(
            (None, 2, block_len, HDIM), lambda h, b, ids, t=t: (ids[b * ntiles + t], 0, 0, h)
        )
        for t in range(ntiles)
    ]
    live_spec = pl.BlockSpec((None, 1, ntiles * block_len), lambda h, b, ids: (b, 0, 0))
    own_spec = pl.BlockSpec((nblocks, 2, block_len, HDIM), lambda h, b, ids: (0, 0, 0, h))
    edge_spec = pl.BlockSpec((2, 2, block_len, HDIM), lambda h, b, ids: (0, 0, 0, h))
    glob_spec = pl.BlockSpec((GLOB, 2, block_len, HDIM), lambda h, b, ids: (0, 0, 0, h))
    rand_spec = pl.BlockSpec((None, nrand, 2, block_len, HDIM), lambda h, b, ids: (b, 0, 0, 0, h))
    flops = 12 * nblocks * heads_kv * (group_width // HDIM) * block_len * ntiles * block_len * HDIM
    grid_spec = pltpu.PrefetchScalarGridSpec(
        num_scalar_prefetch=1,
        grid=(heads_kv, nblocks),
        in_specs=[row_spec, row_spec, *tile_specs, live_spec],
        out_specs=[row_spec, own_spec, edge_spec, glob_spec, rand_spec],
    )
    outs = pl.pallas_call(
        attention_kernel,
        grid_spec=grid_spec,
        out_shape=[
            jax.ShapeDtypeStruct((shard_tokens, qwidth), jnp.bfloat16),
            jax.ShapeDtypeStruct((nblocks, 2, block_len, kwidth), jnp.float32),
            jax.ShapeDtypeStruct((2, 2, block_len, kwidth), jnp.float32),
            jax.ShapeDtypeStruct((GLOB, 2, block_len, kwidth), jnp.float32),
            jax.ShapeDtypeStruct((nblocks, nrand, 2, block_len, kwidth), jnp.bfloat16),
        ],
        compiler_params=pltpu.CompilerParams(
            dimension_semantics=("arbitrary", "arbitrary")
        ),
        cost_estimate=pl.CostEstimate(
            flops=flops,
            transcendentals=nblocks * qwidth // HDIM * block_len * ntiles * block_len,
            bytes_accessed=shard_tokens * qwidth * 6 + nblocks * ntiles * block_len * kwidth * 6,
        ),
    )(tile_ids.reshape(-1), query_rows, grad_rows, *([all_blocks] * ntiles), live)
    return outs


def request_plan(request_lists, this_shard, query_blocks):
    shards, count = request_lists.shape
    capacity = -(-count // shards)
    owner_ids = request_lists // query_blocks
    local_ids = request_lists % query_blocks
    order = jnp.arange(count, dtype=jnp.int32)
    earlier = order[None, :] < order[:, None]
    same_owner = owner_ids[:, :, None] == owner_ids[:, None, :]
    slot_rank = jnp.sum(same_owner & earlier[None], axis=2)
    slot_ids = jnp.arange(capacity, dtype=jnp.int32)
    chosen = (owner_ids[:, None, :] == this_shard) & (
        slot_rank[:, None, :] == slot_ids[None, :, None]
    )
    serve_block = jnp.sum(jnp.where(chosen, local_ids[:, None, :], 0), axis=2)
    slot_used = jnp.any(chosen, axis=2)
    owner_mine = lax.dynamic_index_in_dim(owner_ids, this_shard, 0, keepdims=False)
    rank_mine = lax.dynamic_index_in_dim(slot_rank, this_shard, 0, keepdims=False)
    return (serve_block, slot_used, owner_mine, rank_mine)


def serve_tiles(own_blocks, request_info):
    serve_block, slot_used = (request_info[0], request_info[1])
    shards, capacity = serve_block.shape
    gathered = jnp.take(own_blocks, serve_block.reshape(-1), axis=1)
    gathered = gathered.reshape(2, shards, capacity, own_blocks.shape[2], own_blocks.shape[3])
    return jnp.where(slot_used[None, :, :, None, None], gathered, jnp.zeros((), own_blocks.dtype))


def pick_tiles(received, request_info):
    return received[:, request_info[2], request_info[3]]


def place_terms(terms, request_info):
    serve_block = request_info[0]
    shards, capacity = serve_block.shape
    holder = jnp.zeros((2, shards, capacity, terms.shape[2], terms.shape[3]), terms.dtype)
    return holder.at[:, request_info[2], request_info[3]].set(terms)


def absorb_terms(received, request_info, query_blocks):
    serve_block, slot_used = (request_info[0], request_info[1])
    onehot = (
        slot_used[:, :, None]
        & (serve_block[:, :, None] == jnp.arange(query_blocks, dtype=jnp.int32)[None, None, :])
    ).astype(jnp.bfloat16)
    return jnp.einsum("ncq,xncsk->xqsk", onehot, received, preferred_element_type=jnp.float32)


def token_live(tile_ids, pad_sizes, query_blocks, shard_tokens, total_blocks):
    valid = (tile_ids >= 0) & (tile_ids < total_blocks)
    safe_ids = jnp.clip(tile_ids, 0, total_blocks - 1)
    owner_shard = safe_ids // query_blocks
    shards = pad_sizes.shape[0]
    pad_of = jnp.sum(
        jnp.where(owner_shard[..., None] == jnp.arange(shards, dtype=jnp.int32), pad_sizes, 0),
        axis=-1,
    )
    within = (safe_ids % query_blocks)[..., None] * BLK + jnp.arange(BLK, dtype=jnp.int32)
    return valid[..., None] & (within < (shard_tokens - pad_of)[..., None])


def body(queries, keys, values, out_grads, random_blocks, global_blocks, pad_lengths):
    query_rows = queries[0]
    key_rows = keys[0]
    value_rows = values[0]
    grad_rows = out_grads[0]
    random_table = random_blocks[0]
    global_ids = global_blocks[0]
    pad_sizes = pad_lengths[0]
    shards = lax.axis_size("seq")
    this_shard = lax.axis_index("seq")
    shard_tokens, qwidth = query_rows.shape
    kwidth = key_rows.shape[1]
    query_blocks = shard_tokens // BLK
    total_blocks = query_blocks * shards
    own_blocks = jnp.stack(
        [key_rows.reshape(query_blocks, BLK, kwidth), value_rows.reshape(query_blocks, BLK, kwidth)],
        axis=1,
    )
    up = [(i, (i + 1) % shards) for i in range(shards - 1)]
    down = [(j, i) for i, j in up]
    edge_before = lax.ppermute(own_blocks[query_blocks - 1 :], "seq", up)
    edge_after = lax.ppermute(own_blocks[:1], "seq", down)
    global_mine = [
        jnp.where(
            global_ids[g] // query_blocks == this_shard,
            lax.dynamic_index_in_dim(own_blocks, global_ids[g] % query_blocks, 0, keepdims=True),
            jnp.zeros((), own_blocks.dtype),
        )
        for g in range(GLOB)
    ]
    global_tiles = tree_sum(jnp.concatenate(global_mine, axis=0), "seq")
    requests = random_table.reshape(shards, query_blocks * RAND)
    plan = request_plan(requests, this_shard, query_blocks)
    serve_block, slot_used, owner_mine, rank_mine = plan
    capacity = serve_block.shape[1]
    served = jnp.take(own_blocks, serve_block.reshape(-1), axis=0)
    received = lax.all_to_all(served, "seq", 0, 0, tiled=True)
    sources = jnp.concatenate([own_blocks, edge_before, edge_after, global_tiles, received], axis=0)
    nb = query_blocks
    block_range = jnp.arange(nb, dtype=jnp.int32)
    source_ids = jnp.concatenate(
        [
            jnp.where(block_range == 0, nb, block_range - 1)[:, None],
            block_range[:, None],
            jnp.where(block_range == nb - 1, nb + 1, block_range + 1)[:, None],
            jnp.broadcast_to(nb + 2 + jnp.arange(GLOB, dtype=jnp.int32)[None, :], (nb, GLOB)),
            (nb + 2 + GLOB + owner_mine * capacity + rank_mine).reshape(nb, RAND),
        ],
        axis=1,
    )
    source_ids = jnp.clip(source_ids, 0, sources.shape[0] - 1)
    random_three = random_table.reshape(shards, query_blocks, RAND)
    base_ids = this_shard * query_blocks + block_range
    window_ids = base_ids[:, None] + jnp.arange(-1, 2, dtype=jnp.int32)[None, :]
    my_random = lax.dynamic_index_in_dim(random_three, this_shard, 0, keepdims=False)
    tile_ids = jnp.concatenate(
        [window_ids, jnp.broadcast_to(global_ids[None, :], (query_blocks, GLOB)), my_random], axis=1
    )
    key_live = token_live(tile_ids, pad_sizes, query_blocks, shard_tokens, total_blocks)
    query_grad, local_sum, edge_terms, global_part, random_part = block_backward(
        query_rows, grad_rows, sources, source_ids, key_live
    )
    handed_query = from_behind(query_grad, "section", -1)
    edge_low = edge_terms.astype(jnp.bfloat16)
    from_after = lax.ppermute(edge_low[:1], "seq", down)
    from_before = lax.ppermute(edge_low[1:], "seq", up)
    holder = jnp.zeros((shards, capacity, 2, BLK, kwidth), random_part.dtype)
    holder = holder.at[owner_mine, rank_mine].set(
        random_part.reshape(query_blocks * RAND, 2, BLK, kwidth)
    )
    returned = lax.all_to_all(
        holder.reshape(shards * capacity, 2, BLK, kwidth), "seq", 0, 0, tiled=True
    )
    onehot = (
        slot_used.reshape(-1)[None, :]
        & (serve_block.reshape(-1)[None, :] == block_range[:, None])
    ).astype(jnp.bfloat16)
    kv_sum = local_sum + jnp.einsum(
        "qf,fxsk->qxsk", onehot, returned, preferred_element_type=jnp.float32
    )
    kv_sum = kv_sum.at[nb - 1].add(from_after[0].astype(jnp.float32))
    kv_sum = kv_sum.at[0].add(from_before[0].astype(jnp.float32))
    global_total = tree_sum(global_part, "seq")
    global_pick = (
        (global_ids[:, None] // query_blocks == this_shard)
        & (global_ids[:, None] % query_blocks == block_range[None, :])
    ).astype(jnp.float32)
    kv_sum = kv_sum + jnp.einsum(
        "gq,gxsk->qxsk", global_pick, global_total, precision=lax.Precision.HIGHEST
    )
    kv_grad = jnp.concatenate(
        [
            kv_sum[:, 0].reshape(shard_tokens, kwidth).astype(jnp.bfloat16),
            kv_sum[:, 1].reshape(shard_tokens, kwidth).astype(jnp.bfloat16),
        ],
        axis=-1,
    )
    handed_kv = from_behind(kv_grad, "section", -1)
    return (
        handed_query[None],
        handed_kv[None, :, :kwidth],
        handed_kv[None, :, kwidth:],
    )


def solution(mesh):
    in_specs = (
        P("section", "seq", None),
        P("section", "seq", None),
        P("section", "seq", None),
        P("section", "seq", None),
        P("section", None, None),
        P("section", None),
        P("section", None),
    )
    out_specs = (P("section", "seq", None), P("section", "seq", None), P("section", "seq", None))
    return jax.shard_map(body, mesh=mesh, in_specs=in_specs, out_specs=out_specs, check_vma=False)
```

```python
import math

import jax
import jax.numpy as jnp
from jax import lax
from jax.experimental import pallas as pl
from jax.experimental.pallas import tpu as pltpu
from jax.sharding import PartitionSpec as P

HDIM = 128
BLK = 64
GLOB = 2
RAND = 3


def extended_2(array, sides, width):
    for axis, dim in sides:
        devices, length = (lax.axis_size(axis), array.shape[dim])
        up = [(i, (i + 1) % devices) for i in range(devices - 1)]
        down = [(j, i) for i, j in up]
        last = lax.slice_in_dim(array, length - width, length, axis=dim)
        leading = lax.slice_in_dim(array, 0, width, axis=dim)
        before = lax.ppermute(last, axis, up)
        after = lax.ppermute(leading, axis, down)
        array = jnp.concatenate([before, array, after], axis=dim)
    return array


def broadcast(array, axis, root):
    mine = lax.axis_index(axis) == root
    return lax.psum(jnp.where(mine, array, jnp.zeros_like(array)), axis)


def from_behind(block, axis, distance):
    devices = range(lax.axis_size(axis))
    route = [((i - distance) % len(devices), i) for i in devices]
    return lax.ppermute(block, axis, route)


def tree_sum(array, axis):
    devices = lax.axis_size(axis)
    if devices & (devices - 1):
        return lax.psum(array, axis)
    step = 1
    while step < devices:
        array = array + lax.ppermute(array, axis, [(i, i ^ step) for i in range(devices)])
        step *= 2
    return array


def attention_kernel(ids_ref, q_ref, g_ref, *refs):
    del ids_ref
    ntiles = len(refs) - 6
    tile_refs = refs[:ntiles]
    live_ref = refs[ntiles]
    dq_ref, own_ref, edge_ref, glob_ref, rand_ref = refs[ntiles + 1 :]
    nblocks = own_ref.shape[0]
    block_len, width = q_ref.shape
    group = width // HDIM
    near = 3 + GLOB
    b = pl.program_id(1)
    score_scale = 1.0 / math.sqrt(HDIM)
    query = q_ref[...]
    grad = g_ref[...]
    query_rows = jnp.concatenate(
        [query[:, g * HDIM : (g + 1) * HDIM] for g in range(group)], axis=0
    )
    grad_rows = jnp.concatenate([grad[:, g * HDIM : (g + 1) * HDIM] for g in range(group)], axis=0)
    key_rows = jnp.concatenate([tile_refs[t][0] for t in range(ntiles)], axis=0)
    value_rows = jnp.concatenate([tile_refs[t][1] for t in range(ntiles)], axis=0)
    live = live_ref[...] > 0.5
    contract_last = (((1,), (1,)), ((), ()))
    contract_first = (((0,), (0,)), ((), ()))
    scores = (
        lax.dot_general(key_rows, query_rows, contract_last, preferred_element_type=jnp.float32)
        * score_scale
    )
    scores = jnp.where(live, scores, -1e30)
    row_max = jnp.max(scores, axis=0, keepdims=True)
    shifted = jnp.exp(scores - row_max)
    total = jnp.sum(shifted, axis=0, keepdims=True)
    probs = shifted * (1.0 / total)
    probs_low = probs.astype(jnp.bfloat16)
    output = lax.dot_general(
        value_rows, probs_low, contract_first, preferred_element_type=jnp.float32
    )
    grad_cols = grad_rows.astype(jnp.float32).T
    row_dot = jnp.sum(grad_cols * output, axis=0, keepdims=True)
    prob_grad = lax.dot_general(
        value_rows, grad_rows, contract_last, preferred_element_type=jnp.float32
    )
    score_grad = (probs * (prob_grad - row_dot)).astype(jnp.bfloat16)
    query_grad = (
        lax.dot_general(key_rows, score_grad, contract_first, preferred_element_type=jnp.float32)
        * score_scale
    ).T
    key_grad = jnp.dot(score_grad, query_rows, preferred_element_type=jnp.float32) * score_scale
    value_grad = jnp.dot(probs_low, grad_rows, preferred_element_type=jnp.float32)
    for g in range(group):
        dq_ref[:, g * HDIM : (g + 1) * HDIM] = query_grad[g * block_len : (g + 1) * block_len].astype(
            dq_ref.dtype
        )
    terms = jnp.stack(
        [key_grad.reshape(ntiles, block_len, HDIM), value_grad.reshape(ntiles, block_len, HDIM)],
        axis=1,
    )

    @pl.when(b == 0)
    def _():
        own_ref[...] = jnp.zeros_like(own_ref)
        glob_ref[...] = jnp.zeros_like(glob_ref)
        edge_ref[0] = terms[0]

    @pl.when(b > 0)
    def _():
        before = jnp.maximum(b - 1, 0)
        own_ref[before] = own_ref[before] + terms[0]

    own_ref[b] = own_ref[b] + terms[1]

    @pl.when(b < nblocks - 1)
    def _():
        after = jnp.minimum(b + 1, nblocks - 1)
        own_ref[after] = own_ref[after] + terms[2]

    @pl.when(b == nblocks - 1)
    def _():
        edge_ref[1] = terms[2]

    glob_ref[...] = glob_ref[...] + terms[3:near]
    rand_ref[...] = terms[near:].astype(rand_ref.dtype)


def block_backward(query_rows, grad_rows, all_blocks, tile_ids, key_live):
    shard_tokens, qwidth = query_rows.shape
    _, _, block_len, kwidth = all_blocks.shape
    nblocks, ntiles = tile_ids.shape
    heads_kv = kwidth // HDIM
    group_width = qwidth // heads_kv
    near = 3 + GLOB
    nrand = ntiles - near
    live = key_live.reshape(nblocks, ntiles * block_len, 1).astype(jnp.float32)
    row_spec = pl.BlockSpec((block_len, group_width), lambda h, b, ids: (b, h))
    tile_specs = [
        pl.BlockSpec(
            (None, 2, block_len, HDIM), lambda h, b, ids, t=t: (ids[b * ntiles + t], 0, 0, h)
        )
        for t in range(ntiles)
    ]
    live_spec = pl.BlockSpec((None, ntiles * block_len, 1), lambda h, b, ids: (b, 0, 0))
    own_spec = pl.BlockSpec((nblocks, 2, block_len, HDIM), lambda h, b, ids: (0, 0, 0, h))
    edge_spec = pl.BlockSpec((2, 2, block_len, HDIM), lambda h, b, ids: (0, 0, 0, h))
    glob_spec = pl.BlockSpec((GLOB, 2, block_len, HDIM), lambda h, b, ids: (0, 0, 0, h))
    rand_spec = pl.BlockSpec((None, nrand, 2, block_len, HDIM), lambda h, b, ids: (b, 0, 0, 0, h))
    flops = 12 * nblocks * heads_kv * (group_width // HDIM) * block_len * ntiles * block_len * HDIM
    grid_spec = pltpu.PrefetchScalarGridSpec(
        num_scalar_prefetch=1,
        grid=(heads_kv, nblocks),
        in_specs=[row_spec, row_spec, *tile_specs, live_spec],
        out_specs=[row_spec, own_spec, edge_spec, glob_spec, rand_spec],
    )
    outs = pl.pallas_call(
        attention_kernel,
        grid_spec=grid_spec,
        out_shape=[
            jax.ShapeDtypeStruct((shard_tokens, qwidth), jnp.bfloat16),
            jax.ShapeDtypeStruct((nblocks, 2, block_len, kwidth), jnp.float32),
            jax.ShapeDtypeStruct((2, 2, block_len, kwidth), jnp.float32),
            jax.ShapeDtypeStruct((GLOB, 2, block_len, kwidth), jnp.float32),
            jax.ShapeDtypeStruct((nblocks, nrand, 2, block_len, kwidth), jnp.bfloat16),
        ],
        compiler_params=pltpu.CompilerParams(
            dimension_semantics=("arbitrary", "arbitrary")
        ),
        cost_estimate=pl.CostEstimate(
            flops=flops,
            transcendentals=nblocks * qwidth // HDIM * block_len * ntiles * block_len,
            bytes_accessed=shard_tokens * qwidth * 6 + nblocks * ntiles * block_len * kwidth * 6,
        ),
    )(tile_ids.reshape(-1), query_rows, grad_rows, *([all_blocks] * ntiles), live)
    return outs


def request_plan(request_lists, this_shard, query_blocks):
    shards, count = request_lists.shape
    capacity = -(-count // shards)
    owner_ids = request_lists // query_blocks
    local_ids = request_lists % query_blocks
    order = jnp.arange(count, dtype=jnp.int32)
    earlier = order[None, :] < order[:, None]
    same_owner = owner_ids[:, :, None] == owner_ids[:, None, :]
    slot_rank = jnp.sum(same_owner & earlier[None], axis=2)
    slot_ids = jnp.arange(capacity, dtype=jnp.int32)
    chosen = (owner_ids[:, None, :] == this_shard) & (
        slot_rank[:, None, :] == slot_ids[None, :, None]
    )
    serve_block = jnp.sum(jnp.where(chosen, local_ids[:, None, :], 0), axis=2)
    slot_used = jnp.any(chosen, axis=2)
    owner_mine = lax.dynamic_index_in_dim(owner_ids, this_shard, 0, keepdims=False)
    rank_mine = lax.dynamic_index_in_dim(slot_rank, this_shard, 0, keepdims=False)
    return (serve_block, slot_used, owner_mine, rank_mine)


def serve_tiles(own_blocks, request_info):
    serve_block, slot_used = (request_info[0], request_info[1])
    shards, capacity = serve_block.shape
    gathered = jnp.take(own_blocks, serve_block.reshape(-1), axis=1)
    gathered = gathered.reshape(2, shards, capacity, own_blocks.shape[2], own_blocks.shape[3])
    return jnp.where(slot_used[None, :, :, None, None], gathered, jnp.zeros((), own_blocks.dtype))


def pick_tiles(received, request_info):
    return received[:, request_info[2], request_info[3]]


def place_terms(terms, request_info):
    serve_block = request_info[0]
    shards, capacity = serve_block.shape
    holder = jnp.zeros((2, shards, capacity, terms.shape[2], terms.shape[3]), terms.dtype)
    return holder.at[:, request_info[2], request_info[3]].set(terms)


def absorb_terms(received, request_info, query_blocks):
    serve_block, slot_used = (request_info[0], request_info[1])
    onehot = (
        slot_used[:, :, None]
        & (serve_block[:, :, None] == jnp.arange(query_blocks, dtype=jnp.int32)[None, None, :])
    ).astype(jnp.bfloat16)
    return jnp.einsum("ncq,xncsk->xqsk", onehot, received, preferred_element_type=jnp.float32)


def token_live(tile_ids, pad_sizes, query_blocks, shard_tokens, total_blocks):
    valid = (tile_ids >= 0) & (tile_ids < total_blocks)
    safe_ids = jnp.clip(tile_ids, 0, total_blocks - 1)
    owner_shard = safe_ids // query_blocks
    shards = pad_sizes.shape[0]
    pad_of = jnp.sum(
        jnp.where(owner_shard[..., None] == jnp.arange(shards, dtype=jnp.int32), pad_sizes, 0),
        axis=-1,
    )
    within = (safe_ids % query_blocks)[..., None] * BLK + jnp.arange(BLK, dtype=jnp.int32)
    return valid[..., None] & (within < (shard_tokens - pad_of)[..., None])


def body(queries, keys, values, out_grads, random_blocks, global_blocks, pad_lengths):
    query_rows = queries[0]
    key_rows = keys[0]
    value_rows = values[0]
    grad_rows = out_grads[0]
    random_table = random_blocks[0]
    global_ids = global_blocks[0]
    pad_sizes = pad_lengths[0]
    shards = lax.axis_size("seq")
    this_shard = lax.axis_index("seq")
    shard_tokens, qwidth = query_rows.shape
    kwidth = key_rows.shape[1]
    query_blocks = shard_tokens // BLK
    total_blocks = query_blocks * shards
    own_blocks = jnp.stack(
        [key_rows.reshape(query_blocks, BLK, kwidth), value_rows.reshape(query_blocks, BLK, kwidth)],
        axis=1,
    )
    up = [(i, (i + 1) % shards) for i in range(shards - 1)]
    down = [(j, i) for i, j in up]
    edge_before = lax.ppermute(own_blocks[query_blocks - 1 :], "seq", up)
    edge_after = lax.ppermute(own_blocks[:1], "seq", down)
    global_mine = [
        jnp.where(
            global_ids[g] // query_blocks == this_shard,
            lax.dynamic_index_in_dim(own_blocks, global_ids[g] % query_blocks, 0, keepdims=True),
            jnp.zeros((), own_blocks.dtype),
        )
        for g in range(GLOB)
    ]
    global_tiles = tree_sum(jnp.concatenate(global_mine, axis=0), "seq")
    requests = random_table.reshape(shards, query_blocks * RAND)
    plan = request_plan(requests, this_shard, query_blocks)
    serve_block, slot_used, owner_mine, rank_mine = plan
    capacity = serve_block.shape[1]
    served = jnp.take(own_blocks, serve_block.reshape(-1), axis=0)
    received = lax.all_to_all(served, "seq", 0, 0, tiled=True)
    sources = jnp.concatenate([own_blocks, edge_before, edge_after, global_tiles, received], axis=0)
    nb = query_blocks
    block_range = jnp.arange(nb, dtype=jnp.int32)
    source_ids = jnp.concatenate(
        [
            jnp.where(block_range == 0, nb, block_range - 1)[:, None],
            block_range[:, None],
            jnp.where(block_range == nb - 1, nb + 1, block_range + 1)[:, None],
            jnp.broadcast_to(nb + 2 + jnp.arange(GLOB, dtype=jnp.int32)[None, :], (nb, GLOB)),
            (nb + 2 + GLOB + owner_mine * capacity + rank_mine).reshape(nb, RAND),
        ],
        axis=1,
    )
    source_ids = jnp.clip(source_ids, 0, sources.shape[0] - 1)
    random_three = random_table.reshape(shards, query_blocks, RAND)
    base_ids = this_shard * query_blocks + block_range
    window_ids = base_ids[:, None] + jnp.arange(-1, 2, dtype=jnp.int32)[None, :]
    my_random = lax.dynamic_index_in_dim(random_three, this_shard, 0, keepdims=False)
    tile_ids = jnp.concatenate(
        [window_ids, jnp.broadcast_to(global_ids[None, :], (query_blocks, GLOB)), my_random], axis=1
    )
    key_live = token_live(tile_ids, pad_sizes, query_blocks, shard_tokens, total_blocks)
    query_grad, local_sum, edge_terms, global_part, random_part = block_backward(
        query_rows, grad_rows, sources, source_ids, key_live
    )
    handed_query = from_behind(query_grad, "section", -1)
    edge_low = edge_terms.astype(jnp.bfloat16)
    from_after = lax.ppermute(edge_low[:1], "seq", down)
    from_before = lax.ppermute(edge_low[1:], "seq", up)
    holder = jnp.zeros((shards, capacity, 2, BLK, kwidth), random_part.dtype)
    holder = holder.at[owner_mine, rank_mine].set(
        random_part.reshape(query_blocks * RAND, 2, BLK, kwidth)
    )
    returned = lax.all_to_all(
        holder.reshape(shards * capacity, 2, BLK, kwidth), "seq", 0, 0, tiled=True
    )
    onehot = (
        slot_used.reshape(-1)[None, :]
        & (serve_block.reshape(-1)[None, :] == block_range[:, None])
    ).astype(jnp.bfloat16)
    kv_sum = local_sum + jnp.einsum(
        "qf,fxsk->qxsk", onehot, returned, preferred_element_type=jnp.float32
    )
    kv_sum = kv_sum.at[nb - 1].add(from_after[0].astype(jnp.float32))
    kv_sum = kv_sum.at[0].add(from_before[0].astype(jnp.float32))
    global_total = tree_sum(global_part, "seq")
    global_pick = (
        (global_ids[:, None] // query_blocks == this_shard)
        & (global_ids[:, None] % query_blocks == block_range[None, :])
    ).astype(jnp.float32)
    kv_sum = kv_sum + jnp.einsum(
        "gq,gxsk->qxsk", global_pick, global_total, precision=lax.Precision.HIGHEST
    )
    kv_grad = jnp.concatenate(
        [
            kv_sum[:, 0].reshape(shard_tokens, kwidth).astype(jnp.bfloat16),
            kv_sum[:, 1].reshape(shard_tokens, kwidth).astype(jnp.bfloat16),
        ],
        axis=-1,
    )
    handed_kv = from_behind(kv_grad, "section", -1)
    return (
        handed_query[None],
        handed_kv[None, :, :kwidth],
        handed_kv[None, :, kwidth:],
    )


def solution(mesh):
    in_specs = (
        P("section", "seq", None),
        P("section", "seq", None),
        P("section", "seq", None),
        P("section", "seq", None),
        P("section", None, None),
        P("section", None),
        P("section", None),
    )
    out_specs = (P("section", "seq", None), P("section", "seq", None), P("section", "seq", None))
    return jax.shard_map(body, mesh=mesh, in_specs=in_specs, out_specs=out_specs, check_vma=False)
```

```python
import math

import jax
import jax.numpy as jnp
from jax import lax
from jax.experimental import pallas as pl
from jax.experimental.pallas import tpu as pltpu
from jax.sharding import PartitionSpec as P

HDIM = 128
BLK = 64
GLOB = 2
RAND = 3


def extended_2(array, sides, width):
    for axis, dim in sides:
        devices, length = (lax.axis_size(axis), array.shape[dim])
        up = [(i, (i + 1) % devices) for i in range(devices - 1)]
        down = [(j, i) for i, j in up]
        last = lax.slice_in_dim(array, length - width, length, axis=dim)
        leading = lax.slice_in_dim(array, 0, width, axis=dim)
        before = lax.ppermute(last, axis, up)
        after = lax.ppermute(leading, axis, down)
        array = jnp.concatenate([before, array, after], axis=dim)
    return array


def broadcast(array, axis, root):
    mine = lax.axis_index(axis) == root
    return lax.psum(jnp.where(mine, array, jnp.zeros_like(array)), axis)


def from_behind(block, axis, distance):
    devices = range(lax.axis_size(axis))
    route = [((i - distance) % len(devices), i) for i in devices]
    return lax.ppermute(block, axis, route)


def tree_sum(array, axis):
    devices = lax.axis_size(axis)
    if devices & (devices - 1):
        return lax.psum(array, axis)
    step = 1
    while step < devices:
        array = array + lax.ppermute(array, axis, [(i, i ^ step) for i in range(devices)])
        step *= 2
    return array


def attention_kernel(ids_ref, q_ref, g_ref, *refs):
    del ids_ref
    ntiles = len(refs) - 6
    tile_refs = refs[:ntiles]
    live_ref = refs[ntiles]
    dq_ref, own_ref, edge_ref, glob_ref, rand_ref = refs[ntiles + 1 :]
    nblocks = own_ref.shape[0]
    block_len, width = q_ref.shape
    group = width // HDIM
    near = 3 + GLOB
    b = pl.program_id(1)
    score_scale = 1.0 / math.sqrt(HDIM)
    query = q_ref[...]
    grad = g_ref[...]
    query_rows = jnp.concatenate(
        [query[:, g * HDIM : (g + 1) * HDIM] for g in range(group)], axis=0
    )
    grad_rows = jnp.concatenate([grad[:, g * HDIM : (g + 1) * HDIM] for g in range(group)], axis=0)
    key_rows = jnp.concatenate([tile_refs[t][0] for t in range(ntiles)], axis=0)
    value_rows = jnp.concatenate([tile_refs[t][1] for t in range(ntiles)], axis=0)
    live = live_ref[...] > 0.5
    contract_last = (((1,), (1,)), ((), ()))
    contract_first = (((0,), (0,)), ((), ()))
    scores = (
        lax.dot_general(key_rows, query_rows, contract_last, preferred_element_type=jnp.float32)
        * score_scale
    )
    scores = jnp.where(live, scores, -1e30)
    row_max = jnp.max(scores, axis=0, keepdims=True)
    shifted = jnp.exp(scores - row_max)
    total = jnp.sum(shifted, axis=0, keepdims=True)
    probs = shifted * (1.0 / total)
    probs_low = probs.astype(jnp.bfloat16)
    output = lax.dot_general(
        value_rows, probs_low, contract_first, preferred_element_type=jnp.float32
    )
    grad_cols = grad_rows.astype(jnp.float32).T
    row_dot = jnp.sum(grad_cols * output, axis=0, keepdims=True)
    prob_grad = lax.dot_general(
        value_rows, grad_rows, contract_last, preferred_element_type=jnp.float32
    )
    score_grad = (probs * (prob_grad - row_dot)).astype(jnp.bfloat16)
    query_grad = (
        lax.dot_general(key_rows, score_grad, contract_first, preferred_element_type=jnp.float32)
        * score_scale
    ).T
    key_grad = jnp.dot(score_grad, query_rows, preferred_element_type=jnp.float32) * score_scale
    value_grad = jnp.dot(probs_low, grad_rows, preferred_element_type=jnp.float32)
    for g in range(group):
        dq_ref[:, g * HDIM : (g + 1) * HDIM] = query_grad[g * block_len : (g + 1) * block_len].astype(
            dq_ref.dtype
        )
    terms = jnp.stack(
        [key_grad.reshape(ntiles, block_len, HDIM), value_grad.reshape(ntiles, block_len, HDIM)],
        axis=1,
    )

    @pl.when(b == 0)
    def _():
        own_ref[...] = jnp.zeros_like(own_ref)
        glob_ref[...] = jnp.zeros_like(glob_ref)
        edge_ref[0] = terms[0]

    @pl.when(b > 0)
    def _():
        before = jnp.maximum(b - 1, 0)
        own_ref[before] = own_ref[before] + terms[0]

    own_ref[b] = own_ref[b] + terms[1]

    @pl.when(b < nblocks - 1)
    def _():
        after = jnp.minimum(b + 1, nblocks - 1)
        own_ref[after] = own_ref[after] + terms[2]

    @pl.when(b == nblocks - 1)
    def _():
        edge_ref[1] = terms[2]

    glob_ref[...] = glob_ref[...] + terms[3:near]
    rand_ref[...] = terms[near:].astype(rand_ref.dtype)


def block_backward(query_rows, grad_rows, all_blocks, tile_ids, key_live):
    shard_tokens, qwidth = query_rows.shape
    _, _, block_len, kwidth = all_blocks.shape
    nblocks, ntiles = tile_ids.shape
    heads_kv = kwidth // HDIM
    group_width = qwidth // heads_kv
    near = 3 + GLOB
    nrand = ntiles - near
    live = key_live.reshape(nblocks, ntiles * block_len, 1).astype(jnp.float32)
    row_spec = pl.BlockSpec((block_len, group_width), lambda h, b, ids: (b, h))
    tile_specs = [
        pl.BlockSpec(
            (None, 2, block_len, HDIM), lambda h, b, ids, t=t: (ids[b * ntiles + t], 0, 0, h)
        )
        for t in range(ntiles)
    ]
    live_spec = pl.BlockSpec((None, ntiles * block_len, 1), lambda h, b, ids: (b, 0, 0))
    own_spec = pl.BlockSpec((nblocks, 2, block_len, HDIM), lambda h, b, ids: (0, 0, 0, h))
    edge_spec = pl.BlockSpec((2, 2, block_len, HDIM), lambda h, b, ids: (0, 0, 0, h))
    glob_spec = pl.BlockSpec((GLOB, 2, block_len, HDIM), lambda h, b, ids: (0, 0, 0, h))
    rand_spec = pl.BlockSpec((None, nrand, 2, block_len, HDIM), lambda h, b, ids: (b, 0, 0, 0, h))
    flops = 12 * nblocks * heads_kv * (group_width // HDIM) * block_len * ntiles * block_len * HDIM
    grid_spec = pltpu.PrefetchScalarGridSpec(
        num_scalar_prefetch=1,
        grid=(heads_kv, nblocks),
        in_specs=[row_spec, row_spec, *tile_specs, live_spec],
        out_specs=[row_spec, own_spec, edge_spec, glob_spec, rand_spec],
    )
    outs = pl.pallas_call(
        attention_kernel,
        grid_spec=grid_spec,
        out_shape=[
            jax.ShapeDtypeStruct((shard_tokens, qwidth), jnp.bfloat16),
            jax.ShapeDtypeStruct((nblocks, 2, block_len, kwidth), jnp.float32),
            jax.ShapeDtypeStruct((2, 2, block_len, kwidth), jnp.float32),
            jax.ShapeDtypeStruct((GLOB, 2, block_len, kwidth), jnp.float32),
            jax.ShapeDtypeStruct((nblocks, nrand, 2, block_len, kwidth), jnp.bfloat16),
        ],
        compiler_params=pltpu.CompilerParams(
            dimension_semantics=("arbitrary", "arbitrary")
        ),
        cost_estimate=pl.CostEstimate(
            flops=flops,
            transcendentals=nblocks * qwidth // HDIM * block_len * ntiles * block_len,
            bytes_accessed=shard_tokens * qwidth * 6 + nblocks * ntiles * block_len * kwidth * 6,
        ),
    )(tile_ids.reshape(-1), query_rows, grad_rows, *([all_blocks] * ntiles), live)
    return outs


def request_plan(request_lists, this_shard, query_blocks):
    shards, count = request_lists.shape
    capacity = -(-count // shards)
    owner_ids = request_lists // query_blocks
    local_ids = request_lists % query_blocks
    order = jnp.arange(count, dtype=jnp.int32)
    earlier = order[None, :] < order[:, None]
    same_owner = owner_ids[:, :, None] == owner_ids[:, None, :]
    slot_rank = jnp.sum(same_owner & earlier[None], axis=2)
    slot_ids = jnp.arange(capacity, dtype=jnp.int32)
    chosen = (owner_ids[:, None, :] == this_shard) & (
        slot_rank[:, None, :] == slot_ids[None, :, None]
    )
    serve_block = jnp.sum(jnp.where(chosen, local_ids[:, None, :], 0), axis=2)
    slot_used = jnp.any(chosen, axis=2)
    owner_mine = lax.dynamic_index_in_dim(owner_ids, this_shard, 0, keepdims=False)
    rank_mine = lax.dynamic_index_in_dim(slot_rank, this_shard, 0, keepdims=False)
    return (serve_block, slot_used, owner_mine, rank_mine)


def serve_tiles(own_blocks, request_info):
    serve_block, slot_used = (request_info[0], request_info[1])
    shards, capacity = serve_block.shape
    gathered = jnp.take(own_blocks, serve_block.reshape(-1), axis=1)
    gathered = gathered.reshape(2, shards, capacity, own_blocks.shape[2], own_blocks.shape[3])
    return jnp.where(slot_used[None, :, :, None, None], gathered, jnp.zeros((), own_blocks.dtype))


def pick_tiles(received, request_info):
    return received[:, request_info[2], request_info[3]]


def place_terms(terms, request_info):
    serve_block = request_info[0]
    shards, capacity = serve_block.shape
    holder = jnp.zeros((2, shards, capacity, terms.shape[2], terms.shape[3]), terms.dtype)
    return holder.at[:, request_info[2], request_info[3]].set(terms)


def absorb_terms(received, request_info, query_blocks):
    serve_block, slot_used = (request_info[0], request_info[1])
    onehot = (
        slot_used[:, :, None]
        & (serve_block[:, :, None] == jnp.arange(query_blocks, dtype=jnp.int32)[None, None, :])
    ).astype(jnp.bfloat16)
    return jnp.einsum("ncq,xncsk->xqsk", onehot, received, preferred_element_type=jnp.float32)


def token_live(tile_ids, pad_sizes, query_blocks, shard_tokens, total_blocks):
    valid = (tile_ids >= 0) & (tile_ids < total_blocks)
    safe_ids = jnp.clip(tile_ids, 0, total_blocks - 1)
    owner_shard = safe_ids // query_blocks
    shards = pad_sizes.shape[0]
    pad_of = jnp.sum(
        jnp.where(owner_shard[..., None] == jnp.arange(shards, dtype=jnp.int32), pad_sizes, 0),
        axis=-1,
    )
    within = (safe_ids % query_blocks)[..., None] * BLK + jnp.arange(BLK, dtype=jnp.int32)
    return valid[..., None] & (within < (shard_tokens - pad_of)[..., None])


def body(queries, keys, values, out_grads, random_blocks, global_blocks, pad_lengths):
    query_rows = queries[0]
    key_rows = keys[0]
    value_rows = values[0]
    grad_rows = out_grads[0]
    random_table = random_blocks[0]
    global_ids = global_blocks[0]
    pad_sizes = pad_lengths[0]
    shards = lax.axis_size("seq")
    this_shard = lax.axis_index("seq")
    shard_tokens, qwidth = query_rows.shape
    kwidth = key_rows.shape[1]
    query_blocks = shard_tokens // BLK
    total_blocks = query_blocks * shards
    own_blocks = jnp.stack(
        [key_rows.reshape(query_blocks, BLK, kwidth), value_rows.reshape(query_blocks, BLK, kwidth)],
        axis=1,
    )
    up = [(i, (i + 1) % shards) for i in range(shards - 1)]
    down = [(j, i) for i, j in up]
    edge_before = lax.ppermute(own_blocks[query_blocks - 1 :], "seq", up)
    edge_after = lax.ppermute(own_blocks[:1], "seq", down)
    global_mine = [
        jnp.where(
            global_ids[g] // query_blocks == this_shard,
            lax.dynamic_index_in_dim(own_blocks, global_ids[g] % query_blocks, 0, keepdims=True),
            jnp.zeros((), own_blocks.dtype),
        )
        for g in range(GLOB)
    ]
    global_tiles = tree_sum(jnp.concatenate(global_mine, axis=0), "seq")
    requests = random_table.reshape(shards, query_blocks * RAND)
    plan = request_plan(requests, this_shard, query_blocks)
    serve_block, slot_used, owner_mine, rank_mine = plan
    capacity = serve_block.shape[1]
    served = jnp.take(own_blocks, serve_block.reshape(-1), axis=0)
    served, global_tiles = lax.optimization_barrier((served, global_tiles))
    received = lax.all_to_all(served, "seq", 0, 0, tiled=True)
    sources = jnp.concatenate([own_blocks, edge_before, edge_after, global_tiles, received], axis=0)
    nb = query_blocks
    block_range = jnp.arange(nb, dtype=jnp.int32)
    source_ids = jnp.concatenate(
        [
            jnp.where(block_range == 0, nb, block_range - 1)[:, None],
            block_range[:, None],
            jnp.where(block_range == nb - 1, nb + 1, block_range + 1)[:, None],
            jnp.broadcast_to(nb + 2 + jnp.arange(GLOB, dtype=jnp.int32)[None, :], (nb, GLOB)),
            (nb + 2 + GLOB + owner_mine * capacity + rank_mine).reshape(nb, RAND),
        ],
        axis=1,
    )
    source_ids = jnp.clip(source_ids, 0, sources.shape[0] - 1)
    random_three = random_table.reshape(shards, query_blocks, RAND)
    base_ids = this_shard * query_blocks + block_range
    window_ids = base_ids[:, None] + jnp.arange(-1, 2, dtype=jnp.int32)[None, :]
    my_random = lax.dynamic_index_in_dim(random_three, this_shard, 0, keepdims=False)
    tile_ids = jnp.concatenate(
        [window_ids, jnp.broadcast_to(global_ids[None, :], (query_blocks, GLOB)), my_random], axis=1
    )
    key_live = token_live(tile_ids, pad_sizes, query_blocks, shard_tokens, total_blocks)
    query_grad, local_sum, edge_terms, global_part, random_part = block_backward(
        query_rows, grad_rows, sources, source_ids, key_live
    )
    handed_query = from_behind(query_grad, "section", -1)
    edge_low = edge_terms.astype(jnp.bfloat16)
    from_after = lax.ppermute(edge_low[:1], "seq", down)
    from_before = lax.ppermute(edge_low[1:], "seq", up)
    holder = jnp.zeros((shards, capacity, 2, BLK, kwidth), random_part.dtype)
    holder = holder.at[owner_mine, rank_mine].set(
        random_part.reshape(query_blocks * RAND, 2, BLK, kwidth)
    )
    global_total = tree_sum(global_part, "seq")
    holder, global_total = lax.optimization_barrier((holder, global_total))
    returned = lax.all_to_all(
        holder.reshape(shards * capacity, 2, BLK, kwidth), "seq", 0, 0, tiled=True
    )
    onehot = (
        slot_used.reshape(-1)[None, :]
        & (serve_block.reshape(-1)[None, :] == block_range[:, None])
    ).astype(jnp.bfloat16)
    kv_sum = local_sum + jnp.einsum(
        "qf,fxsk->qxsk", onehot, returned, preferred_element_type=jnp.float32
    )
    kv_sum = kv_sum.at[nb - 1].add(from_after[0].astype(jnp.float32))
    kv_sum = kv_sum.at[0].add(from_before[0].astype(jnp.float32))
    global_pick = (
        (global_ids[:, None] // query_blocks == this_shard)
        & (global_ids[:, None] % query_blocks == block_range[None, :])
    ).astype(jnp.float32)
    kv_sum = kv_sum + jnp.einsum(
        "gq,gxsk->qxsk", global_pick, global_total, precision=lax.Precision.HIGHEST
    )
    kv_grad = jnp.concatenate(
        [
            kv_sum[:, 0].reshape(shard_tokens, kwidth).astype(jnp.bfloat16),
            kv_sum[:, 1].reshape(shard_tokens, kwidth).astype(jnp.bfloat16),
        ],
        axis=-1,
    )
    handed_kv = from_behind(kv_grad, "section", -1)
    return (
        handed_query[None],
        handed_kv[None, :, :kwidth],
        handed_kv[None, :, kwidth:],
    )


def solution(mesh):
    in_specs = (
        P("section", "seq", None),
        P("section", "seq", None),
        P("section", "seq", None),
        P("section", "seq", None),
        P("section", None, None),
        P("section", None),
        P("section", None),
    )
    out_specs = (P("section", "seq", None), P("section", "seq", None), P("section", "seq", None))
    return jax.shard_map(body, mesh=mesh, in_specs=in_specs, out_specs=out_specs, check_vma=False)
```

```python
import math

import jax
import jax.numpy as jnp
from jax import lax
from jax.experimental import pallas as pl
from jax.experimental.pallas import tpu as pltpu
from jax.sharding import PartitionSpec as P

HDIM = 128
BLK = 64
GLOB = 2
RAND = 3


def extended_2(array, sides, width):
    for axis, dim in sides:
        devices, length = (lax.axis_size(axis), array.shape[dim])
        up = [(i, (i + 1) % devices) for i in range(devices - 1)]
        down = [(j, i) for i, j in up]
        last = lax.slice_in_dim(array, length - width, length, axis=dim)
        leading = lax.slice_in_dim(array, 0, width, axis=dim)
        before = lax.ppermute(last, axis, up)
        after = lax.ppermute(leading, axis, down)
        array = jnp.concatenate([before, array, after], axis=dim)
    return array


def broadcast(array, axis, root):
    mine = lax.axis_index(axis) == root
    return lax.psum(jnp.where(mine, array, jnp.zeros_like(array)), axis)


def from_behind(block, axis, distance):
    devices = range(lax.axis_size(axis))
    route = [((i - distance) % len(devices), i) for i in devices]
    return lax.ppermute(block, axis, route)


def attention_kernel(ids_ref, q_ref, g_ref, *refs):
    del ids_ref
    ntiles = len(refs) - 6
    tile_refs = refs[:ntiles]
    live_ref = refs[ntiles]
    dq_ref, own_ref, edge_ref, glob_ref, rand_ref = refs[ntiles + 1 :]
    nblocks = own_ref.shape[0]
    block_len, width = q_ref.shape
    group = width // HDIM
    near = 3 + GLOB
    b = pl.program_id(1)
    score_scale = 1.0 / math.sqrt(HDIM)
    query = q_ref[...]
    grad = g_ref[...]
    query_rows = jnp.concatenate(
        [query[:, g * HDIM : (g + 1) * HDIM] for g in range(group)], axis=0
    )
    grad_rows = jnp.concatenate([grad[:, g * HDIM : (g + 1) * HDIM] for g in range(group)], axis=0)
    key_rows = jnp.concatenate([tile_refs[t][0] for t in range(ntiles)], axis=0)
    value_rows = jnp.concatenate([tile_refs[t][1] for t in range(ntiles)], axis=0)
    live = live_ref[...] > 0.5
    contract_last = (((1,), (1,)), ((), ()))
    contract_first = (((0,), (0,)), ((), ()))
    scores = (
        lax.dot_general(key_rows, query_rows, contract_last, preferred_element_type=jnp.float32)
        * score_scale
    )
    scores = jnp.where(live, scores, -1e30)
    row_max = jnp.max(scores, axis=0, keepdims=True)
    shifted = jnp.exp(scores - row_max)
    total = jnp.sum(shifted, axis=0, keepdims=True)
    probs = shifted * (1.0 / total)
    probs_low = probs.astype(jnp.bfloat16)
    output = lax.dot_general(
        value_rows, probs_low, contract_first, preferred_element_type=jnp.float32
    )
    grad_cols = grad_rows.astype(jnp.float32).T
    row_dot = jnp.sum(grad_cols * output, axis=0, keepdims=True)
    prob_grad = lax.dot_general(
        value_rows, grad_rows, contract_last, preferred_element_type=jnp.float32
    )
    score_grad = (probs * (prob_grad - row_dot)).astype(jnp.bfloat16)
    query_grad = (
        lax.dot_general(key_rows, score_grad, contract_first, preferred_element_type=jnp.float32)
        * score_scale
    ).T
    key_grad = jnp.dot(score_grad, query_rows, preferred_element_type=jnp.float32) * score_scale
    value_grad = jnp.dot(probs_low, grad_rows, preferred_element_type=jnp.float32)
    for g in range(group):
        dq_ref[:, g * HDIM : (g + 1) * HDIM] = query_grad[g * block_len : (g + 1) * block_len].astype(
            dq_ref.dtype
        )
    terms = jnp.stack(
        [key_grad.reshape(ntiles, block_len, HDIM), value_grad.reshape(ntiles, block_len, HDIM)],
        axis=1,
    )

    @pl.when(b == 0)
    def _():
        own_ref[...] = jnp.zeros_like(own_ref)
        glob_ref[...] = jnp.zeros_like(glob_ref)
        edge_ref[0] = terms[0]

    @pl.when(b > 0)
    def _():
        before = jnp.maximum(b - 1, 0)
        own_ref[before] = own_ref[before] + terms[0]

    own_ref[b] = own_ref[b] + terms[1]

    @pl.when(b < nblocks - 1)
    def _():
        after = jnp.minimum(b + 1, nblocks - 1)
        own_ref[after] = own_ref[after] + terms[2]

    @pl.when(b == nblocks - 1)
    def _():
        edge_ref[1] = terms[2]

    glob_ref[...] = glob_ref[...] + terms[3:near]
    rand_ref[...] = terms[near:].astype(rand_ref.dtype)


def block_backward(query_rows, grad_rows, all_blocks, tile_ids, key_live):
    shard_tokens, qwidth = query_rows.shape
    _, _, block_len, kwidth = all_blocks.shape
    nblocks, ntiles = tile_ids.shape
    heads_kv = kwidth // HDIM
    group_width = qwidth // heads_kv
    near = 3 + GLOB
    nrand = ntiles - near
    live = key_live.reshape(nblocks, ntiles * block_len, 1).astype(jnp.float32)
    row_spec = pl.BlockSpec((block_len, group_width), lambda h, b, ids: (b, h))
    tile_specs = [
        pl.BlockSpec(
            (None, 2, block_len, HDIM), lambda h, b, ids, t=t: (ids[b * ntiles + t], 0, 0, h)
        )
        for t in range(ntiles)
    ]
    live_spec = pl.BlockSpec((None, ntiles * block_len, 1), lambda h, b, ids: (b, 0, 0))
    own_spec = pl.BlockSpec((nblocks, 2, block_len, HDIM), lambda h, b, ids: (0, 0, 0, h))
    edge_spec = pl.BlockSpec((2, 2, block_len, HDIM), lambda h, b, ids: (0, 0, 0, h))
    glob_spec = pl.BlockSpec((GLOB, 2, block_len, HDIM), lambda h, b, ids: (0, 0, 0, h))
    rand_spec = pl.BlockSpec((None, nrand, 2, block_len, HDIM), lambda h, b, ids: (b, 0, 0, 0, h))
    flops = 12 * nblocks * heads_kv * (group_width // HDIM) * block_len * ntiles * block_len * HDIM
    grid_spec = pltpu.PrefetchScalarGridSpec(
        num_scalar_prefetch=1,
        grid=(heads_kv, nblocks),
        in_specs=[row_spec, row_spec, *tile_specs, live_spec],
        out_specs=[row_spec, own_spec, edge_spec, glob_spec, rand_spec],
    )
    outs = pl.pallas_call(
        attention_kernel,
        grid_spec=grid_spec,
        out_shape=[
            jax.ShapeDtypeStruct((shard_tokens, qwidth), jnp.bfloat16),
            jax.ShapeDtypeStruct((nblocks, 2, block_len, kwidth), jnp.float32),
            jax.ShapeDtypeStruct((2, 2, block_len, kwidth), jnp.float32),
            jax.ShapeDtypeStruct((GLOB, 2, block_len, kwidth), jnp.float32),
            jax.ShapeDtypeStruct((nblocks, nrand, 2, block_len, kwidth), jnp.bfloat16),
        ],
        compiler_params=pltpu.CompilerParams(
            dimension_semantics=("arbitrary", "arbitrary")
        ),
        cost_estimate=pl.CostEstimate(
            flops=flops,
            transcendentals=nblocks * qwidth // HDIM * block_len * ntiles * block_len,
            bytes_accessed=shard_tokens * qwidth * 6 + nblocks * ntiles * block_len * kwidth * 6,
        ),
    )(tile_ids.reshape(-1), query_rows, grad_rows, *([all_blocks] * ntiles), live)
    return outs


def request_plan(request_lists, this_shard, query_blocks):
    shards, count = request_lists.shape
    capacity = -(-count // shards)
    owner_ids = request_lists // query_blocks
    local_ids = request_lists % query_blocks
    order = jnp.arange(count, dtype=jnp.int32)
    earlier = order[None, :] < order[:, None]
    same_owner = owner_ids[:, :, None] == owner_ids[:, None, :]
    slot_rank = jnp.sum(same_owner & earlier[None], axis=2)
    slot_ids = jnp.arange(capacity, dtype=jnp.int32)
    chosen = (owner_ids[:, None, :] == this_shard) & (
        slot_rank[:, None, :] == slot_ids[None, :, None]
    )
    serve_block = jnp.sum(jnp.where(chosen, local_ids[:, None, :], 0), axis=2)
    slot_used = jnp.any(chosen, axis=2)
    owner_mine = lax.dynamic_index_in_dim(owner_ids, this_shard, 0, keepdims=False)
    rank_mine = lax.dynamic_index_in_dim(slot_rank, this_shard, 0, keepdims=False)
    return (serve_block, slot_used, owner_mine, rank_mine)


def serve_tiles(own_blocks, request_info):
    serve_block, slot_used = (request_info[0], request_info[1])
    shards, capacity = serve_block.shape
    gathered = jnp.take(own_blocks, serve_block.reshape(-1), axis=1)
    gathered = gathered.reshape(2, shards, capacity, own_blocks.shape[2], own_blocks.shape[3])
    return jnp.where(slot_used[None, :, :, None, None], gathered, jnp.zeros((), own_blocks.dtype))


def pick_tiles(received, request_info):
    return received[:, request_info[2], request_info[3]]


def place_terms(terms, request_info):
    serve_block = request_info[0]
    shards, capacity = serve_block.shape
    holder = jnp.zeros((2, shards, capacity, terms.shape[2], terms.shape[3]), terms.dtype)
    return holder.at[:, request_info[2], request_info[3]].set(terms)


def absorb_terms(received, request_info, query_blocks):
    serve_block, slot_used = (request_info[0], request_info[1])
    onehot = (
        slot_used[:, :, None]
        & (serve_block[:, :, None] == jnp.arange(query_blocks, dtype=jnp.int32)[None, None, :])
    ).astype(jnp.bfloat16)
    return jnp.einsum("ncq,xncsk->xqsk", onehot, received, preferred_element_type=jnp.float32)


def token_live(tile_ids, pad_sizes, query_blocks, shard_tokens, total_blocks):
    valid = (tile_ids >= 0) & (tile_ids < total_blocks)
    safe_ids = jnp.clip(tile_ids, 0, total_blocks - 1)
    owner_shard = safe_ids // query_blocks
    shards = pad_sizes.shape[0]
    pad_of = jnp.sum(
        jnp.where(owner_shard[..., None] == jnp.arange(shards, dtype=jnp.int32), pad_sizes, 0),
        axis=-1,
    )
    within = (safe_ids % query_blocks)[..., None] * BLK + jnp.arange(BLK, dtype=jnp.int32)
    return valid[..., None] & (within < (shard_tokens - pad_of)[..., None])


def body(queries, keys, values, out_grads, random_blocks, global_blocks, pad_lengths):
    query_rows = queries[0]
    key_rows = keys[0]
    value_rows = values[0]
    grad_rows = out_grads[0]
    random_table = random_blocks[0]
    global_ids = global_blocks[0]
    pad_sizes = pad_lengths[0]
    shards = lax.axis_size("seq")
    this_shard = lax.axis_index("seq")
    shard_tokens, qwidth = query_rows.shape
    kwidth = key_rows.shape[1]
    query_blocks = shard_tokens // BLK
    total_blocks = query_blocks * shards
    near = 3 + GLOB
    kvpair = jnp.stack(
        [key_rows.reshape(query_blocks, BLK, kwidth), value_rows.reshape(query_blocks, BLK, kwidth)],
        axis=1,
    )
    all_blocks = lax.all_gather(kvpair, "seq", axis=0, tiled=True)
    random_three = random_table.reshape(shards, query_blocks, RAND)
    base_ids = this_shard * query_blocks + jnp.arange(query_blocks, dtype=jnp.int32)
    window_ids = base_ids[:, None] + jnp.arange(-1, 2, dtype=jnp.int32)[None, :]
    my_random = lax.dynamic_index_in_dim(random_three, this_shard, 0, keepdims=False)
    tile_ids = jnp.concatenate(
        [window_ids, jnp.broadcast_to(global_ids[None, :], (query_blocks, GLOB)), my_random], axis=1
    )
    safe_ids = jnp.clip(tile_ids, 0, total_blocks - 1)
    key_live = token_live(tile_ids, pad_sizes, query_blocks, shard_tokens, total_blocks)
    query_grad, local_sum, edge_terms, global_part, random_part = block_backward(
        query_rows, grad_rows, all_blocks, safe_ids, key_live
    )
    handed_query = from_behind(query_grad, "section", -1)
    foreign = jnp.concatenate(
        [
            edge_terms.astype(jnp.bfloat16),
            global_part.astype(jnp.bfloat16),
            random_part.reshape(query_blocks * RAND, 2, BLK, kwidth),
        ],
        axis=0,
    )
    foreign_ids = jnp.concatenate(
        [
            safe_ids[0:1, 0],
            safe_ids[query_blocks - 1 : query_blocks, 2],
            global_ids,
            my_random.reshape(-1),
        ]
    )
    onehot = (
        foreign_ids[None, :] == jnp.arange(total_blocks, dtype=jnp.int32)[:, None]
    ).astype(jnp.bfloat16)
    partial = jnp.einsum(
        "nf,fxsk->nxsk", onehot, foreign, preferred_element_type=jnp.float32
    ).astype(jnp.bfloat16)
    returned = lax.psum_scatter(
        partial, "seq", scatter_dimension=0, tiled=True
    )
    kv_sum = local_sum + returned.astype(jnp.float32)
    kv_grad = jnp.concatenate(
        [
            kv_sum[:, 0].reshape(shard_tokens, kwidth).astype(jnp.bfloat16),
            kv_sum[:, 1].reshape(shard_tokens, kwidth).astype(jnp.bfloat16),
        ],
        axis=-1,
    )
    handed_kv = from_behind(kv_grad, "section", -1)
    return (
        handed_query[None],
        handed_kv[None, :, :kwidth],
        handed_kv[None, :, kwidth:],
    )


def solution(mesh):
    in_specs = (
        P("section", "seq", None),
        P("section", "seq", None),
        P("section", "seq", None),
        P("section", "seq", None),
        P("section", None, None),
        P("section", None),
        P("section", None),
    )
    out_specs = (P("section", "seq", None), P("section", "seq", None), P("section", "seq", None))
    return jax.shard_map(body, mesh=mesh, in_specs=in_specs, out_specs=out_specs, check_vma=False)
```

```python
import math

import jax
import jax.numpy as jnp
from jax import lax
from jax.experimental import pallas as pl
from jax.experimental.pallas import tpu as pltpu
from jax.sharding import PartitionSpec as P

HDIM = 128
BLK = 64
GLOB = 2
RAND = 3


def extended_2(array, sides, width):
    for axis, dim in sides:
        devices, length = (lax.axis_size(axis), array.shape[dim])
        up = [(i, (i + 1) % devices) for i in range(devices - 1)]
        down = [(j, i) for i, j in up]
        last = lax.slice_in_dim(array, length - width, length, axis=dim)
        leading = lax.slice_in_dim(array, 0, width, axis=dim)
        before = lax.ppermute(last, axis, up)
        after = lax.ppermute(leading, axis, down)
        array = jnp.concatenate([before, array, after], axis=dim)
    return array


def broadcast(array, axis, root):
    mine = lax.axis_index(axis) == root
    return lax.psum(jnp.where(mine, array, jnp.zeros_like(array)), axis)


def from_behind(block, axis, distance):
    devices = range(lax.axis_size(axis))
    route = [((i - distance) % len(devices), i) for i in devices]
    return lax.ppermute(block, axis, route)


def attention_kernel(ids_ref, q_ref, g_ref, *refs):
    del ids_ref
    ntiles = len(refs) - 6
    tile_refs = refs[:ntiles]
    live_ref = refs[ntiles]
    dq_ref, own_ref, edge_ref, glob_ref, rand_ref = refs[ntiles + 1 :]
    nblocks = own_ref.shape[0]
    block_len, width = q_ref.shape
    group = width // HDIM
    near = 3 + GLOB
    b = pl.program_id(1)
    score_scale = 1.0 / math.sqrt(HDIM)
    query = q_ref[...]
    grad = g_ref[...]
    query_rows = jnp.concatenate(
        [query[:, g * HDIM : (g + 1) * HDIM] for g in range(group)], axis=0
    )
    grad_rows = jnp.concatenate([grad[:, g * HDIM : (g + 1) * HDIM] for g in range(group)], axis=0)
    key_rows = jnp.concatenate([tile_refs[t][0] for t in range(ntiles)], axis=0)
    value_rows = jnp.concatenate([tile_refs[t][1] for t in range(ntiles)], axis=0)
    live = live_ref[...] > 0.5
    contract_last = (((1,), (1,)), ((), ()))
    contract_first = (((0,), (0,)), ((), ()))
    scores = (
        lax.dot_general(key_rows, query_rows, contract_last, preferred_element_type=jnp.float32)
        * score_scale
    )
    scores = jnp.where(live, scores, -1e30)
    row_max = jnp.max(scores, axis=0, keepdims=True)
    shifted = jnp.exp(scores - row_max)
    total = jnp.sum(shifted, axis=0, keepdims=True)
    probs = shifted * (1.0 / total)
    probs_low = probs.astype(jnp.bfloat16)
    output = lax.dot_general(
        value_rows, probs_low, contract_first, preferred_element_type=jnp.float32
    )
    grad_cols = grad_rows.astype(jnp.float32).T
    row_dot = jnp.sum(grad_cols * output, axis=0, keepdims=True)
    prob_grad = lax.dot_general(
        value_rows, grad_rows, contract_last, preferred_element_type=jnp.float32
    )
    score_grad = (probs * (prob_grad - row_dot)).astype(jnp.bfloat16)
    query_grad = (
        lax.dot_general(key_rows, score_grad, contract_first, preferred_element_type=jnp.float32)
        * score_scale
    ).T
    key_grad = jnp.dot(score_grad, query_rows, preferred_element_type=jnp.float32) * score_scale
    value_grad = jnp.dot(probs_low, grad_rows, preferred_element_type=jnp.float32)
    for g in range(group):
        dq_ref[:, g * HDIM : (g + 1) * HDIM] = query_grad[g * block_len : (g + 1) * block_len].astype(
            dq_ref.dtype
        )
    terms = jnp.stack(
        [key_grad.reshape(ntiles, block_len, HDIM), value_grad.reshape(ntiles, block_len, HDIM)],
        axis=1,
    )

    @pl.when(b == 0)
    def _():
        own_ref[...] = jnp.zeros_like(own_ref)
        glob_ref[...] = jnp.zeros_like(glob_ref)
        edge_ref[0] = terms[0]

    @pl.when(b > 0)
    def _():
        before = jnp.maximum(b - 1, 0)
        own_ref[before] = own_ref[before] + terms[0]

    own_ref[b] = own_ref[b] + terms[1]

    @pl.when(b < nblocks - 1)
    def _():
        after = jnp.minimum(b + 1, nblocks - 1)
        own_ref[after] = own_ref[after] + terms[2]

    @pl.when(b == nblocks - 1)
    def _():
        edge_ref[1] = terms[2]

    glob_ref[...] = glob_ref[...] + terms[3:near]
    rand_ref[...] = terms[near:].astype(rand_ref.dtype)


def block_backward(query_rows, grad_rows, all_blocks, tile_ids, key_live):
    shard_tokens, qwidth = query_rows.shape
    _, _, block_len, kwidth = all_blocks.shape
    nblocks, ntiles = tile_ids.shape
    heads_kv = kwidth // HDIM
    group_width = qwidth // heads_kv
    near = 3 + GLOB
    nrand = ntiles - near
    live = key_live.reshape(nblocks, ntiles * block_len, 1).astype(jnp.float32)
    row_spec = pl.BlockSpec((block_len, group_width), lambda h, b, ids: (b, h))
    tile_specs = [
        pl.BlockSpec(
            (None, 2, block_len, HDIM), lambda h, b, ids, t=t: (ids[b * ntiles + t], 0, 0, h)
        )
        for t in range(ntiles)
    ]
    live_spec = pl.BlockSpec((None, ntiles * block_len, 1), lambda h, b, ids: (b, 0, 0))
    own_spec = pl.BlockSpec((nblocks, 2, block_len, HDIM), lambda h, b, ids: (0, 0, 0, h))
    edge_spec = pl.BlockSpec((2, 2, block_len, HDIM), lambda h, b, ids: (0, 0, 0, h))
    glob_spec = pl.BlockSpec((GLOB, 2, block_len, HDIM), lambda h, b, ids: (0, 0, 0, h))
    rand_spec = pl.BlockSpec((None, nrand, 2, block_len, HDIM), lambda h, b, ids: (b, 0, 0, 0, h))
    flops = 12 * nblocks * heads_kv * (group_width // HDIM) * block_len * ntiles * block_len * HDIM
    grid_spec = pltpu.PrefetchScalarGridSpec(
        num_scalar_prefetch=1,
        grid=(heads_kv, nblocks),
        in_specs=[row_spec, row_spec, *tile_specs, live_spec],
        out_specs=[row_spec, own_spec, edge_spec, glob_spec, rand_spec],
    )
    outs = pl.pallas_call(
        attention_kernel,
        grid_spec=grid_spec,
        out_shape=[
            jax.ShapeDtypeStruct((shard_tokens, qwidth), jnp.bfloat16),
            jax.ShapeDtypeStruct((nblocks, 2, block_len, kwidth), jnp.float32),
            jax.ShapeDtypeStruct((2, 2, block_len, kwidth), jnp.float32),
            jax.ShapeDtypeStruct((GLOB, 2, block_len, kwidth), jnp.float32),
            jax.ShapeDtypeStruct((nblocks, nrand, 2, block_len, kwidth), jnp.bfloat16),
        ],
        compiler_params=pltpu.CompilerParams(
            dimension_semantics=("arbitrary", "arbitrary")
        ),
        cost_estimate=pl.CostEstimate(
            flops=flops,
            transcendentals=nblocks * qwidth // HDIM * block_len * ntiles * block_len,
            bytes_accessed=shard_tokens * qwidth * 6 + nblocks * ntiles * block_len * kwidth * 6,
        ),
    )(tile_ids.reshape(-1), query_rows, grad_rows, *([all_blocks] * ntiles), live)
    return outs


def request_plan(request_lists, this_shard, query_blocks):
    shards, count = request_lists.shape
    capacity = -(-count // shards)
    owner_ids = request_lists // query_blocks
    local_ids = request_lists % query_blocks
    order = jnp.arange(count, dtype=jnp.int32)
    earlier = order[None, :] < order[:, None]
    same_owner = owner_ids[:, :, None] == owner_ids[:, None, :]
    slot_rank = jnp.sum(same_owner & earlier[None], axis=2)
    slot_ids = jnp.arange(capacity, dtype=jnp.int32)
    chosen = (owner_ids[:, None, :] == this_shard) & (
        slot_rank[:, None, :] == slot_ids[None, :, None]
    )
    serve_block = jnp.sum(jnp.where(chosen, local_ids[:, None, :], 0), axis=2)
    slot_used = jnp.any(chosen, axis=2)
    owner_mine = lax.dynamic_index_in_dim(owner_ids, this_shard, 0, keepdims=False)
    rank_mine = lax.dynamic_index_in_dim(slot_rank, this_shard, 0, keepdims=False)
    return (serve_block, slot_used, owner_mine, rank_mine)


def token_live(tile_ids, pad_sizes, query_blocks, shard_tokens, total_blocks):
    valid = (tile_ids >= 0) & (tile_ids < total_blocks)
    safe_ids = jnp.clip(tile_ids, 0, total_blocks - 1)
    owner_shard = safe_ids // query_blocks
    shards = pad_sizes.shape[0]
    pad_of = jnp.sum(
        jnp.where(owner_shard[..., None] == jnp.arange(shards, dtype=jnp.int32), pad_sizes, 0),
        axis=-1,
    )
    within = (safe_ids % query_blocks)[..., None] * BLK + jnp.arange(BLK, dtype=jnp.int32)
    return valid[..., None] & (within < (shard_tokens - pad_of)[..., None])


def body(queries, keys, values, out_grads, random_blocks, global_blocks, pad_lengths):
    query_rows = queries[0]
    key_rows = keys[0]
    value_rows = values[0]
    grad_rows = out_grads[0]
    random_table = random_blocks[0]
    global_ids = global_blocks[0]
    pad_sizes = pad_lengths[0]
    shards = lax.axis_size("seq")
    this_shard = lax.axis_index("seq")
    shard_tokens, qwidth = query_rows.shape
    kwidth = key_rows.shape[1]
    query_blocks = shard_tokens // BLK
    total_blocks = query_blocks * shards
    own_blocks = jnp.stack(
        [key_rows.reshape(query_blocks, BLK, kwidth), value_rows.reshape(query_blocks, BLK, kwidth)],
        axis=1,
    )
    up = [(i, (i + 1) % shards) for i in range(shards - 1)]
    down = [(j, i) for i, j in up]
    edge_before = lax.ppermute(own_blocks[query_blocks - 1 :], "seq", up)
    edge_after = lax.ppermute(own_blocks[:1], "seq", down)
    global_mine = [
        jnp.where(
            global_ids[g] // query_blocks == this_shard,
            lax.dynamic_index_in_dim(own_blocks, global_ids[g] % query_blocks, 0, keepdims=True),
            jnp.zeros((), own_blocks.dtype),
        )
        for g in range(GLOB)
    ]
    requests = random_table.reshape(shards, query_blocks * RAND)
    plan = request_plan(requests, this_shard, query_blocks)
    serve_block, slot_used, owner_mine, rank_mine = plan
    capacity = serve_block.shape[1]
    block_rows = 2 * BLK
    served = jnp.take(own_blocks, serve_block.reshape(-1), axis=0).reshape(
        shards, capacity * block_rows, kwidth
    )
    global_chunks = jnp.concatenate(global_mine, axis=0).reshape(shards, -1, kwidth)
    received = lax.all_to_all(
        jnp.concatenate([served, global_chunks], axis=1), "seq", 0, 0, tiled=True
    )
    random_tiles = received[:, : capacity * block_rows].reshape(shards * capacity, 2, BLK, kwidth)
    global_piece = jnp.sum(received[:, capacity * block_rows :], axis=0, dtype=own_blocks.dtype)
    global_tiles = lax.all_to_all(
        jnp.broadcast_to(global_piece[None], (shards,) + global_piece.shape), "seq", 0, 0, tiled=True
    ).reshape(GLOB, 2, BLK, kwidth)
    received = random_tiles
    sources = jnp.concatenate([own_blocks, edge_before, edge_after, global_tiles, received], axis=0)
    nb = query_blocks
    block_range = jnp.arange(nb, dtype=jnp.int32)
    source_ids = jnp.concatenate(
        [
            jnp.where(block_range == 0, nb, block_range - 1)[:, None],
            block_range[:, None],
            jnp.where(block_range == nb - 1, nb + 1, block_range + 1)[:, None],
            jnp.broadcast_to(nb + 2 + jnp.arange(GLOB, dtype=jnp.int32)[None, :], (nb, GLOB)),
            (nb + 2 + GLOB + owner_mine * capacity + rank_mine).reshape(nb, RAND),
        ],
        axis=1,
    )
    source_ids = jnp.clip(source_ids, 0, sources.shape[0] - 1)
    random_three = random_table.reshape(shards, query_blocks, RAND)
    base_ids = this_shard * query_blocks + block_range
    window_ids = base_ids[:, None] + jnp.arange(-1, 2, dtype=jnp.int32)[None, :]
    my_random = lax.dynamic_index_in_dim(random_three, this_shard, 0, keepdims=False)
    tile_ids = jnp.concatenate(
        [window_ids, jnp.broadcast_to(global_ids[None, :], (query_blocks, GLOB)), my_random], axis=1
    )
    key_live = token_live(tile_ids, pad_sizes, query_blocks, shard_tokens, total_blocks)
    query_grad, local_sum, edge_terms, global_part, random_part = block_backward(
        query_rows, grad_rows, sources, source_ids, key_live
    )
    handed_query = from_behind(query_grad, "section", -1)
    edge_low = edge_terms.astype(jnp.bfloat16)
    from_after = lax.ppermute(edge_low[:1], "seq", down)
    from_before = lax.ppermute(edge_low[1:], "seq", up)
    holder = jnp.zeros((shards, capacity, 2, BLK, kwidth), random_part.dtype)
    holder = holder.at[owner_mine, rank_mine].set(
        random_part.reshape(query_blocks * RAND, 2, BLK, kwidth)
    )
    global_low = global_part.astype(jnp.bfloat16).reshape(shards, -1, kwidth)
    returned = lax.all_to_all(
        jnp.concatenate([holder.reshape(shards, capacity * block_rows, kwidth), global_low], axis=1),
        "seq",
        0,
        0,
        tiled=True,
    )
    random_back = returned[:, : capacity * block_rows].reshape(shards * capacity, 2, BLK, kwidth)
    global_sum = jnp.sum(returned[:, capacity * block_rows :].astype(jnp.float32), axis=0)
    global_total = lax.all_to_all(
        jnp.broadcast_to(global_sum[None], (shards,) + global_sum.shape), "seq", 0, 0, tiled=True
    ).reshape(GLOB, 2, BLK, kwidth)
    onehot = (
        slot_used.reshape(-1)[None, :]
        & (serve_block.reshape(-1)[None, :] == block_range[:, None])
    ).astype(jnp.bfloat16)
    kv_sum = local_sum + jnp.einsum(
        "qf,fxsk->qxsk", onehot, random_back, preferred_element_type=jnp.float32
    )
    kv_sum = kv_sum.at[nb - 1].add(from_after[0].astype(jnp.float32))
    kv_sum = kv_sum.at[0].add(from_before[0].astype(jnp.float32))
    global_pick = (
        (global_ids[:, None] // query_blocks == this_shard)
        & (global_ids[:, None] % query_blocks == block_range[None, :])
    ).astype(jnp.float32)
    kv_sum = kv_sum + jnp.einsum(
        "gq,gxsk->qxsk", global_pick, global_total, precision=lax.Precision.HIGHEST
    )
    kv_grad = jnp.concatenate(
        [
            kv_sum[:, 0].reshape(shard_tokens, kwidth).astype(jnp.bfloat16),
            kv_sum[:, 1].reshape(shard_tokens, kwidth).astype(jnp.bfloat16),
        ],
        axis=-1,
    )
    handed_kv = from_behind(kv_grad, "section", -1)
    return (
        handed_query[None],
        handed_kv[None, :, :kwidth],
        handed_kv[None, :, kwidth:],
    )


def solution(mesh):
    in_specs = (
        P("section", "seq", None),
        P("section", "seq", None),
        P("section", "seq", None),
        P("section", "seq", None),
        P("section", None, None),
        P("section", None),
        P("section", None),
    )
    out_specs = (P("section", "seq", None), P("section", "seq", None), P("section", "seq", None))
    return jax.shard_map(body, mesh=mesh, in_specs=in_specs, out_specs=out_specs, check_vma=False)
```

```python
import math

import jax
import jax.numpy as jnp
from jax import lax
from jax.experimental import pallas as pl
from jax.experimental.pallas import tpu as pltpu
from jax.sharding import PartitionSpec as P

HDIM = 128
BLK = 64
GLOB = 2
RAND = 3


def extended_2(array, sides, width):
    for axis, dim in sides:
        devices, length = (lax.axis_size(axis), array.shape[dim])
        up = [(i, (i + 1) % devices) for i in range(devices - 1)]
        down = [(j, i) for i, j in up]
        last = lax.slice_in_dim(array, length - width, length, axis=dim)
        leading = lax.slice_in_dim(array, 0, width, axis=dim)
        before = lax.ppermute(last, axis, up)
        after = lax.ppermute(leading, axis, down)
        array = jnp.concatenate([before, array, after], axis=dim)
    return array


def broadcast(array, axis, root):
    mine = lax.axis_index(axis) == root
    return lax.psum(jnp.where(mine, array, jnp.zeros_like(array)), axis)


def from_behind(block, axis, distance):
    devices = range(lax.axis_size(axis))
    route = [((i - distance) % len(devices), i) for i in devices]
    return lax.ppermute(block, axis, route)


def attention_kernel(ids_ref, q_ref, g_ref, *refs):
    del ids_ref
    ntiles = len(refs) - 6
    tile_refs = refs[:ntiles]
    live_ref = refs[ntiles]
    dq_ref, own_ref, edge_ref, glob_ref, rand_ref = refs[ntiles + 1 :]
    nblocks = own_ref.shape[0]
    block_len, width = q_ref.shape
    group = width // HDIM
    near = 3 + GLOB
    b = pl.program_id(1)
    score_scale = 1.0 / math.sqrt(HDIM)
    query = q_ref[...]
    grad = g_ref[...]
    query_rows = jnp.concatenate(
        [query[:, g * HDIM : (g + 1) * HDIM] for g in range(group)], axis=0
    )
    grad_rows = jnp.concatenate([grad[:, g * HDIM : (g + 1) * HDIM] for g in range(group)], axis=0)
    key_rows = jnp.concatenate([tile_refs[t][:block_len] for t in range(ntiles)], axis=0)
    value_rows = jnp.concatenate([tile_refs[t][block_len:] for t in range(ntiles)], axis=0)
    live = live_ref[...] > 0.5
    contract_last = (((1,), (1,)), ((), ()))
    contract_first = (((0,), (0,)), ((), ()))
    scores = (
        lax.dot_general(key_rows, query_rows, contract_last, preferred_element_type=jnp.float32)
        * score_scale
    )
    scores = jnp.where(live, scores, -1e30)
    row_max = jnp.max(scores, axis=0, keepdims=True)
    shifted = jnp.exp(scores - row_max)
    total = jnp.sum(shifted, axis=0, keepdims=True)
    probs = shifted * (1.0 / total)
    probs_low = probs.astype(jnp.bfloat16)
    output = lax.dot_general(
        value_rows, probs_low, contract_first, preferred_element_type=jnp.float32
    )
    grad_cols = grad_rows.astype(jnp.float32).T
    row_dot = jnp.sum(grad_cols * output, axis=0, keepdims=True)
    prob_grad = lax.dot_general(
        value_rows, grad_rows, contract_last, preferred_element_type=jnp.float32
    )
    score_grad = (probs * (prob_grad - row_dot)).astype(jnp.bfloat16)
    query_grad = (
        lax.dot_general(key_rows, score_grad, contract_first, preferred_element_type=jnp.float32)
        * score_scale
    ).T
    key_grad = jnp.dot(score_grad, query_rows, preferred_element_type=jnp.float32) * score_scale
    value_grad = jnp.dot(probs_low, grad_rows, preferred_element_type=jnp.float32)
    for g in range(group):
        dq_ref[:, g * HDIM : (g + 1) * HDIM] = query_grad[g * block_len : (g + 1) * block_len].astype(
            dq_ref.dtype
        )
    terms = jnp.stack(
        [key_grad.reshape(ntiles, block_len, HDIM), value_grad.reshape(ntiles, block_len, HDIM)],
        axis=1,
    )

    @pl.when(b == 0)
    def _():
        own_ref[...] = jnp.zeros_like(own_ref)
        glob_ref[...] = jnp.zeros_like(glob_ref)
        edge_ref[0] = terms[0]

    @pl.when(b > 0)
    def _():
        before = jnp.maximum(b - 1, 0)
        own_ref[before] = own_ref[before] + terms[0]

    own_ref[b] = own_ref[b] + terms[1]

    @pl.when(b < nblocks - 1)
    def _():
        after = jnp.minimum(b + 1, nblocks - 1)
        own_ref[after] = own_ref[after] + terms[2]

    @pl.when(b == nblocks - 1)
    def _():
        edge_ref[1] = terms[2]

    glob_ref[...] = glob_ref[...] + terms[3:near]
    rand_ref[...] = terms[near:].astype(rand_ref.dtype)


def block_backward(query_rows, grad_rows, window, global_tiles, received, random_ids, key_live):
    shard_tokens, qwidth = query_rows.shape
    kwidth = window.shape[-1]
    nblocks = window.shape[0] - 2
    block_len = window.shape[1] // 2
    near = 3 + GLOB
    nrand = random_ids.shape[0] // (2 * nblocks)
    ntiles = near + nrand
    heads_kv = kwidth // HDIM
    group_width = qwidth // heads_kv
    pair_rows = 2 * block_len
    live = key_live.reshape(nblocks, ntiles * block_len, 1).astype(jnp.float32)
    row_spec = pl.BlockSpec((block_len, group_width), lambda h, b, ids: (b, h))
    tile_specs = [
        pl.BlockSpec((None, pair_rows, HDIM), lambda h, b, ids, t=t: (b + t, 0, h)) for t in range(3)
    ]
    tile_specs += [
        pl.BlockSpec((None, pair_rows, HDIM), lambda h, b, ids, g=g: (g, 0, h)) for g in range(GLOB)
    ]
    tile_specs += [
        pl.BlockSpec(
            (None, pair_rows, HDIM),
            lambda h, b, ids, r=r: (ids[(b * nrand + r) * 2], ids[(b * nrand + r) * 2 + 1], h),
        )
        for r in range(nrand)
    ]
    live_spec = pl.BlockSpec((None, ntiles * block_len, 1), lambda h, b, ids: (b, 0, 0))
    own_spec = pl.BlockSpec((nblocks, 2, block_len, HDIM), lambda h, b, ids: (0, 0, 0, h))
    edge_spec = pl.BlockSpec((2, 2, block_len, HDIM), lambda h, b, ids: (0, 0, 0, h))
    glob_spec = pl.BlockSpec((GLOB, 2, block_len, HDIM), lambda h, b, ids: (0, 0, 0, h))
    rand_spec = pl.BlockSpec((None, nrand, 2, block_len, HDIM), lambda h, b, ids: (b, 0, 0, 0, h))
    flops = 12 * nblocks * heads_kv * (group_width // HDIM) * block_len * ntiles * block_len * HDIM
    grid_spec = pltpu.PrefetchScalarGridSpec(
        num_scalar_prefetch=1,
        grid=(heads_kv, nblocks),
        in_specs=[row_spec, row_spec, *tile_specs, live_spec],
        out_specs=[row_spec, own_spec, edge_spec, glob_spec, rand_spec],
    )
    outs = pl.pallas_call(
        attention_kernel,
        grid_spec=grid_spec,
        out_shape=[
            jax.ShapeDtypeStruct((shard_tokens, qwidth), jnp.bfloat16),
            jax.ShapeDtypeStruct((nblocks, 2, block_len, kwidth), jnp.float32),
            jax.ShapeDtypeStruct((2, 2, block_len, kwidth), jnp.float32),
            jax.ShapeDtypeStruct((GLOB, 2, block_len, kwidth), jnp.float32),
            jax.ShapeDtypeStruct((nblocks, nrand, 2, block_len, kwidth), jnp.bfloat16),
        ],
        compiler_params=pltpu.CompilerParams(
            dimension_semantics=("arbitrary", "arbitrary")
        ),
        cost_estimate=pl.CostEstimate(
            flops=flops,
            transcendentals=nblocks * qwidth // HDIM * block_len * ntiles * block_len,
            bytes_accessed=shard_tokens * qwidth * 6 + nblocks * ntiles * block_len * kwidth * 6,
        ),
    )(
        random_ids,
        query_rows,
        grad_rows,
        *([window] * 3),
        *([global_tiles] * GLOB),
        *([received] * nrand),
        live,
    )
    return outs


def request_plan(request_lists, this_shard, query_blocks):
    shards, count = request_lists.shape
    capacity = -(-count // shards)
    owner_ids = request_lists // query_blocks
    local_ids = request_lists % query_blocks
    order = jnp.arange(count, dtype=jnp.int32)
    earlier = order[None, :] < order[:, None]
    same_owner = owner_ids[:, :, None] == owner_ids[:, None, :]
    slot_rank = jnp.sum(same_owner & earlier[None], axis=2)
    slot_ids = jnp.arange(capacity, dtype=jnp.int32)
    chosen = (owner_ids[:, None, :] == this_shard) & (
        slot_rank[:, None, :] == slot_ids[None, :, None]
    )
    serve_block = jnp.sum(jnp.where(chosen, local_ids[:, None, :], 0), axis=2)
    slot_used = jnp.any(chosen, axis=2)
    owner_mine = lax.dynamic_index_in_dim(owner_ids, this_shard, 0, keepdims=False)
    rank_mine = lax.dynamic_index_in_dim(slot_rank, this_shard, 0, keepdims=False)
    return (serve_block, slot_used, owner_mine, rank_mine)


def token_live(tile_ids, pad_sizes, query_blocks, shard_tokens, total_blocks):
    valid = (tile_ids >= 0) & (tile_ids < total_blocks)
    safe_ids = jnp.clip(tile_ids, 0, total_blocks - 1)
    owner_shard = safe_ids // query_blocks
    shards = pad_sizes.shape[0]
    pad_of = jnp.sum(
        jnp.where(owner_shard[..., None] == jnp.arange(shards, dtype=jnp.int32), pad_sizes, 0),
        axis=-1,
    )
    within = (safe_ids % query_blocks)[..., None] * BLK + jnp.arange(BLK, dtype=jnp.int32)
    return valid[..., None] & (within < (shard_tokens - pad_of)[..., None])


def body(queries, keys, values, out_grads, random_blocks, global_blocks, pad_lengths):
    query_rows = queries[0]
    key_rows = keys[0]
    value_rows = values[0]
    grad_rows = out_grads[0]
    random_table = random_blocks[0]
    global_ids = global_blocks[0]
    pad_sizes = pad_lengths[0]
    shards = lax.axis_size("seq")
    this_shard = lax.axis_index("seq")
    shard_tokens, qwidth = query_rows.shape
    kwidth = key_rows.shape[1]
    query_blocks = shard_tokens // BLK
    total_blocks = query_blocks * shards
    own_blocks = jnp.stack(
        [key_rows.reshape(query_blocks, BLK, kwidth), value_rows.reshape(query_blocks, BLK, kwidth)],
        axis=1,
    )
    up = [(i, (i + 1) % shards) for i in range(shards - 1)]
    down = [(j, i) for i, j in up]
    edge_before = lax.ppermute(own_blocks[query_blocks - 1 :], "seq", up)
    edge_after = lax.ppermute(own_blocks[:1], "seq", down)
    requests = random_table.reshape(shards, query_blocks * RAND)
    plan = request_plan(requests, this_shard, query_blocks)
    serve_block, slot_used, owner_mine, rank_mine = plan
    capacity = serve_block.shape[1]
    block_rows = 2 * BLK
    nb = query_blocks
    own_rows = jnp.concatenate(
        [own_blocks.reshape(nb * block_rows, kwidth), jnp.zeros((1, kwidth), own_blocks.dtype)]
    )
    row_range = jnp.arange(block_rows, dtype=jnp.int32)
    served_idx = (serve_block[:, :, None] * block_rows + row_range).reshape(shards, -1)
    global_owned = global_ids // query_blocks == this_shard
    global_idx = jnp.where(
        global_owned[:, None], (global_ids % query_blocks)[:, None] * block_rows + row_range, nb * block_rows
    ).reshape(shards, -1)
    payload_idx = jnp.concatenate([served_idx, global_idx], axis=1)
    payload = jnp.take(own_rows, payload_idx.reshape(-1), axis=0, mode="clip").reshape(
        shards, -1, kwidth
    )
    received = lax.all_to_all(payload, "seq", 0, 0, tiled=True)
    global_piece = jnp.sum(received[:, capacity * block_rows :], axis=0, dtype=own_blocks.dtype)
    global_tiles = lax.all_to_all(
        jnp.broadcast_to(global_piece[None], (shards,) + global_piece.shape), "seq", 0, 0, tiled=True
    ).reshape(GLOB, block_rows, kwidth)
    window = jnp.concatenate([edge_before, own_blocks, edge_after], axis=0).reshape(
        nb + 2, block_rows, kwidth
    )
    block_range = jnp.arange(nb, dtype=jnp.int32)
    random_ids = jnp.stack(
        [owner_mine, jnp.clip(rank_mine, 0, capacity - 1)], axis=1
    ).reshape(-1)
    random_three = random_table.reshape(shards, query_blocks, RAND)
    base_ids = this_shard * query_blocks + block_range
    window_ids = base_ids[:, None] + jnp.arange(-1, 2, dtype=jnp.int32)[None, :]
    my_random = lax.dynamic_index_in_dim(random_three, this_shard, 0, keepdims=False)
    tile_ids = jnp.concatenate(
        [window_ids, jnp.broadcast_to(global_ids[None, :], (query_blocks, GLOB)), my_random], axis=1
    )
    key_live = token_live(tile_ids, pad_sizes, query_blocks, shard_tokens, total_blocks)
    query_grad, local_sum, edge_terms, global_part, random_part = block_backward(
        query_rows, grad_rows, window, global_tiles, received, random_ids, key_live
    )
    handed_query = from_behind(query_grad, "section", -1)
    edge_low = edge_terms.astype(jnp.bfloat16)
    from_after = lax.ppermute(edge_low[:1], "seq", down)
    from_before = lax.ppermute(edge_low[1:], "seq", up)
    holder = jnp.zeros((shards, capacity, 2, BLK, kwidth), random_part.dtype)
    holder = holder.at[owner_mine, rank_mine].set(
        random_part.reshape(query_blocks * RAND, 2, BLK, kwidth)
    )
    global_low = global_part.astype(jnp.bfloat16).reshape(shards, -1, kwidth)
    returned = lax.all_to_all(
        jnp.concatenate([holder.reshape(shards, capacity * block_rows, kwidth), global_low], axis=1),
        "seq",
        0,
        0,
        tiled=True,
    )
    random_back = returned[:, : capacity * block_rows].reshape(shards * capacity, 2, BLK, kwidth)
    global_sum = jnp.sum(returned[:, capacity * block_rows :].astype(jnp.float32), axis=0)
    global_sum = global_sum.astype(jnp.bfloat16)
    global_total = lax.all_to_all(
        jnp.broadcast_to(global_sum[None], (shards,) + global_sum.shape), "seq", 0, 0, tiled=True
    ).reshape(GLOB, 2, BLK, kwidth).astype(jnp.float32)
    onehot = (
        slot_used.reshape(-1)[None, :]
        & (serve_block.reshape(-1)[None, :] == block_range[:, None])
    ).astype(jnp.bfloat16)
    kv_sum = local_sum + jnp.einsum(
        "qf,fxsk->qxsk", onehot, random_back, preferred_element_type=jnp.float32
    )
    kv_sum = kv_sum.at[nb - 1].add(from_after[0].astype(jnp.float32))
    kv_sum = kv_sum.at[0].add(from_before[0].astype(jnp.float32))
    global_pick = (
        (global_ids[:, None] // query_blocks == this_shard)
        & (global_ids[:, None] % query_blocks == block_range[None, :])
    ).astype(jnp.float32)
    kv_sum = kv_sum + jnp.einsum(
        "gq,gxsk->qxsk", global_pick, global_total, precision=lax.Precision.HIGHEST
    )
    kv_grad = jnp.concatenate(
        [
            kv_sum[:, 0].reshape(shard_tokens, kwidth).astype(jnp.bfloat16),
            kv_sum[:, 1].reshape(shard_tokens, kwidth).astype(jnp.bfloat16),
        ],
        axis=-1,
    )
    handed_kv = from_behind(kv_grad, "section", -1)
    return (
        handed_query[None],
        handed_kv[None, :, :kwidth],
        handed_kv[None, :, kwidth:],
    )


def solution(mesh):
    in_specs = (
        P("section", "seq", None),
        P("section", "seq", None),
        P("section", "seq", None),
        P("section", "seq", None),
        P("section", None, None),
        P("section", None),
        P("section", None),
    )
    out_specs = (P("section", "seq", None), P("section", "seq", None), P("section", "seq", None))
    return jax.shard_map(body, mesh=mesh, in_specs=in_specs, out_specs=out_specs, check_vma=False)
```

```python
import math

import jax
import jax.numpy as jnp
from jax import lax
from jax.experimental import pallas as pl
from jax.experimental.pallas import tpu as pltpu
from jax.sharding import PartitionSpec as P

HDIM = 128
BLK = 64
GLOB = 2
RAND = 3


def extended_2(array, sides, width):
    for axis, dim in sides:
        devices, length = (lax.axis_size(axis), array.shape[dim])
        up = [(i, (i + 1) % devices) for i in range(devices - 1)]
        down = [(j, i) for i, j in up]
        last = lax.slice_in_dim(array, length - width, length, axis=dim)
        leading = lax.slice_in_dim(array, 0, width, axis=dim)
        before = lax.ppermute(last, axis, up)
        after = lax.ppermute(leading, axis, down)
        array = jnp.concatenate([before, array, after], axis=dim)
    return array


def broadcast(array, axis, root):
    mine = lax.axis_index(axis) == root
    return lax.psum(jnp.where(mine, array, jnp.zeros_like(array)), axis)


def from_behind(block, axis, distance):
    devices = range(lax.axis_size(axis))
    route = [((i - distance) % len(devices), i) for i in devices]
    return lax.ppermute(block, axis, route)


def attention_kernel(ids_ref, q_ref, g_ref, *refs):
    del ids_ref
    ntiles = len(refs) - 6
    tile_refs = refs[:ntiles]
    live_ref = refs[ntiles]
    dq_ref, own_ref, edge_ref, glob_ref, rand_ref = refs[ntiles + 1 :]
    nblocks = own_ref.shape[0]
    block_len, width = q_ref.shape
    group = width // HDIM
    near = 3 + GLOB
    b = pl.program_id(1)
    score_scale = 1.0 / math.sqrt(HDIM)
    query = q_ref[...]
    grad = g_ref[...]
    query_rows = jnp.concatenate(
        [query[:, g * HDIM : (g + 1) * HDIM] for g in range(group)], axis=0
    )
    grad_rows = jnp.concatenate([grad[:, g * HDIM : (g + 1) * HDIM] for g in range(group)], axis=0)
    key_rows = jnp.concatenate([tile_refs[t][:block_len] for t in range(ntiles)], axis=0)
    value_rows = jnp.concatenate([tile_refs[t][block_len:] for t in range(ntiles)], axis=0)
    live = live_ref[...] > 0.5
    contract_last = (((1,), (1,)), ((), ()))
    contract_first = (((0,), (0,)), ((), ()))
    scores = (
        lax.dot_general(key_rows, query_rows, contract_last, preferred_element_type=jnp.float32)
        * score_scale
    )
    scores = jnp.where(live, scores, -1e30)
    row_max = jnp.max(scores, axis=0, keepdims=True)
    shifted = jnp.exp(scores - row_max)
    total = jnp.sum(shifted, axis=0, keepdims=True)
    probs = shifted * (1.0 / total)
    probs_low = probs.astype(jnp.bfloat16)
    output = lax.dot_general(
        value_rows, probs_low, contract_first, preferred_element_type=jnp.float32
    )
    grad_cols = grad_rows.astype(jnp.float32).T
    row_dot = jnp.sum(grad_cols * output, axis=0, keepdims=True)
    prob_grad = lax.dot_general(
        value_rows, grad_rows, contract_last, preferred_element_type=jnp.float32
    )
    score_grad = (probs * (prob_grad - row_dot)).astype(jnp.bfloat16)
    query_grad = (
        lax.dot_general(key_rows, score_grad, contract_first, preferred_element_type=jnp.float32)
        * score_scale
    ).T
    key_grad = jnp.dot(score_grad, query_rows, preferred_element_type=jnp.float32) * score_scale
    value_grad = jnp.dot(probs_low, grad_rows, preferred_element_type=jnp.float32)
    for g in range(group):
        dq_ref[:, g * HDIM : (g + 1) * HDIM] = query_grad[g * block_len : (g + 1) * block_len].astype(
            dq_ref.dtype
        )
    terms = jnp.stack(
        [key_grad.reshape(ntiles, block_len, HDIM), value_grad.reshape(ntiles, block_len, HDIM)],
        axis=1,
    )

    @pl.when(b == 0)
    def _():
        own_ref[...] = jnp.zeros_like(own_ref)
        glob_ref[...] = jnp.zeros_like(glob_ref)
        edge_ref[0] = terms[0]

    @pl.when(b > 0)
    def _():
        before = jnp.maximum(b - 1, 0)
        own_ref[before] = own_ref[before] + terms[0]

    own_ref[b] = own_ref[b] + terms[1]

    @pl.when(b < nblocks - 1)
    def _():
        after = jnp.minimum(b + 1, nblocks - 1)
        own_ref[after] = own_ref[after] + terms[2]

    @pl.when(b == nblocks - 1)
    def _():
        edge_ref[1] = terms[2]

    glob_ref[...] = glob_ref[...] + terms[3:near]
    rand_ref[...] = terms[near:].astype(rand_ref.dtype)


def block_backward(query_rows, grad_rows, window, global_tiles, received, random_ids, key_live):
    shard_tokens, qwidth = query_rows.shape
    kwidth = window.shape[-1]
    nblocks = window.shape[0] - 2
    block_len = window.shape[1] // 2
    near = 3 + GLOB
    nrand = random_ids.shape[0] // (2 * nblocks)
    ntiles = near + nrand
    heads_kv = kwidth // HDIM
    group_width = qwidth // heads_kv
    pair_rows = 2 * block_len
    live = key_live.reshape(nblocks, ntiles * block_len, 1).astype(jnp.float32)
    row_spec = pl.BlockSpec((block_len, group_width), lambda h, b, ids: (b, h))
    tile_specs = [
        pl.BlockSpec((None, pair_rows, HDIM), lambda h, b, ids, t=t: (b + t, 0, h)) for t in range(3)
    ]
    tile_specs += [
        pl.BlockSpec((None, pair_rows, HDIM), lambda h, b, ids, g=g: (g, 0, h)) for g in range(GLOB)
    ]
    tile_specs += [
        pl.BlockSpec(
            (None, pair_rows, HDIM),
            lambda h, b, ids, r=r: (ids[(b * nrand + r) * 2], ids[(b * nrand + r) * 2 + 1], h),
        )
        for r in range(nrand)
    ]
    live_spec = pl.BlockSpec((None, ntiles * block_len, 1), lambda h, b, ids: (b, 0, 0))
    own_spec = pl.BlockSpec((nblocks, 2, block_len, HDIM), lambda h, b, ids: (0, 0, 0, h))
    edge_spec = pl.BlockSpec((2, 2, block_len, HDIM), lambda h, b, ids: (0, 0, 0, h))
    glob_spec = pl.BlockSpec((GLOB, 2, block_len, HDIM), lambda h, b, ids: (0, 0, 0, h))
    rand_spec = pl.BlockSpec((None, nrand, 2, block_len, HDIM), lambda h, b, ids: (b, 0, 0, 0, h))
    flops = 12 * nblocks * heads_kv * (group_width // HDIM) * block_len * ntiles * block_len * HDIM
    grid_spec = pltpu.PrefetchScalarGridSpec(
        num_scalar_prefetch=1,
        grid=(heads_kv, nblocks),
        in_specs=[row_spec, row_spec, *tile_specs, live_spec],
        out_specs=[row_spec, own_spec, edge_spec, glob_spec, rand_spec],
    )
    outs = pl.pallas_call(
        attention_kernel,
        grid_spec=grid_spec,
        out_shape=[
            jax.ShapeDtypeStruct((shard_tokens, qwidth), jnp.bfloat16),
            jax.ShapeDtypeStruct((nblocks, 2, block_len, kwidth), jnp.float32),
            jax.ShapeDtypeStruct((2, 2, block_len, kwidth), jnp.float32),
            jax.ShapeDtypeStruct((GLOB, 2, block_len, kwidth), jnp.float32),
            jax.ShapeDtypeStruct((nblocks, nrand, 2, block_len, kwidth), jnp.bfloat16),
        ],
        compiler_params=pltpu.CompilerParams(
            dimension_semantics=("arbitrary", "arbitrary")
        ),
        cost_estimate=pl.CostEstimate(
            flops=flops,
            transcendentals=nblocks * qwidth // HDIM * block_len * ntiles * block_len,
            bytes_accessed=shard_tokens * qwidth * 6 + nblocks * ntiles * block_len * kwidth * 6,
        ),
    )(
        random_ids,
        query_rows,
        grad_rows,
        *([window] * 3),
        *([global_tiles] * GLOB),
        *([received] * nrand),
        live,
    )
    return outs


def request_plan(request_lists, this_shard, query_blocks):
    shards, count = request_lists.shape
    capacity = -(-count // shards)
    owner_ids = request_lists // query_blocks
    local_ids = request_lists % query_blocks
    order = jnp.arange(count, dtype=jnp.int32)
    earlier = order[None, :] < order[:, None]
    same_owner = owner_ids[:, :, None] == owner_ids[:, None, :]
    slot_rank = jnp.sum(same_owner & earlier[None], axis=2)
    slot_ids = jnp.arange(capacity, dtype=jnp.int32)
    chosen = (owner_ids[:, None, :] == this_shard) & (
        slot_rank[:, None, :] == slot_ids[None, :, None]
    )
    serve_block = jnp.sum(jnp.where(chosen, local_ids[:, None, :], 0), axis=2)
    slot_used = jnp.any(chosen, axis=2)
    owner_mine = lax.dynamic_index_in_dim(owner_ids, this_shard, 0, keepdims=False)
    rank_mine = lax.dynamic_index_in_dim(slot_rank, this_shard, 0, keepdims=False)
    return (serve_block, slot_used, owner_mine, rank_mine)


def token_live(tile_ids, pad_sizes, query_blocks, shard_tokens, total_blocks):
    valid = (tile_ids >= 0) & (tile_ids < total_blocks)
    safe_ids = jnp.clip(tile_ids, 0, total_blocks - 1)
    owner_shard = safe_ids // query_blocks
    shards = pad_sizes.shape[0]
    pad_of = jnp.sum(
        jnp.where(owner_shard[..., None] == jnp.arange(shards, dtype=jnp.int32), pad_sizes, 0),
        axis=-1,
    )
    within = (safe_ids % query_blocks)[..., None] * BLK + jnp.arange(BLK, dtype=jnp.int32)
    return valid[..., None] & (within < (shard_tokens - pad_of)[..., None])


def body(queries, keys, values, out_grads, random_blocks, global_blocks, pad_lengths):
    query_rows = queries[0]
    key_rows = keys[0]
    value_rows = values[0]
    grad_rows = out_grads[0]
    random_table = random_blocks[0]
    global_ids = global_blocks[0]
    pad_sizes = pad_lengths[0]
    shards = lax.axis_size("seq")
    this_shard = lax.axis_index("seq")
    shard_tokens, qwidth = query_rows.shape
    kwidth = key_rows.shape[1]
    query_blocks = shard_tokens // BLK
    total_blocks = query_blocks * shards
    own_blocks = jnp.stack(
        [key_rows.reshape(query_blocks, BLK, kwidth), value_rows.reshape(query_blocks, BLK, kwidth)],
        axis=1,
    )
    up = [(i, (i + 1) % shards) for i in range(shards - 1)]
    down = [(j, i) for i, j in up]
    edge_before = lax.ppermute(own_blocks[query_blocks - 1 :], "seq", up)
    edge_after = lax.ppermute(own_blocks[:1], "seq", down)
    requests = random_table.reshape(shards, query_blocks * RAND)
    plan = request_plan(requests, this_shard, query_blocks)
    serve_block, slot_used, owner_mine, rank_mine = plan
    capacity = serve_block.shape[1]
    block_rows = 2 * BLK
    nb = query_blocks
    unit_rows = GLOB * block_rows // shards
    unit_span = block_rows // unit_rows
    own_units = jnp.concatenate(
        [
            own_blocks.reshape(nb * unit_span, unit_rows, kwidth),
            jnp.zeros((1, unit_rows, kwidth), own_blocks.dtype),
        ]
    )
    unit_range = jnp.arange(unit_span, dtype=jnp.int32)
    served_idx = (serve_block[:, :, None] * unit_span + unit_range).reshape(shards, -1)
    global_owned = global_ids // query_blocks == this_shard
    global_idx = jnp.where(
        global_owned[:, None],
        (global_ids % query_blocks)[:, None] * unit_span + unit_range,
        nb * unit_span,
    ).reshape(shards, -1)
    payload_idx = jnp.concatenate([served_idx, global_idx], axis=1)
    payload = jnp.take(own_units, payload_idx.reshape(-1), axis=0, mode="clip").reshape(
        shards, -1, kwidth
    )
    received = lax.all_to_all(payload, "seq", 0, 0, tiled=True)
    global_piece = jnp.sum(received[:, capacity * block_rows :], axis=0, dtype=own_blocks.dtype)
    global_tiles = lax.all_to_all(
        jnp.broadcast_to(global_piece[None], (shards,) + global_piece.shape), "seq", 0, 0, tiled=True
    ).reshape(GLOB, block_rows, kwidth)
    window = jnp.concatenate([edge_before, own_blocks, edge_after], axis=0).reshape(
        nb + 2, block_rows, kwidth
    )
    block_range = jnp.arange(nb, dtype=jnp.int32)
    random_ids = jnp.stack(
        [owner_mine, jnp.clip(rank_mine, 0, capacity - 1)], axis=1
    ).reshape(-1)
    random_three = random_table.reshape(shards, query_blocks, RAND)
    base_ids = this_shard * query_blocks + block_range
    window_ids = base_ids[:, None] + jnp.arange(-1, 2, dtype=jnp.int32)[None, :]
    my_random = lax.dynamic_index_in_dim(random_three, this_shard, 0, keepdims=False)
    tile_ids = jnp.concatenate(
        [window_ids, jnp.broadcast_to(global_ids[None, :], (query_blocks, GLOB)), my_random], axis=1
    )
    key_live = token_live(tile_ids, pad_sizes, query_blocks, shard_tokens, total_blocks)
    query_grad, local_sum, edge_terms, global_part, random_part = block_backward(
        query_rows, grad_rows, window, global_tiles, received, random_ids, key_live
    )
    handed_query = from_behind(query_grad, "section", -1)
    edge_low = edge_terms.astype(jnp.bfloat16)
    from_after = lax.ppermute(edge_low[:1], "seq", down)
    from_before = lax.ppermute(edge_low[1:], "seq", up)
    holder = jnp.zeros((shards, capacity, 2, BLK, kwidth), random_part.dtype)
    holder = holder.at[owner_mine, rank_mine].set(
        random_part.reshape(query_blocks * RAND, 2, BLK, kwidth)
    )
    global_low = global_part.astype(jnp.bfloat16).reshape(shards, -1, kwidth)
    returned = lax.all_to_all(
        jnp.concatenate([holder.reshape(shards, capacity * block_rows, kwidth), global_low], axis=1),
        "seq",
        0,
        0,
        tiled=True,
    )
    random_back = returned[:, : capacity * block_rows].reshape(shards * capacity, 2, BLK, kwidth)
    global_sum = jnp.sum(returned[:, capacity * block_rows :].astype(jnp.float32), axis=0)
    global_sum = global_sum.astype(jnp.bfloat16)
    global_total = lax.all_to_all(
        jnp.broadcast_to(global_sum[None], (shards,) + global_sum.shape), "seq", 0, 0, tiled=True
    ).reshape(GLOB, 2, BLK, kwidth).astype(jnp.float32)
    onehot = (
        slot_used.reshape(-1)[None, :]
        & (serve_block.reshape(-1)[None, :] == block_range[:, None])
    ).astype(jnp.bfloat16)
    kv_sum = local_sum + jnp.einsum(
        "qf,fxsk->qxsk", onehot, random_back, preferred_element_type=jnp.float32
    )
    kv_sum = kv_sum.at[nb - 1].add(from_after[0].astype(jnp.float32))
    kv_sum = kv_sum.at[0].add(from_before[0].astype(jnp.float32))
    global_pick = (
        (global_ids[:, None] // query_blocks == this_shard)
        & (global_ids[:, None] % query_blocks == block_range[None, :])
    ).astype(jnp.float32)
    kv_sum = kv_sum + jnp.einsum(
        "gq,gxsk->qxsk", global_pick, global_total, precision=lax.Precision.HIGHEST
    )
    kv_grad = jnp.concatenate(
        [
            kv_sum[:, 0].reshape(shard_tokens, kwidth).astype(jnp.bfloat16),
            kv_sum[:, 1].reshape(shard_tokens, kwidth).astype(jnp.bfloat16),
        ],
        axis=-1,
    )
    handed_kv = from_behind(kv_grad, "section", -1)
    return (
        handed_query[None],
        handed_kv[None, :, :kwidth],
        handed_kv[None, :, kwidth:],
    )


def solution(mesh):
    in_specs = (
        P("section", "seq", None),
        P("section", "seq", None),
        P("section", "seq", None),
        P("section", "seq", None),
        P("section", None, None),
        P("section", None),
        P("section", None),
    )
    out_specs = (P("section", "seq", None), P("section", "seq", None), P("section", "seq", None))
    return jax.shard_map(body, mesh=mesh, in_specs=in_specs, out_specs=out_specs, check_vma=False)
```

```python
import math

import jax
import jax.numpy as jnp
from jax import lax
from jax.experimental import pallas as pl
from jax.experimental.pallas import tpu as pltpu
from jax.sharding import PartitionSpec as P

HDIM = 128
BLK = 64
GLOB = 2
RAND = 3


def extended_2(array, sides, width):
    for axis, dim in sides:
        devices, length = (lax.axis_size(axis), array.shape[dim])
        up = [(i, (i + 1) % devices) for i in range(devices - 1)]
        down = [(j, i) for i, j in up]
        last = lax.slice_in_dim(array, length - width, length, axis=dim)
        leading = lax.slice_in_dim(array, 0, width, axis=dim)
        before = lax.ppermute(last, axis, up)
        after = lax.ppermute(leading, axis, down)
        array = jnp.concatenate([before, array, after], axis=dim)
    return array


def broadcast(array, axis, root):
    mine = lax.axis_index(axis) == root
    return lax.psum(jnp.where(mine, array, jnp.zeros_like(array)), axis)


def from_behind(block, axis, distance):
    devices = range(lax.axis_size(axis))
    route = [((i - distance) % len(devices), i) for i in devices]
    return lax.ppermute(block, axis, route)


def attention_kernel(ids_ref, q_ref, g_ref, *refs):
    del ids_ref
    ntiles = len(refs) - 6
    tile_refs = refs[:ntiles]
    live_ref = refs[ntiles]
    dq_ref, own_ref, edge_ref, glob_ref, rand_ref = refs[ntiles + 1 :]
    nblocks = own_ref.shape[0]
    block_len, width = q_ref.shape
    group = width // HDIM
    near = 3 + GLOB
    b = pl.program_id(1)
    score_scale = 1.0 / math.sqrt(HDIM)
    query = q_ref[...]
    grad = g_ref[...]
    query_rows = jnp.concatenate(
        [query[:, g * HDIM : (g + 1) * HDIM] for g in range(group)], axis=0
    )
    grad_rows = jnp.concatenate([grad[:, g * HDIM : (g + 1) * HDIM] for g in range(group)], axis=0)
    key_rows = jnp.concatenate([tile_refs[t][:block_len] for t in range(ntiles)], axis=0)
    value_rows = jnp.concatenate([tile_refs[t][block_len:] for t in range(ntiles)], axis=0)
    live = live_ref[...] > 0.5
    contract_last = (((1,), (1,)), ((), ()))
    contract_first = (((0,), (0,)), ((), ()))
    scores = (
        lax.dot_general(key_rows, query_rows, contract_last, preferred_element_type=jnp.float32)
        * score_scale
    )
    scores = jnp.where(live, scores, -1e30)
    row_max = jnp.max(scores, axis=0, keepdims=True)
    shifted = jnp.exp(scores - row_max)
    total = jnp.sum(shifted, axis=0, keepdims=True)
    probs = shifted * (1.0 / total)
    probs_low = probs.astype(jnp.bfloat16)
    output = lax.dot_general(
        value_rows, probs_low, contract_first, preferred_element_type=jnp.float32
    )
    grad_cols = grad_rows.astype(jnp.float32).T
    row_dot = jnp.sum(grad_cols * output, axis=0, keepdims=True)
    prob_grad = lax.dot_general(
        value_rows, grad_rows, contract_last, preferred_element_type=jnp.float32
    )
    score_grad = (probs * (prob_grad - row_dot)).astype(jnp.bfloat16)
    query_grad = (
        lax.dot_general(key_rows, score_grad, contract_first, preferred_element_type=jnp.float32)
        * score_scale
    ).T
    key_grad = jnp.dot(score_grad, query_rows, preferred_element_type=jnp.float32) * score_scale
    value_grad = jnp.dot(probs_low, grad_rows, preferred_element_type=jnp.float32)
    for g in range(group):
        dq_ref[:, g * HDIM : (g + 1) * HDIM] = query_grad[g * block_len : (g + 1) * block_len].astype(
            dq_ref.dtype
        )
    terms = jnp.stack(
        [key_grad.reshape(ntiles, block_len, HDIM), value_grad.reshape(ntiles, block_len, HDIM)],
        axis=1,
    )

    @pl.when(b == 0)
    def _():
        own_ref[...] = jnp.zeros_like(own_ref)
        glob_ref[...] = jnp.zeros_like(glob_ref)
        edge_ref[0] = terms[0]

    @pl.when(b > 0)
    def _():
        before = jnp.maximum(b - 1, 0)
        own_ref[before] = own_ref[before] + terms[0]

    own_ref[b] = own_ref[b] + terms[1]

    @pl.when(b < nblocks - 1)
    def _():
        after = jnp.minimum(b + 1, nblocks - 1)
        own_ref[after] = own_ref[after] + terms[2]

    @pl.when(b == nblocks - 1)
    def _():
        edge_ref[1] = terms[2]

    glob_ref[...] = glob_ref[...] + terms[3:near]
    rand_ref[...] = terms[near:].astype(rand_ref.dtype)


def block_backward(query_rows, grad_rows, window, global_tiles, received, random_ids, key_live):
    shard_tokens, qwidth = query_rows.shape
    kwidth = window.shape[-1]
    nblocks = window.shape[0] - 2
    block_len = window.shape[1] // 2
    near = 3 + GLOB
    nrand = random_ids.shape[0] // (2 * nblocks)
    ntiles = near + nrand
    heads_kv = kwidth // HDIM
    group_width = qwidth // heads_kv
    pair_rows = 2 * block_len
    live = key_live.reshape(nblocks, ntiles * block_len, 1).astype(jnp.float32)
    row_spec = pl.BlockSpec((block_len, group_width), lambda h, b, ids: (b, h))
    tile_specs = [
        pl.BlockSpec((None, pair_rows, HDIM), lambda h, b, ids, t=t: (b + t, 0, h)) for t in range(3)
    ]
    tile_specs += [
        pl.BlockSpec((None, pair_rows, HDIM), lambda h, b, ids, g=g: (g, 0, h)) for g in range(GLOB)
    ]
    tile_specs += [
        pl.BlockSpec(
            (None, pair_rows, HDIM),
            lambda h, b, ids, r=r: (ids[(b * nrand + r) * 2], ids[(b * nrand + r) * 2 + 1], h),
        )
        for r in range(nrand)
    ]
    live_spec = pl.BlockSpec((None, ntiles * block_len, 1), lambda h, b, ids: (b, 0, 0))
    own_spec = pl.BlockSpec((nblocks, 2, block_len, HDIM), lambda h, b, ids: (0, 0, 0, h))
    edge_spec = pl.BlockSpec((2, 2, block_len, HDIM), lambda h, b, ids: (0, 0, 0, h))
    glob_spec = pl.BlockSpec((GLOB, 2, block_len, HDIM), lambda h, b, ids: (0, 0, 0, h))
    rand_spec = pl.BlockSpec((None, nrand, 2, block_len, HDIM), lambda h, b, ids: (b, 0, 0, 0, h))
    flops = 12 * nblocks * heads_kv * (group_width // HDIM) * block_len * ntiles * block_len * HDIM
    grid_spec = pltpu.PrefetchScalarGridSpec(
        num_scalar_prefetch=1,
        grid=(heads_kv, nblocks),
        in_specs=[row_spec, row_spec, *tile_specs, live_spec],
        out_specs=[row_spec, own_spec, edge_spec, glob_spec, rand_spec],
    )
    outs = pl.pallas_call(
        attention_kernel,
        grid_spec=grid_spec,
        out_shape=[
            jax.ShapeDtypeStruct((shard_tokens, qwidth), jnp.bfloat16),
            jax.ShapeDtypeStruct((nblocks, 2, block_len, kwidth), jnp.float32),
            jax.ShapeDtypeStruct((2, 2, block_len, kwidth), jnp.float32),
            jax.ShapeDtypeStruct((GLOB, 2, block_len, kwidth), jnp.float32),
            jax.ShapeDtypeStruct((nblocks, nrand, 2, block_len, kwidth), jnp.bfloat16),
        ],
        compiler_params=pltpu.CompilerParams(
            dimension_semantics=("arbitrary", "arbitrary")
        ),
        cost_estimate=pl.CostEstimate(
            flops=flops,
            transcendentals=nblocks * qwidth // HDIM * block_len * ntiles * block_len,
            bytes_accessed=shard_tokens * qwidth * 6 + nblocks * ntiles * block_len * kwidth * 6,
        ),
    )(
        random_ids,
        query_rows,
        grad_rows,
        *([window] * 3),
        *([global_tiles] * GLOB),
        *([received] * nrand),
        live,
    )
    return outs


def request_plan(request_lists, this_shard, query_blocks):
    shards, count = request_lists.shape
    capacity = -(-count // shards)
    owner_ids = request_lists // query_blocks
    local_ids = request_lists % query_blocks
    order = jnp.arange(count, dtype=jnp.int32)
    earlier = order[None, :] < order[:, None]
    same_owner = owner_ids[:, :, None] == owner_ids[:, None, :]
    slot_rank = jnp.sum(same_owner & earlier[None], axis=2)
    slot_ids = jnp.arange(capacity, dtype=jnp.int32)
    chosen = (owner_ids[:, None, :] == this_shard) & (
        slot_rank[:, None, :] == slot_ids[None, :, None]
    )
    serve_block = jnp.sum(jnp.where(chosen, local_ids[:, None, :], 0), axis=2)
    slot_used = jnp.any(chosen, axis=2)
    owner_mine = lax.dynamic_index_in_dim(owner_ids, this_shard, 0, keepdims=False)
    rank_mine = lax.dynamic_index_in_dim(slot_rank, this_shard, 0, keepdims=False)
    return (serve_block, slot_used, owner_mine, rank_mine)


def token_live(tile_ids, pad_sizes, query_blocks, shard_tokens, total_blocks):
    valid = (tile_ids >= 0) & (tile_ids < total_blocks)
    safe_ids = jnp.clip(tile_ids, 0, total_blocks - 1)
    owner_shard = safe_ids // query_blocks
    shards = pad_sizes.shape[0]
    pad_of = jnp.sum(
        jnp.where(owner_shard[..., None] == jnp.arange(shards, dtype=jnp.int32), pad_sizes, 0),
        axis=-1,
    )
    within = (safe_ids % query_blocks)[..., None] * BLK + jnp.arange(BLK, dtype=jnp.int32)
    return valid[..., None] & (within < (shard_tokens - pad_of)[..., None])


def body(queries, keys, values, out_grads, random_blocks, global_blocks, pad_lengths):
    query_rows = queries[0]
    key_rows = keys[0]
    value_rows = values[0]
    grad_rows = out_grads[0]
    random_table = random_blocks[0]
    global_ids = global_blocks[0]
    pad_sizes = pad_lengths[0]
    shards = lax.axis_size("seq")
    this_shard = lax.axis_index("seq")
    shard_tokens, qwidth = query_rows.shape
    kwidth = key_rows.shape[1]
    query_blocks = shard_tokens // BLK
    total_blocks = query_blocks * shards
    own_blocks = jnp.stack(
        [key_rows.reshape(query_blocks, BLK, kwidth), value_rows.reshape(query_blocks, BLK, kwidth)],
        axis=1,
    )
    up = [(i, (i + 1) % shards) for i in range(shards - 1)]
    down = [(j, i) for i, j in up]
    edge_before = lax.ppermute(own_blocks[query_blocks - 1 :], "seq", up)
    edge_after = lax.ppermute(own_blocks[:1], "seq", down)
    requests = random_table.reshape(shards, query_blocks * RAND)
    plan = request_plan(requests, this_shard, query_blocks)
    serve_block, slot_used, owner_mine, rank_mine = plan
    capacity = serve_block.shape[1]
    block_rows = 2 * BLK
    nb = query_blocks
    unit_rows = GLOB * block_rows // shards
    unit_span = block_rows // unit_rows
    own_units = jnp.concatenate(
        [
            own_blocks.reshape(nb * unit_span, unit_rows, kwidth),
            jnp.zeros((1, unit_rows, kwidth), own_blocks.dtype),
        ]
    )
    unit_range = jnp.arange(unit_span, dtype=jnp.int32)
    served_idx = (serve_block[:, :, None] * unit_span + unit_range).reshape(shards, -1)
    global_owned = global_ids // query_blocks == this_shard
    global_idx = jnp.where(
        global_owned[:, None],
        (global_ids % query_blocks)[:, None] * unit_span + unit_range,
        nb * unit_span,
    ).reshape(shards, -1)
    payload_idx = jnp.concatenate([served_idx, global_idx], axis=1)
    payload = jnp.take(own_units, payload_idx.reshape(-1), axis=0, mode="clip").reshape(
        shards, -1, kwidth
    )
    received = lax.all_to_all(payload, "seq", 0, 0, tiled=True)
    global_piece = jnp.sum(received[:, capacity * block_rows :], axis=0, dtype=own_blocks.dtype)
    global_tiles = lax.all_to_all(
        jnp.broadcast_to(global_piece[None], (shards,) + global_piece.shape), "seq", 0, 0, tiled=True
    ).reshape(GLOB, block_rows, kwidth)
    window = jnp.concatenate([edge_before, own_blocks, edge_after], axis=0).reshape(
        nb + 2, block_rows, kwidth
    )
    block_range = jnp.arange(nb, dtype=jnp.int32)
    random_ids = jnp.stack(
        [owner_mine, jnp.clip(rank_mine, 0, capacity - 1)], axis=1
    ).reshape(-1)
    random_three = random_table.reshape(shards, query_blocks, RAND)
    base_ids = this_shard * query_blocks + block_range
    window_ids = base_ids[:, None] + jnp.arange(-1, 2, dtype=jnp.int32)[None, :]
    my_random = lax.dynamic_index_in_dim(random_three, this_shard, 0, keepdims=False)
    tile_ids = jnp.concatenate(
        [window_ids, jnp.broadcast_to(global_ids[None, :], (query_blocks, GLOB)), my_random], axis=1
    )
    key_live = token_live(tile_ids, pad_sizes, query_blocks, shard_tokens, total_blocks)
    query_grad, local_sum, edge_terms, global_part, random_part = block_backward(
        query_rows, grad_rows, window, global_tiles, received, random_ids, key_live
    )
    handed_query = from_behind(query_grad, "section", -1)
    edge_low = edge_terms.astype(jnp.bfloat16)
    from_after = lax.ppermute(edge_low[:1], "seq", down)
    from_before = lax.ppermute(edge_low[1:], "seq", up)
    ntile = query_blocks * RAND
    global_low = global_part.astype(jnp.bfloat16).reshape(shards, unit_rows, kwidth)
    term_units = jnp.concatenate(
        [
            random_part.reshape(ntile * unit_span, unit_rows, kwidth),
            global_low,
            jnp.zeros((1, unit_rows, kwidth), random_part.dtype),
        ]
    )
    tile_range = jnp.arange(ntile, dtype=jnp.int32)
    slot_match = (owner_mine[None, None, :] == jnp.arange(shards, dtype=jnp.int32)[:, None, None]) & (
        rank_mine[None, None, :] == jnp.arange(capacity, dtype=jnp.int32)[None, :, None]
    )
    slot_tile = jnp.sum(jnp.where(slot_match, tile_range, 0), axis=2)
    slot_idx = jnp.where(
        jnp.any(slot_match, axis=2)[:, :, None],
        slot_tile[:, :, None] * unit_span + unit_range,
        ntile * unit_span + shards,
    ).reshape(shards, -1)
    back_idx = jnp.concatenate(
        [slot_idx, ntile * unit_span + jnp.arange(shards, dtype=jnp.int32)[:, None]], axis=1
    )
    returned = lax.all_to_all(
        jnp.take(term_units, back_idx.reshape(-1), axis=0, mode="clip").reshape(shards, -1, kwidth),
        "seq",
        0,
        0,
        tiled=True,
    )
    random_back = returned[:, : capacity * block_rows].reshape(shards * capacity, 2, BLK, kwidth)
    global_sum = jnp.sum(returned[:, capacity * block_rows :].astype(jnp.float32), axis=0)
    global_sum = global_sum.astype(jnp.bfloat16)
    global_total = lax.all_to_all(
        jnp.broadcast_to(global_sum[None], (shards,) + global_sum.shape), "seq", 0, 0, tiled=True
    ).reshape(GLOB, 2, BLK, kwidth).astype(jnp.float32)
    onehot = (
        slot_used.reshape(-1)[None, :]
        & (serve_block.reshape(-1)[None, :] == block_range[:, None])
    ).astype(jnp.bfloat16)
    kv_sum = local_sum + jnp.einsum(
        "qf,fxsk->qxsk", onehot, random_back, preferred_element_type=jnp.float32
    )
    kv_sum = kv_sum.at[nb - 1].add(from_after[0].astype(jnp.float32))
    kv_sum = kv_sum.at[0].add(from_before[0].astype(jnp.float32))
    global_pick = (
        (global_ids[:, None] // query_blocks == this_shard)
        & (global_ids[:, None] % query_blocks == block_range[None, :])
    ).astype(jnp.float32)
    kv_sum = kv_sum + jnp.einsum(
        "gq,gxsk->qxsk", global_pick, global_total, precision=lax.Precision.HIGHEST
    )
    kv_grad = jnp.concatenate(
        [
            kv_sum[:, 0].reshape(shard_tokens, kwidth).astype(jnp.bfloat16),
            kv_sum[:, 1].reshape(shard_tokens, kwidth).astype(jnp.bfloat16),
        ],
        axis=-1,
    )
    handed_kv = from_behind(kv_grad, "section", -1)
    return (
        handed_query[None],
        handed_kv[None, :, :kwidth],
        handed_kv[None, :, kwidth:],
    )


def solution(mesh):
    in_specs = (
        P("section", "seq", None),
        P("section", "seq", None),
        P("section", "seq", None),
        P("section", "seq", None),
        P("section", None, None),
        P("section", None),
        P("section", None),
    )
    out_specs = (P("section", "seq", None), P("section", "seq", None), P("section", "seq", None))
    return jax.shard_map(body, mesh=mesh, in_specs=in_specs, out_specs=out_specs, check_vma=False)
```

```python
import math

import jax
import jax.numpy as jnp
from jax import lax
from jax.experimental import pallas as pl
from jax.experimental.pallas import tpu as pltpu
from jax.sharding import PartitionSpec as P

HDIM = 128
BLK = 64
GLOB = 2
RAND = 3


def extended_2(array, sides, width):
    for axis, dim in sides:
        devices, length = (lax.axis_size(axis), array.shape[dim])
        up = [(i, (i + 1) % devices) for i in range(devices - 1)]
        down = [(j, i) for i, j in up]
        last = lax.slice_in_dim(array, length - width, length, axis=dim)
        leading = lax.slice_in_dim(array, 0, width, axis=dim)
        before = lax.ppermute(last, axis, up)
        after = lax.ppermute(leading, axis, down)
        array = jnp.concatenate([before, array, after], axis=dim)
    return array


def broadcast(array, axis, root):
    mine = lax.axis_index(axis) == root
    return lax.psum(jnp.where(mine, array, jnp.zeros_like(array)), axis)


def from_behind(block, axis, distance):
    devices = range(lax.axis_size(axis))
    route = [((i - distance) % len(devices), i) for i in devices]
    return lax.ppermute(block, axis, route)


def copy_kernel(src_ref, dst_ref):
    dst_ref[...] = src_ref[...]


def fresh_copy(array):
    rows, width = array.shape[-2:]
    spec = pl.BlockSpec((None, rows, width), lambda i: (0, 0, 0))
    return pl.pallas_call(
        copy_kernel,
        grid=(1,),
        in_specs=[spec],
        out_specs=spec,
        out_shape=jax.ShapeDtypeStruct(array.shape, array.dtype),
        cost_estimate=pl.CostEstimate(flops=0, transcendentals=0, bytes_accessed=2 * array.size * array.dtype.itemsize),
    )(array)


def attention_kernel(ids_ref, q_ref, g_ref, *refs):
    del ids_ref
    ntiles = len(refs) - 6
    tile_refs = refs[:ntiles]
    live_ref = refs[ntiles]
    dq_ref, own_ref, edge_ref, glob_ref, rand_ref = refs[ntiles + 1 :]
    nblocks = own_ref.shape[0]
    block_len, width = q_ref.shape
    group = width // HDIM
    near = 3 + GLOB
    b = pl.program_id(1)
    score_scale = 1.0 / math.sqrt(HDIM)
    query = q_ref[...]
    grad = g_ref[...]
    query_rows = jnp.concatenate(
        [query[:, g * HDIM : (g + 1) * HDIM] for g in range(group)], axis=0
    )
    grad_rows = jnp.concatenate([grad[:, g * HDIM : (g + 1) * HDIM] for g in range(group)], axis=0)
    key_rows = jnp.concatenate([tile_refs[t][:block_len] for t in range(ntiles)], axis=0)
    value_rows = jnp.concatenate([tile_refs[t][block_len:] for t in range(ntiles)], axis=0)
    live = live_ref[...] > 0.5
    contract_last = (((1,), (1,)), ((), ()))
    contract_first = (((0,), (0,)), ((), ()))
    scores = (
        lax.dot_general(key_rows, query_rows, contract_last, preferred_element_type=jnp.float32)
        * score_scale
    )
    scores = jnp.where(live, scores, -1e30)
    row_max = jnp.max(scores, axis=0, keepdims=True)
    shifted = jnp.exp(scores - row_max)
    total = jnp.sum(shifted, axis=0, keepdims=True)
    probs = shifted * (1.0 / total)
    probs_low = probs.astype(jnp.bfloat16)
    output = lax.dot_general(
        value_rows, probs_low, contract_first, preferred_element_type=jnp.float32
    )
    grad_cols = grad_rows.astype(jnp.float32).T
    row_dot = jnp.sum(grad_cols * output, axis=0, keepdims=True)
    prob_grad = lax.dot_general(
        value_rows, grad_rows, contract_last, preferred_element_type=jnp.float32
    )
    score_grad = (probs * (prob_grad - row_dot)).astype(jnp.bfloat16)
    query_grad = (
        lax.dot_general(key_rows, score_grad, contract_first, preferred_element_type=jnp.float32)
        * score_scale
    ).T
    key_grad = jnp.dot(score_grad, query_rows, preferred_element_type=jnp.float32) * score_scale
    value_grad = jnp.dot(probs_low, grad_rows, preferred_element_type=jnp.float32)
    for g in range(group):
        dq_ref[:, g * HDIM : (g + 1) * HDIM] = query_grad[g * block_len : (g + 1) * block_len].astype(
            dq_ref.dtype
        )
    terms = jnp.stack(
        [key_grad.reshape(ntiles, block_len, HDIM), value_grad.reshape(ntiles, block_len, HDIM)],
        axis=1,
    )

    @pl.when(b == 0)
    def _():
        own_ref[...] = jnp.zeros_like(own_ref)
        glob_ref[...] = jnp.zeros_like(glob_ref)
        edge_ref[0] = terms[0]

    @pl.when(b > 0)
    def _():
        before = jnp.maximum(b - 1, 0)
        own_ref[before] = own_ref[before] + terms[0]

    own_ref[b] = own_ref[b] + terms[1]

    @pl.when(b < nblocks - 1)
    def _():
        after = jnp.minimum(b + 1, nblocks - 1)
        own_ref[after] = own_ref[after] + terms[2]

    @pl.when(b == nblocks - 1)
    def _():
        edge_ref[1] = terms[2]

    glob_ref[...] = glob_ref[...] + terms[3:near]
    rand_ref[...] = terms[near:].astype(rand_ref.dtype)


def block_backward(query_rows, grad_rows, window, global_tiles, received, random_ids, key_live):
    shard_tokens, qwidth = query_rows.shape
    kwidth = window.shape[-1]
    nblocks = window.shape[0] - 2
    block_len = window.shape[1] // 2
    near = 3 + GLOB
    nrand = random_ids.shape[0] // (2 * nblocks)
    ntiles = near + nrand
    heads_kv = kwidth // HDIM
    group_width = qwidth // heads_kv
    pair_rows = 2 * block_len
    live = key_live.reshape(nblocks, ntiles * block_len, 1).astype(jnp.float32)
    row_spec = pl.BlockSpec((block_len, group_width), lambda h, b, ids: (b, h))
    tile_specs = [
        pl.BlockSpec((None, pair_rows, HDIM), lambda h, b, ids, t=t: (b + t, 0, h)) for t in range(3)
    ]
    tile_specs += [
        pl.BlockSpec((None, pair_rows, HDIM), lambda h, b, ids, g=g: (g, 0, h)) for g in range(GLOB)
    ]
    tile_specs += [
        pl.BlockSpec(
            (None, pair_rows, HDIM),
            lambda h, b, ids, r=r: (ids[(b * nrand + r) * 2], ids[(b * nrand + r) * 2 + 1], h),
        )
        for r in range(nrand)
    ]
    live_spec = pl.BlockSpec((None, ntiles * block_len, 1), lambda h, b, ids: (b, 0, 0))
    own_spec = pl.BlockSpec((nblocks, 2, block_len, HDIM), lambda h, b, ids: (0, 0, 0, h))
    edge_spec = pl.BlockSpec((2, 2, block_len, HDIM), lambda h, b, ids: (0, 0, 0, h))
    glob_spec = pl.BlockSpec((GLOB, 2, block_len, HDIM), lambda h, b, ids: (0, 0, 0, h))
    rand_spec = pl.BlockSpec((None, nrand, 2, block_len, HDIM), lambda h, b, ids: (b, 0, 0, 0, h))
    flops = 12 * nblocks * heads_kv * (group_width // HDIM) * block_len * ntiles * block_len * HDIM
    grid_spec = pltpu.PrefetchScalarGridSpec(
        num_scalar_prefetch=1,
        grid=(heads_kv, nblocks),
        in_specs=[row_spec, row_spec, *tile_specs, live_spec],
        out_specs=[row_spec, own_spec, edge_spec, glob_spec, rand_spec],
    )
    outs = pl.pallas_call(
        attention_kernel,
        grid_spec=grid_spec,
        out_shape=[
            jax.ShapeDtypeStruct((shard_tokens, qwidth), jnp.bfloat16),
            jax.ShapeDtypeStruct((nblocks, 2, block_len, kwidth), jnp.float32),
            jax.ShapeDtypeStruct((2, 2, block_len, kwidth), jnp.float32),
            jax.ShapeDtypeStruct((GLOB, 2, block_len, kwidth), jnp.float32),
            jax.ShapeDtypeStruct((nblocks, nrand, 2, block_len, kwidth), jnp.bfloat16),
        ],
        compiler_params=pltpu.CompilerParams(
            dimension_semantics=("arbitrary", "arbitrary")
        ),
        cost_estimate=pl.CostEstimate(
            flops=flops,
            transcendentals=nblocks * qwidth // HDIM * block_len * ntiles * block_len,
            bytes_accessed=shard_tokens * qwidth * 6 + nblocks * ntiles * block_len * kwidth * 6,
        ),
    )(
        random_ids,
        query_rows,
        grad_rows,
        *([window] * 3),
        *([global_tiles] * GLOB),
        *([received] * nrand),
        live,
    )
    return outs


def request_plan(request_lists, this_shard, query_blocks):
    shards, count = request_lists.shape
    capacity = -(-count // shards)
    owner_ids = request_lists // query_blocks
    local_ids = request_lists % query_blocks
    order = jnp.arange(count, dtype=jnp.int32)
    earlier = order[None, :] < order[:, None]
    same_owner = owner_ids[:, :, None] == owner_ids[:, None, :]
    slot_rank = jnp.sum(same_owner & earlier[None], axis=2)
    slot_ids = jnp.arange(capacity, dtype=jnp.int32)
    chosen = (owner_ids[:, None, :] == this_shard) & (
        slot_rank[:, None, :] == slot_ids[None, :, None]
    )
    serve_block = jnp.sum(jnp.where(chosen, local_ids[:, None, :], 0), axis=2)
    slot_used = jnp.any(chosen, axis=2)
    owner_mine = lax.dynamic_index_in_dim(owner_ids, this_shard, 0, keepdims=False)
    rank_mine = lax.dynamic_index_in_dim(slot_rank, this_shard, 0, keepdims=False)
    return (serve_block, slot_used, owner_mine, rank_mine)


def token_live(tile_ids, pad_sizes, query_blocks, shard_tokens, total_blocks):
    valid = (tile_ids >= 0) & (tile_ids < total_blocks)
    safe_ids = jnp.clip(tile_ids, 0, total_blocks - 1)
    owner_shard = safe_ids // query_blocks
    shards = pad_sizes.shape[0]
    pad_of = jnp.sum(
        jnp.where(owner_shard[..., None] == jnp.arange(shards, dtype=jnp.int32), pad_sizes, 0),
        axis=-1,
    )
    within = (safe_ids % query_blocks)[..., None] * BLK + jnp.arange(BLK, dtype=jnp.int32)
    return valid[..., None] & (within < (shard_tokens - pad_of)[..., None])


def body(queries, keys, values, out_grads, random_blocks, global_blocks, pad_lengths):
    query_rows = queries[0]
    key_rows = keys[0]
    value_rows = values[0]
    grad_rows = out_grads[0]
    random_table = random_blocks[0]
    global_ids = global_blocks[0]
    pad_sizes = pad_lengths[0]
    shards = lax.axis_size("seq")
    this_shard = lax.axis_index("seq")
    shard_tokens, qwidth = query_rows.shape
    kwidth = key_rows.shape[1]
    query_blocks = shard_tokens // BLK
    total_blocks = query_blocks * shards
    own_blocks = jnp.stack(
        [key_rows.reshape(query_blocks, BLK, kwidth), value_rows.reshape(query_blocks, BLK, kwidth)],
        axis=1,
    )
    up = [(i, (i + 1) % shards) for i in range(shards - 1)]
    down = [(j, i) for i, j in up]
    edge_before = lax.ppermute(own_blocks[query_blocks - 1 :], "seq", up)
    edge_after = lax.ppermute(own_blocks[:1], "seq", down)
    requests = random_table.reshape(shards, query_blocks * RAND)
    plan = request_plan(requests, this_shard, query_blocks)
    serve_block, slot_used, owner_mine, rank_mine = plan
    capacity = serve_block.shape[1]
    block_rows = 2 * BLK
    nb = query_blocks
    unit_rows = GLOB * block_rows // shards
    unit_span = block_rows // unit_rows
    own_units = jnp.concatenate(
        [
            own_blocks.reshape(nb * unit_span, unit_rows, kwidth),
            jnp.zeros((1, unit_rows, kwidth), own_blocks.dtype),
        ]
    )
    unit_range = jnp.arange(unit_span, dtype=jnp.int32)
    served_idx = (serve_block[:, :, None] * unit_span + unit_range).reshape(shards, -1)
    global_owned = global_ids // query_blocks == this_shard
    global_idx = jnp.where(
        global_owned[:, None],
        (global_ids % query_blocks)[:, None] * unit_span + unit_range,
        nb * unit_span,
    ).reshape(shards, -1)
    payload_idx = jnp.concatenate([served_idx, global_idx], axis=1)
    payload = jnp.take(own_units, payload_idx.reshape(-1), axis=0, mode="clip").reshape(
        shards, -1, kwidth
    )
    received = lax.all_to_all(payload, "seq", 0, 0, tiled=True)
    global_piece = jnp.sum(received[:, capacity * block_rows :], axis=0, dtype=own_blocks.dtype)
    global_tiles = lax.all_to_all(
        jnp.broadcast_to(global_piece[None], (shards,) + global_piece.shape), "seq", 0, 0, tiled=True
    ).reshape(GLOB, block_rows, kwidth)
    window = jnp.concatenate([edge_before, own_blocks, edge_after], axis=0).reshape(
        nb + 2, block_rows, kwidth
    )
    block_range = jnp.arange(nb, dtype=jnp.int32)
    random_ids = jnp.stack(
        [owner_mine, jnp.clip(rank_mine, 0, capacity - 1)], axis=1
    ).reshape(-1)
    random_three = random_table.reshape(shards, query_blocks, RAND)
    base_ids = this_shard * query_blocks + block_range
    window_ids = base_ids[:, None] + jnp.arange(-1, 2, dtype=jnp.int32)[None, :]
    my_random = lax.dynamic_index_in_dim(random_three, this_shard, 0, keepdims=False)
    tile_ids = jnp.concatenate(
        [window_ids, jnp.broadcast_to(global_ids[None, :], (query_blocks, GLOB)), my_random], axis=1
    )
    key_live = token_live(tile_ids, pad_sizes, query_blocks, shard_tokens, total_blocks)
    query_grad, local_sum, edge_terms, global_part, random_part = block_backward(
        query_rows, grad_rows, window, global_tiles, received, random_ids, key_live
    )
    handed_query = from_behind(query_grad[None], "section", -1)
    edge_low = edge_terms.astype(jnp.bfloat16)
    from_after = lax.ppermute(edge_low[:1], "seq", down)
    from_before = lax.ppermute(edge_low[1:], "seq", up)
    ntile = query_blocks * RAND
    global_low = global_part.astype(jnp.bfloat16).reshape(shards, unit_rows, kwidth)
    term_units = jnp.concatenate(
        [
            random_part.reshape(ntile * unit_span, unit_rows, kwidth),
            global_low,
            jnp.zeros((1, unit_rows, kwidth), random_part.dtype),
        ]
    )
    tile_range = jnp.arange(ntile, dtype=jnp.int32)
    slot_match = (owner_mine[None, None, :] == jnp.arange(shards, dtype=jnp.int32)[:, None, None]) & (
        rank_mine[None, None, :] == jnp.arange(capacity, dtype=jnp.int32)[None, :, None]
    )
    slot_tile = jnp.sum(jnp.where(slot_match, tile_range, 0), axis=2)
    slot_idx = jnp.where(
        jnp.any(slot_match, axis=2)[:, :, None],
        slot_tile[:, :, None] * unit_span + unit_range,
        ntile * unit_span + shards,
    ).reshape(shards, -1)
    back_idx = jnp.concatenate(
        [slot_idx, ntile * unit_span + jnp.arange(shards, dtype=jnp.int32)[:, None]], axis=1
    )
    returned = lax.all_to_all(
        jnp.take(term_units, back_idx.reshape(-1), axis=0, mode="clip").reshape(shards, -1, kwidth),
        "seq",
        0,
        0,
        tiled=True,
    )
    random_back = returned[:, : capacity * block_rows].reshape(shards * capacity, 2, BLK, kwidth)
    global_sum = jnp.sum(returned[:, capacity * block_rows :].astype(jnp.float32), axis=0)
    global_sum = global_sum.astype(jnp.bfloat16)
    global_total = lax.all_to_all(
        jnp.broadcast_to(global_sum[None], (shards,) + global_sum.shape), "seq", 0, 0, tiled=True
    ).reshape(GLOB, 2, BLK, kwidth).astype(jnp.float32)
    onehot = (
        slot_used.reshape(-1)[None, :]
        & (serve_block.reshape(-1)[None, :] == block_range[:, None])
    ).astype(jnp.bfloat16)
    kv_sum = local_sum + jnp.einsum(
        "qf,fxsk->qxsk", onehot, random_back, preferred_element_type=jnp.float32
    )
    kv_sum = kv_sum.at[nb - 1].add(from_after[0].astype(jnp.float32))
    kv_sum = kv_sum.at[0].add(from_before[0].astype(jnp.float32))
    global_pick = (
        (global_ids[:, None] // query_blocks == this_shard)
        & (global_ids[:, None] % query_blocks == block_range[None, :])
    ).astype(jnp.float32)
    kv_sum = kv_sum + jnp.einsum(
        "gq,gxsk->qxsk", global_pick, global_total, precision=lax.Precision.HIGHEST
    )
    kv_grad = jnp.concatenate(
        [
            kv_sum[:, 0].reshape(shard_tokens, kwidth).astype(jnp.bfloat16),
            kv_sum[:, 1].reshape(shard_tokens, kwidth).astype(jnp.bfloat16),
        ],
        axis=-1,
    )
    handed_query, kv_grad = lax.optimization_barrier((fresh_copy(handed_query), kv_grad))
    handed_kv = from_behind(kv_grad, "section", -1)
    return (
        handed_query,
        handed_kv[None, :, :kwidth],
        handed_kv[None, :, kwidth:],
    )


def solution(mesh):
    in_specs = (
        P("section", "seq", None),
        P("section", "seq", None),
        P("section", "seq", None),
        P("section", "seq", None),
        P("section", None, None),
        P("section", None),
        P("section", None),
    )
    out_specs = (P("section", "seq", None), P("section", "seq", None), P("section", "seq", None))
    return jax.shard_map(body, mesh=mesh, in_specs=in_specs, out_specs=out_specs, check_vma=False)
```

```python
import math

import jax
import jax.numpy as jnp
from jax import lax
from jax.experimental import pallas as pl
from jax.experimental.pallas import tpu as pltpu
from jax.sharding import PartitionSpec as P

HDIM = 128
BLK = 64
GLOB = 2
RAND = 3


def extended_2(array, sides, width):
    for axis, dim in sides:
        devices, length = (lax.axis_size(axis), array.shape[dim])
        up = [(i, (i + 1) % devices) for i in range(devices - 1)]
        down = [(j, i) for i, j in up]
        last = lax.slice_in_dim(array, length - width, length, axis=dim)
        leading = lax.slice_in_dim(array, 0, width, axis=dim)
        before = lax.ppermute(last, axis, up)
        after = lax.ppermute(leading, axis, down)
        array = jnp.concatenate([before, array, after], axis=dim)
    return array


def broadcast(array, axis, root):
    mine = lax.axis_index(axis) == root
    return lax.psum(jnp.where(mine, array, jnp.zeros_like(array)), axis)


def from_behind(block, axis, distance):
    devices = range(lax.axis_size(axis))
    route = [((i - distance) % len(devices), i) for i in devices]
    return lax.ppermute(block, axis, route)


def chunk_sum(chunks, axis):
    devices = lax.axis_size(axis)
    me = lax.axis_index(axis)
    total = lax.dynamic_index_in_dim(chunks, me, 0, keepdims=False)
    for d in range(1, devices):
        send = lax.dynamic_index_in_dim(chunks, (me + d) % devices, 0, keepdims=False)
        total = total + lax.ppermute(send, axis, [(i, (i + d) % devices) for i in range(devices)])
    return total


def chunk_gather(piece, axis):
    devices = lax.axis_size(axis)
    me = lax.axis_index(axis)
    stacked = [piece] + [
        lax.ppermute(piece, axis, [(i, (i + d) % devices) for i in range(devices)])
        for d in range(1, devices)
    ]
    order = (me - jnp.arange(devices, dtype=jnp.int32)) % devices
    return jnp.take(jnp.stack(stacked), order, axis=0, mode="clip")


def copy_kernel(src_ref, dst_ref):
    dst_ref[...] = src_ref[...]


def fresh_copy(array):
    rows, width = array.shape[-2:]
    spec = pl.BlockSpec((None, rows, width), lambda i: (0, 0, 0))
    return pl.pallas_call(
        copy_kernel,
        grid=(1,),
        in_specs=[spec],
        out_specs=spec,
        out_shape=jax.ShapeDtypeStruct(array.shape, array.dtype),
        cost_estimate=pl.CostEstimate(flops=0, transcendentals=0, bytes_accessed=2 * array.size * array.dtype.itemsize),
    )(array)


def attention_kernel(ids_ref, q_ref, g_ref, *refs):
    del ids_ref
    ntiles = len(refs) - 6
    tile_refs = refs[:ntiles]
    live_ref = refs[ntiles]
    dq_ref, own_ref, edge_ref, glob_ref, rand_ref = refs[ntiles + 1 :]
    nblocks = own_ref.shape[0]
    block_len, width = q_ref.shape
    group = width // HDIM
    near = 3 + GLOB
    b = pl.program_id(1)
    score_scale = 1.0 / math.sqrt(HDIM)
    query = q_ref[...]
    grad = g_ref[...]
    query_rows = jnp.concatenate(
        [query[:, g * HDIM : (g + 1) * HDIM] for g in range(group)], axis=0
    )
    grad_rows = jnp.concatenate([grad[:, g * HDIM : (g + 1) * HDIM] for g in range(group)], axis=0)
    key_rows = jnp.concatenate([tile_refs[t][:block_len] for t in range(ntiles)], axis=0)
    value_rows = jnp.concatenate([tile_refs[t][block_len:] for t in range(ntiles)], axis=0)
    live = live_ref[...] > 0.5
    contract_last = (((1,), (1,)), ((), ()))
    contract_first = (((0,), (0,)), ((), ()))
    scores = (
        lax.dot_general(key_rows, query_rows, contract_last, preferred_element_type=jnp.float32)
        * score_scale
    )
    scores = jnp.where(live, scores, -1e30)
    row_max = jnp.max(scores, axis=0, keepdims=True)
    shifted = jnp.exp(scores - row_max)
    total = jnp.sum(shifted, axis=0, keepdims=True)
    probs = shifted * (1.0 / total)
    probs_low = probs.astype(jnp.bfloat16)
    output = lax.dot_general(
        value_rows, probs_low, contract_first, preferred_element_type=jnp.float32
    )
    grad_cols = grad_rows.astype(jnp.float32).T
    row_dot = jnp.sum(grad_cols * output, axis=0, keepdims=True)
    prob_grad = lax.dot_general(
        value_rows, grad_rows, contract_last, preferred_element_type=jnp.float32
    )
    score_grad = (probs * (prob_grad - row_dot)).astype(jnp.bfloat16)
    query_grad = (
        lax.dot_general(key_rows, score_grad, contract_first, preferred_element_type=jnp.float32)
        * score_scale
    ).T
    key_grad = jnp.dot(score_grad, query_rows, preferred_element_type=jnp.float32) * score_scale
    value_grad = jnp.dot(probs_low, grad_rows, preferred_element_type=jnp.float32)
    for g in range(group):
        dq_ref[:, g * HDIM : (g + 1) * HDIM] = query_grad[g * block_len : (g + 1) * block_len].astype(
            dq_ref.dtype
        )
    terms = jnp.stack(
        [key_grad.reshape(ntiles, block_len, HDIM), value_grad.reshape(ntiles, block_len, HDIM)],
        axis=1,
    )

    @pl.when(b == 0)
    def _():
        own_ref[...] = jnp.zeros_like(own_ref)
        glob_ref[...] = jnp.zeros_like(glob_ref)
        edge_ref[0] = terms[0]

    @pl.when(b > 0)
    def _():
        before = jnp.maximum(b - 1, 0)
        own_ref[before] = own_ref[before] + terms[0]

    own_ref[b] = own_ref[b] + terms[1]

    @pl.when(b < nblocks - 1)
    def _():
        after = jnp.minimum(b + 1, nblocks - 1)
        own_ref[after] = own_ref[after] + terms[2]

    @pl.when(b == nblocks - 1)
    def _():
        edge_ref[1] = terms[2]

    glob_ref[...] = glob_ref[...] + terms[3:near]
    rand_ref[...] = terms[near:].astype(rand_ref.dtype)


def block_backward(query_rows, grad_rows, window, global_tiles, received, random_ids, key_live):
    shard_tokens, qwidth = query_rows.shape
    kwidth = window.shape[-1]
    nblocks = window.shape[0] - 2
    block_len = window.shape[1] // 2
    near = 3 + GLOB
    nrand = random_ids.shape[0] // (2 * nblocks)
    ntiles = near + nrand
    heads_kv = kwidth // HDIM
    group_width = qwidth // heads_kv
    pair_rows = 2 * block_len
    live = key_live.reshape(nblocks, ntiles * block_len, 1).astype(jnp.float32)
    row_spec = pl.BlockSpec((block_len, group_width), lambda h, b, ids: (b, h))
    tile_specs = [
        pl.BlockSpec((None, pair_rows, HDIM), lambda h, b, ids, t=t: (b + t, 0, h)) for t in range(3)
    ]
    tile_specs += [
        pl.BlockSpec((None, pair_rows, HDIM), lambda h, b, ids, g=g: (g, 0, h)) for g in range(GLOB)
    ]
    tile_specs += [
        pl.BlockSpec(
            (None, pair_rows, HDIM),
            lambda h, b, ids, r=r: (ids[(b * nrand + r) * 2], ids[(b * nrand + r) * 2 + 1], h),
        )
        for r in range(nrand)
    ]
    live_spec = pl.BlockSpec((None, ntiles * block_len, 1), lambda h, b, ids: (b, 0, 0))
    own_spec = pl.BlockSpec((nblocks, 2, block_len, HDIM), lambda h, b, ids: (0, 0, 0, h))
    edge_spec = pl.BlockSpec((2, 2, block_len, HDIM), lambda h, b, ids: (0, 0, 0, h))
    glob_spec = pl.BlockSpec((GLOB, 2, block_len, HDIM), lambda h, b, ids: (0, 0, 0, h))
    rand_spec = pl.BlockSpec((None, nrand, 2, block_len, HDIM), lambda h, b, ids: (b, 0, 0, 0, h))
    flops = 12 * nblocks * heads_kv * (group_width // HDIM) * block_len * ntiles * block_len * HDIM
    grid_spec = pltpu.PrefetchScalarGridSpec(
        num_scalar_prefetch=1,
        grid=(heads_kv, nblocks),
        in_specs=[row_spec, row_spec, *tile_specs, live_spec],
        out_specs=[row_spec, own_spec, edge_spec, glob_spec, rand_spec],
    )
    outs = pl.pallas_call(
        attention_kernel,
        grid_spec=grid_spec,
        out_shape=[
            jax.ShapeDtypeStruct((shard_tokens, qwidth), jnp.bfloat16),
            jax.ShapeDtypeStruct((nblocks, 2, block_len, kwidth), jnp.float32),
            jax.ShapeDtypeStruct((2, 2, block_len, kwidth), jnp.float32),
            jax.ShapeDtypeStruct((GLOB, 2, block_len, kwidth), jnp.float32),
            jax.ShapeDtypeStruct((nblocks, nrand, 2, block_len, kwidth), jnp.bfloat16),
        ],
        compiler_params=pltpu.CompilerParams(
            dimension_semantics=("arbitrary", "arbitrary")
        ),
        cost_estimate=pl.CostEstimate(
            flops=flops,
            transcendentals=nblocks * qwidth // HDIM * block_len * ntiles * block_len,
            bytes_accessed=shard_tokens * qwidth * 6 + nblocks * ntiles * block_len * kwidth * 6,
        ),
    )(
        random_ids,
        query_rows,
        grad_rows,
        *([window] * 3),
        *([global_tiles] * GLOB),
        *([received] * nrand),
        live,
    )
    return outs


def request_plan(request_lists, this_shard, query_blocks):
    shards, count = request_lists.shape
    capacity = -(-count // shards)
    owner_ids = request_lists // query_blocks
    local_ids = request_lists % query_blocks
    order = jnp.arange(count, dtype=jnp.int32)
    earlier = order[None, :] < order[:, None]
    same_owner = owner_ids[:, :, None] == owner_ids[:, None, :]
    slot_rank = jnp.sum(same_owner & earlier[None], axis=2)
    slot_ids = jnp.arange(capacity, dtype=jnp.int32)
    chosen = (owner_ids[:, None, :] == this_shard) & (
        slot_rank[:, None, :] == slot_ids[None, :, None]
    )
    serve_block = jnp.sum(jnp.where(chosen, local_ids[:, None, :], 0), axis=2)
    slot_used = jnp.any(chosen, axis=2)
    owner_mine = lax.dynamic_index_in_dim(owner_ids, this_shard, 0, keepdims=False)
    rank_mine = lax.dynamic_index_in_dim(slot_rank, this_shard, 0, keepdims=False)
    return (serve_block, slot_used, owner_mine, rank_mine)


def token_live(tile_ids, pad_sizes, query_blocks, shard_tokens, total_blocks):
    valid = (tile_ids >= 0) & (tile_ids < total_blocks)
    safe_ids = jnp.clip(tile_ids, 0, total_blocks - 1)
    owner_shard = safe_ids // query_blocks
    shards = pad_sizes.shape[0]
    pad_of = jnp.sum(
        jnp.where(owner_shard[..., None] == jnp.arange(shards, dtype=jnp.int32), pad_sizes, 0),
        axis=-1,
    )
    within = (safe_ids % query_blocks)[..., None] * BLK + jnp.arange(BLK, dtype=jnp.int32)
    return valid[..., None] & (within < (shard_tokens - pad_of)[..., None])


def body(queries, keys, values, out_grads, random_blocks, global_blocks, pad_lengths):
    query_rows = queries[0]
    key_rows = keys[0]
    value_rows = values[0]
    grad_rows = out_grads[0]
    random_table = random_blocks[0]
    global_ids = global_blocks[0]
    pad_sizes = pad_lengths[0]
    shards = lax.axis_size("seq")
    this_shard = lax.axis_index("seq")
    shard_tokens, qwidth = query_rows.shape
    kwidth = key_rows.shape[1]
    query_blocks = shard_tokens // BLK
    total_blocks = query_blocks * shards
    own_blocks = jnp.stack(
        [key_rows.reshape(query_blocks, BLK, kwidth), value_rows.reshape(query_blocks, BLK, kwidth)],
        axis=1,
    )
    up = [(i, (i + 1) % shards) for i in range(shards - 1)]
    down = [(j, i) for i, j in up]
    edge_before = lax.ppermute(own_blocks[query_blocks - 1 :], "seq", up)
    edge_after = lax.ppermute(own_blocks[:1], "seq", down)
    requests = random_table.reshape(shards, query_blocks * RAND)
    plan = request_plan(requests, this_shard, query_blocks)
    serve_block, slot_used, owner_mine, rank_mine = plan
    capacity = serve_block.shape[1]
    block_rows = 2 * BLK
    nb = query_blocks
    unit_rows = GLOB * block_rows // shards
    unit_span = block_rows // unit_rows
    unit_range = jnp.arange(unit_span, dtype=jnp.int32)
    served = jnp.take(own_blocks, serve_block.reshape(-1), axis=0, mode="clip").reshape(
        shards, capacity * block_rows, kwidth
    )
    global_mine = [
        jnp.where(
            global_ids[g] // query_blocks == this_shard,
            lax.dynamic_index_in_dim(own_blocks, global_ids[g] % query_blocks, 0, keepdims=True),
            jnp.zeros((), own_blocks.dtype),
        )
        for g in range(GLOB)
    ]
    global_chunks = jnp.concatenate(global_mine, axis=0).reshape(shards, unit_rows, kwidth)
    received = lax.all_to_all(served, "seq", 0, 0, tiled=True)
    global_piece = chunk_sum(global_chunks, "seq")
    global_tiles = chunk_gather(global_piece, "seq").reshape(GLOB, block_rows, kwidth)
    window = jnp.concatenate([edge_before, own_blocks, edge_after], axis=0).reshape(
        nb + 2, block_rows, kwidth
    )
    block_range = jnp.arange(nb, dtype=jnp.int32)
    random_ids = jnp.stack(
        [owner_mine, jnp.clip(rank_mine, 0, capacity - 1)], axis=1
    ).reshape(-1)
    random_three = random_table.reshape(shards, query_blocks, RAND)
    base_ids = this_shard * query_blocks + block_range
    window_ids = base_ids[:, None] + jnp.arange(-1, 2, dtype=jnp.int32)[None, :]
    my_random = lax.dynamic_index_in_dim(random_three, this_shard, 0, keepdims=False)
    tile_ids = jnp.concatenate(
        [window_ids, jnp.broadcast_to(global_ids[None, :], (query_blocks, GLOB)), my_random], axis=1
    )
    key_live = token_live(tile_ids, pad_sizes, query_blocks, shard_tokens, total_blocks)
    query_grad, local_sum, edge_terms, global_part, random_part = block_backward(
        query_rows, grad_rows, window, global_tiles, received, random_ids, key_live
    )
    handed_query = from_behind(query_grad[None], "section", -1)
    edge_low = edge_terms.astype(jnp.bfloat16)
    from_after = lax.ppermute(edge_low[:1], "seq", down)
    from_before = lax.ppermute(edge_low[1:], "seq", up)
    ntile = query_blocks * RAND
    global_chunks_back = global_part.reshape(shards, unit_rows, kwidth)
    term_units = jnp.concatenate(
        [
            random_part.reshape(ntile * unit_span, unit_rows, kwidth),
            jnp.zeros((1, unit_rows, kwidth), random_part.dtype),
        ]
    )
    tile_range = jnp.arange(ntile, dtype=jnp.int32)
    slot_match = (owner_mine[None, None, :] == jnp.arange(shards, dtype=jnp.int32)[:, None, None]) & (
        rank_mine[None, None, :] == jnp.arange(capacity, dtype=jnp.int32)[None, :, None]
    )
    slot_tile = jnp.sum(jnp.where(slot_match, tile_range, 0), axis=2)
    back_idx = jnp.where(
        jnp.any(slot_match, axis=2)[:, :, None],
        slot_tile[:, :, None] * unit_span + unit_range,
        ntile * unit_span,
    ).reshape(-1)
    returned = lax.all_to_all(
        jnp.take(term_units, back_idx, axis=0, mode="clip").reshape(shards, -1, kwidth),
        "seq",
        0,
        0,
        tiled=True,
    )
    global_sum = chunk_sum(global_chunks_back, "seq")
    global_total = chunk_gather(global_sum, "seq").reshape(GLOB, 2, BLK, kwidth)
    random_back = returned.reshape(shards * capacity, 2, BLK, kwidth)
    onehot = (
        slot_used.reshape(-1)[None, :]
        & (serve_block.reshape(-1)[None, :] == block_range[:, None])
    ).astype(jnp.bfloat16)
    kv_sum = local_sum + jnp.einsum(
        "qf,fxsk->qxsk", onehot, random_back, preferred_element_type=jnp.float32
    )
    kv_sum = kv_sum.at[nb - 1].add(from_after[0].astype(jnp.float32))
    kv_sum = kv_sum.at[0].add(from_before[0].astype(jnp.float32))
    global_pick = (
        (global_ids[:, None] // query_blocks == this_shard)
        & (global_ids[:, None] % query_blocks == block_range[None, :])
    ).astype(jnp.float32)
    kv_sum = kv_sum + jnp.einsum(
        "gq,gxsk->qxsk", global_pick, global_total, precision=lax.Precision.HIGHEST
    )
    kv_grad = jnp.concatenate(
        [
            kv_sum[:, 0].reshape(shard_tokens, kwidth).astype(jnp.bfloat16),
            kv_sum[:, 1].reshape(shard_tokens, kwidth).astype(jnp.bfloat16),
        ],
        axis=-1,
    )
    handed_query, kv_grad = lax.optimization_barrier((fresh_copy(handed_query), kv_grad))
    handed_kv = from_behind(kv_grad, "section", -1)
    return (
        handed_query,
        handed_kv[None, :, :kwidth],
        handed_kv[None, :, kwidth:],
    )


def solution(mesh):
    in_specs = (
        P("section", "seq", None),
        P("section", "seq", None),
        P("section", "seq", None),
        P("section", "seq", None),
        P("section", None, None),
        P("section", None),
        P("section", None),
    )
    out_specs = (P("section", "seq", None), P("section", "seq", None), P("section", "seq", None))
    return jax.shard_map(body, mesh=mesh, in_specs=in_specs, out_specs=out_specs, check_vma=False)
```

```python
import math

import jax
import jax.numpy as jnp
from jax import lax
from jax.experimental import pallas as pl
from jax.experimental.pallas import tpu as pltpu
from jax.sharding import PartitionSpec as P

HDIM = 128
BLK = 64
GLOB = 2
RAND = 3


def extended_2(array, sides, width):
    for axis, dim in sides:
        devices, length = (lax.axis_size(axis), array.shape[dim])
        up = [(i, (i + 1) % devices) for i in range(devices - 1)]
        down = [(j, i) for i, j in up]
        last = lax.slice_in_dim(array, length - width, length, axis=dim)
        leading = lax.slice_in_dim(array, 0, width, axis=dim)
        before = lax.ppermute(last, axis, up)
        after = lax.ppermute(leading, axis, down)
        array = jnp.concatenate([before, array, after], axis=dim)
    return array


def broadcast(array, axis, root):
    mine = lax.axis_index(axis) == root
    return lax.psum(jnp.where(mine, array, jnp.zeros_like(array)), axis)


def from_behind(block, axis, distance):
    devices = range(lax.axis_size(axis))
    route = [((i - distance) % len(devices), i) for i in devices]
    return lax.ppermute(block, axis, route)


def copy_kernel(src_ref, dst_ref):
    dst_ref[...] = src_ref[...]


def fresh_copy(array):
    rows, width = array.shape[-2:]
    spec = pl.BlockSpec((None, rows, width), lambda i: (0, 0, 0))
    return pl.pallas_call(
        copy_kernel,
        grid=(1,),
        in_specs=[spec],
        out_specs=spec,
        out_shape=jax.ShapeDtypeStruct(array.shape, array.dtype),
        cost_estimate=pl.CostEstimate(flops=0, transcendentals=0, bytes_accessed=2 * array.size * array.dtype.itemsize),
    )(array)


def attention_kernel(ids_ref, q_ref, g_ref, *refs):
    del ids_ref
    ntiles = len(refs) - 7
    tile_refs = refs[:ntiles]
    live_ref = refs[ntiles]
    dq_ref, own_ref, edge_ref, glob_out, rand_ref, glob_ref = refs[ntiles + 1 :]
    nblocks = own_ref.shape[0]
    block_len, width = q_ref.shape
    group = width // HDIM
    near = 3 + GLOB
    b = pl.program_id(1)
    score_scale = 1.0 / math.sqrt(HDIM)
    query = q_ref[...]
    grad = g_ref[...]
    query_rows = jnp.concatenate(
        [query[:, g * HDIM : (g + 1) * HDIM] for g in range(group)], axis=0
    )
    grad_rows = jnp.concatenate([grad[:, g * HDIM : (g + 1) * HDIM] for g in range(group)], axis=0)
    key_rows = jnp.concatenate([tile_refs[t][:block_len] for t in range(ntiles)], axis=0)
    value_rows = jnp.concatenate([tile_refs[t][block_len:] for t in range(ntiles)], axis=0)
    live = live_ref[...] > 0.5
    contract_last = (((1,), (1,)), ((), ()))
    contract_first = (((0,), (0,)), ((), ()))
    scores = (
        lax.dot_general(key_rows, query_rows, contract_last, preferred_element_type=jnp.float32)
        * score_scale
    )
    scores = jnp.where(live, scores, -1e30)
    row_max = jnp.max(scores, axis=0, keepdims=True)
    shifted = jnp.exp(scores - row_max)
    total = jnp.sum(shifted, axis=0, keepdims=True)
    probs = shifted * (1.0 / total)
    probs_low = probs.astype(jnp.bfloat16)
    output = lax.dot_general(
        value_rows, probs_low, contract_first, preferred_element_type=jnp.float32
    )
    grad_cols = grad_rows.astype(jnp.float32).T
    row_dot = jnp.sum(grad_cols * output, axis=0, keepdims=True)
    prob_grad = lax.dot_general(
        value_rows, grad_rows, contract_last, preferred_element_type=jnp.float32
    )
    score_grad = (probs * (prob_grad - row_dot)).astype(jnp.bfloat16)
    query_grad = (
        lax.dot_general(key_rows, score_grad, contract_first, preferred_element_type=jnp.float32)
        * score_scale
    ).T
    key_grad = jnp.dot(score_grad, query_rows, preferred_element_type=jnp.float32) * score_scale
    value_grad = jnp.dot(probs_low, grad_rows, preferred_element_type=jnp.float32)
    for g in range(group):
        dq_ref[:, g * HDIM : (g + 1) * HDIM] = query_grad[g * block_len : (g + 1) * block_len].astype(
            dq_ref.dtype
        )
    terms = jnp.stack(
        [key_grad.reshape(ntiles, block_len, HDIM), value_grad.reshape(ntiles, block_len, HDIM)],
        axis=1,
    )

    @pl.when(b == 0)
    def _():
        own_ref[...] = jnp.zeros_like(own_ref)
        glob_ref[...] = jnp.zeros_like(glob_ref)
        edge_ref[0] = terms[0].astype(edge_ref.dtype)

    @pl.when(b > 0)
    def _():
        before = jnp.maximum(b - 1, 0)
        own_ref[before] = own_ref[before] + terms[0]

    own_ref[b] = own_ref[b] + terms[1]

    @pl.when(b < nblocks - 1)
    def _():
        after = jnp.minimum(b + 1, nblocks - 1)
        own_ref[after] = own_ref[after] + terms[2]

    @pl.when(b == nblocks - 1)
    def _():
        edge_ref[1] = terms[2].astype(edge_ref.dtype)

    glob_ref[...] = glob_ref[...] + terms[3:near]

    @pl.when(b == nblocks - 1)
    def _():
        glob_out[...] = glob_ref[...].astype(glob_out.dtype)
    rand_ref[...] = terms[near:].astype(rand_ref.dtype)


def block_backward(query_rows, grad_rows, window, global_tiles, received, random_ids, key_live):
    shard_tokens, qwidth = query_rows.shape
    kwidth = window.shape[-1]
    nblocks = window.shape[0] - 2
    block_len = window.shape[1] // 2
    near = 3 + GLOB
    nrand = random_ids.shape[0] // (2 * nblocks)
    ntiles = near + nrand
    heads_kv = kwidth // HDIM
    group_width = qwidth // heads_kv
    pair_rows = 2 * block_len
    live = key_live.reshape(nblocks, ntiles * block_len, 1).astype(jnp.float32)
    row_spec = pl.BlockSpec((block_len, group_width), lambda h, b, ids: (b, h))
    tile_specs = [
        pl.BlockSpec((None, pair_rows, HDIM), lambda h, b, ids, t=t: (b + t, 0, h)) for t in range(3)
    ]
    tile_specs += [
        pl.BlockSpec((None, pair_rows, HDIM), lambda h, b, ids, g=g: (g, 0, h)) for g in range(GLOB)
    ]
    tile_specs += [
        pl.BlockSpec(
            (None, pair_rows, HDIM),
            lambda h, b, ids, r=r: (ids[(b * nrand + r) * 2], ids[(b * nrand + r) * 2 + 1], h),
        )
        for r in range(nrand)
    ]
    live_spec = pl.BlockSpec((None, ntiles * block_len, 1), lambda h, b, ids: (b, 0, 0))
    own_spec = pl.BlockSpec((nblocks, 2, block_len, HDIM), lambda h, b, ids: (0, 0, 0, h))
    edge_spec = pl.BlockSpec((2, 2, block_len, HDIM), lambda h, b, ids: (0, 0, 0, h))
    glob_spec = pl.BlockSpec((GLOB, 2, block_len, HDIM), lambda h, b, ids: (0, 0, 0, h))
    rand_spec = pl.BlockSpec((None, nrand, 2, block_len, HDIM), lambda h, b, ids: (b, 0, 0, 0, h))
    flops = 12 * nblocks * heads_kv * (group_width // HDIM) * block_len * ntiles * block_len * HDIM
    grid_spec = pltpu.PrefetchScalarGridSpec(
        num_scalar_prefetch=1,
        grid=(heads_kv, nblocks),
        in_specs=[row_spec, row_spec, *tile_specs, live_spec],
        out_specs=[row_spec, own_spec, edge_spec, glob_spec, rand_spec],
        scratch_shapes=[pltpu.VMEM((GLOB, 2, block_len, HDIM), jnp.float32)],
    )
    outs = pl.pallas_call(
        attention_kernel,
        grid_spec=grid_spec,
        out_shape=[
            jax.ShapeDtypeStruct((shard_tokens, qwidth), jnp.bfloat16),
            jax.ShapeDtypeStruct((nblocks, 2, block_len, kwidth), jnp.float32),
            jax.ShapeDtypeStruct((2, 2, block_len, kwidth), jnp.bfloat16),
            jax.ShapeDtypeStruct((GLOB, 2, block_len, kwidth), jnp.bfloat16),
            jax.ShapeDtypeStruct((nblocks, nrand, 2, block_len, kwidth), jnp.bfloat16),
        ],
        compiler_params=pltpu.CompilerParams(
            dimension_semantics=("arbitrary", "arbitrary")
        ),
        cost_estimate=pl.CostEstimate(
            flops=flops,
            transcendentals=nblocks * qwidth // HDIM * block_len * ntiles * block_len,
            bytes_accessed=shard_tokens * qwidth * 6 + nblocks * ntiles * block_len * kwidth * 6,
        ),
    )(
        random_ids,
        query_rows,
        grad_rows,
        *([window] * 3),
        *([global_tiles] * GLOB),
        *([received] * nrand),
        live,
    )
    return outs


def request_plan(request_lists, this_shard, query_blocks):
    shards, count = request_lists.shape
    capacity = -(-count // shards)
    owner_ids = request_lists // query_blocks
    local_ids = request_lists % query_blocks
    order = jnp.arange(count, dtype=jnp.int32)
    earlier = order[None, :] < order[:, None]
    same_owner = owner_ids[:, :, None] == owner_ids[:, None, :]
    slot_rank = jnp.sum(same_owner & earlier[None], axis=2)
    slot_ids = jnp.arange(capacity, dtype=jnp.int32)
    chosen = (owner_ids[:, None, :] == this_shard) & (
        slot_rank[:, None, :] == slot_ids[None, :, None]
    )
    serve_block = jnp.sum(jnp.where(chosen, local_ids[:, None, :], 0), axis=2)
    slot_used = jnp.any(chosen, axis=2)
    owner_mine = lax.dynamic_index_in_dim(owner_ids, this_shard, 0, keepdims=False)
    rank_mine = lax.dynamic_index_in_dim(slot_rank, this_shard, 0, keepdims=False)
    return (serve_block, slot_used, owner_mine, rank_mine)


def token_live(tile_ids, pad_sizes, query_blocks, shard_tokens, total_blocks):
    valid = (tile_ids >= 0) & (tile_ids < total_blocks)
    safe_ids = jnp.clip(tile_ids, 0, total_blocks - 1)
    owner_shard = safe_ids // query_blocks
    shards = pad_sizes.shape[0]
    pad_of = jnp.sum(
        jnp.where(owner_shard[..., None] == jnp.arange(shards, dtype=jnp.int32), pad_sizes, 0),
        axis=-1,
    )
    within = (safe_ids % query_blocks)[..., None] * BLK + jnp.arange(BLK, dtype=jnp.int32)
    return valid[..., None] & (within < (shard_tokens - pad_of)[..., None])


def body(queries, keys, values, out_grads, random_blocks, global_blocks, pad_lengths):
    query_rows = queries[0]
    key_rows = keys[0]
    value_rows = values[0]
    grad_rows = out_grads[0]
    random_table = random_blocks[0]
    global_ids = global_blocks[0]
    pad_sizes = pad_lengths[0]
    shards = lax.axis_size("seq")
    this_shard = lax.axis_index("seq")
    shard_tokens, qwidth = query_rows.shape
    kwidth = key_rows.shape[1]
    query_blocks = shard_tokens // BLK
    total_blocks = query_blocks * shards
    own_blocks = jnp.stack(
        [key_rows.reshape(query_blocks, BLK, kwidth), value_rows.reshape(query_blocks, BLK, kwidth)],
        axis=1,
    )
    up = [(i, (i + 1) % shards) for i in range(shards - 1)]
    down = [(j, i) for i, j in up]
    edge_before = lax.ppermute(own_blocks[query_blocks - 1 :], "seq", up)
    edge_after = lax.ppermute(own_blocks[:1], "seq", down)
    requests = random_table.reshape(shards, query_blocks * RAND)
    plan = request_plan(requests, this_shard, query_blocks)
    serve_block, slot_used, owner_mine, rank_mine = plan
    capacity = serve_block.shape[1]
    block_rows = 2 * BLK
    nb = query_blocks
    unit_rows = GLOB * block_rows // shards
    unit_span = block_rows // unit_rows
    own_units = jnp.concatenate(
        [
            own_blocks.reshape(nb * unit_span, unit_rows, kwidth),
            jnp.zeros((1, unit_rows, kwidth), own_blocks.dtype),
        ]
    )
    unit_range = jnp.arange(unit_span, dtype=jnp.int32)
    served_idx = (serve_block[:, :, None] * unit_span + unit_range).reshape(shards, -1)
    global_owned = global_ids // query_blocks == this_shard
    global_idx = jnp.where(
        global_owned[:, None],
        (global_ids % query_blocks)[:, None] * unit_span + unit_range,
        nb * unit_span,
    ).reshape(shards, -1)
    payload_idx = jnp.concatenate([served_idx, global_idx], axis=1)
    payload = jnp.take(own_units, payload_idx.reshape(-1), axis=0, mode="clip").reshape(
        shards, -1, kwidth
    )
    received = lax.all_to_all(payload, "seq", 0, 0, tiled=True)
    global_piece = jnp.sum(received[:, capacity * block_rows :], axis=0, dtype=own_blocks.dtype)
    global_tiles = lax.all_to_all(
        jnp.broadcast_to(global_piece[None], (shards,) + global_piece.shape), "seq", 0, 0, tiled=True
    ).reshape(GLOB, block_rows, kwidth)
    window = jnp.concatenate([edge_before, own_blocks, edge_after], axis=0).reshape(
        nb + 2, block_rows, kwidth
    )
    block_range = jnp.arange(nb, dtype=jnp.int32)
    random_ids = jnp.stack(
        [owner_mine, jnp.clip(rank_mine, 0, capacity - 1)], axis=1
    ).reshape(-1)
    random_three = random_table.reshape(shards, query_blocks, RAND)
    base_ids = this_shard * query_blocks + block_range
    window_ids = base_ids[:, None] + jnp.arange(-1, 2, dtype=jnp.int32)[None, :]
    my_random = lax.dynamic_index_in_dim(random_three, this_shard, 0, keepdims=False)
    tile_ids = jnp.concatenate(
        [window_ids, jnp.broadcast_to(global_ids[None, :], (query_blocks, GLOB)), my_random], axis=1
    )
    key_live = token_live(tile_ids, pad_sizes, query_blocks, shard_tokens, total_blocks)
    query_grad, local_sum, edge_terms, global_part, random_part = block_backward(
        query_rows, grad_rows, window, global_tiles, received, random_ids, key_live
    )
    handed_query = from_behind(query_grad[None], "section", -1)
    edge_low = edge_terms.astype(jnp.bfloat16)
    from_after = lax.ppermute(edge_low[:1], "seq", down)
    from_before = lax.ppermute(edge_low[1:], "seq", up)
    ntile = query_blocks * RAND
    global_low = global_part.astype(jnp.bfloat16).reshape(shards, unit_rows, kwidth)
    term_units = jnp.concatenate(
        [
            random_part.reshape(ntile * unit_span, unit_rows, kwidth),
            global_low,
            jnp.zeros((1, unit_rows, kwidth), random_part.dtype),
        ]
    )
    tile_range = jnp.arange(ntile, dtype=jnp.int32)
    slot_match = (owner_mine[None, None, :] == jnp.arange(shards, dtype=jnp.int32)[:, None, None]) & (
        rank_mine[None, None, :] == jnp.arange(capacity, dtype=jnp.int32)[None, :, None]
    )
    slot_tile = jnp.sum(jnp.where(slot_match, tile_range, 0), axis=2)
    slot_idx = jnp.where(
        jnp.any(slot_match, axis=2)[:, :, None],
        slot_tile[:, :, None] * unit_span + unit_range,
        ntile * unit_span + shards,
    ).reshape(shards, -1)
    back_idx = jnp.concatenate(
        [slot_idx, ntile * unit_span + jnp.arange(shards, dtype=jnp.int32)[:, None]], axis=1
    )
    returned = lax.all_to_all(
        jnp.take(term_units, back_idx.reshape(-1), axis=0, mode="clip").reshape(shards, -1, kwidth),
        "seq",
        0,
        0,
        tiled=True,
    )
    random_back = returned[:, : capacity * block_rows].reshape(shards * capacity, 2, BLK, kwidth)
    global_sum = jnp.sum(returned[:, capacity * block_rows :].astype(jnp.float32), axis=0)
    global_sum = global_sum.astype(jnp.bfloat16)
    global_total = lax.all_to_all(
        jnp.broadcast_to(global_sum[None], (shards,) + global_sum.shape), "seq", 0, 0, tiled=True
    ).reshape(GLOB, 2, BLK, kwidth).astype(jnp.float32)
    onehot = (
        slot_used.reshape(-1)[None, :]
        & (serve_block.reshape(-1)[None, :] == block_range[:, None])
    ).astype(jnp.bfloat16)
    kv_sum = local_sum + jnp.einsum(
        "qf,fxsk->qxsk", onehot, random_back, preferred_element_type=jnp.float32
    )
    kv_sum = kv_sum.at[nb - 1].add(from_after[0].astype(jnp.float32))
    kv_sum = kv_sum.at[0].add(from_before[0].astype(jnp.float32))
    global_pick = (
        (global_ids[:, None] // query_blocks == this_shard)
        & (global_ids[:, None] % query_blocks == block_range[None, :])
    ).astype(jnp.float32)
    kv_sum = kv_sum + jnp.einsum(
        "gq,gxsk->qxsk", global_pick, global_total, precision=lax.Precision.HIGHEST
    )
    kv_grad = jnp.concatenate(
        [
            kv_sum[:, 0].reshape(shard_tokens, kwidth).astype(jnp.bfloat16),
            kv_sum[:, 1].reshape(shard_tokens, kwidth).astype(jnp.bfloat16),
        ],
        axis=-1,
    )
    handed_query, kv_grad = lax.optimization_barrier((fresh_copy(handed_query), kv_grad))
    handed_kv = from_behind(kv_grad, "section", -1)
    return (
        handed_query,
        handed_kv[None, :, :kwidth],
        handed_kv[None, :, kwidth:],
    )


def solution(mesh):
    in_specs = (
        P("section", "seq", None),
        P("section", "seq", None),
        P("section", "seq", None),
        P("section", "seq", None),
        P("section", None, None),
        P("section", None),
        P("section", None),
    )
    out_specs = (P("section", "seq", None), P("section", "seq", None), P("section", "seq", None))
    return jax.shard_map(body, mesh=mesh, in_specs=in_specs, out_specs=out_specs, check_vma=False)
```

```python
import math

import jax
import jax.numpy as jnp
from jax import lax
from jax.experimental import pallas as pl
from jax.experimental.pallas import tpu as pltpu
from jax.sharding import PartitionSpec as P

HDIM = 128
BLK = 64
GLOB = 2
RAND = 3


def extended_2(array, sides, width):
    for axis, dim in sides:
        devices, length = (lax.axis_size(axis), array.shape[dim])
        up = [(i, (i + 1) % devices) for i in range(devices - 1)]
        down = [(j, i) for i, j in up]
        last = lax.slice_in_dim(array, length - width, length, axis=dim)
        leading = lax.slice_in_dim(array, 0, width, axis=dim)
        before = lax.ppermute(last, axis, up)
        after = lax.ppermute(leading, axis, down)
        array = jnp.concatenate([before, array, after], axis=dim)
    return array


def broadcast(array, axis, root):
    mine = lax.axis_index(axis) == root
    return lax.psum(jnp.where(mine, array, jnp.zeros_like(array)), axis)


def from_behind(block, axis, distance):
    devices = range(lax.axis_size(axis))
    route = [((i - distance) % len(devices), i) for i in devices]
    return lax.ppermute(block, axis, route)


def copy_kernel(src_ref, dst_ref):
    dst_ref[...] = src_ref[...]


def fresh_copy(array):
    rows, width = array.shape[-2:]
    spec = pl.BlockSpec((None, rows, width), lambda i: (0, 0, 0))
    return pl.pallas_call(
        copy_kernel,
        grid=(1,),
        in_specs=[spec],
        out_specs=spec,
        out_shape=jax.ShapeDtypeStruct(array.shape, array.dtype),
        cost_estimate=pl.CostEstimate(flops=0, transcendentals=0, bytes_accessed=2 * array.size * array.dtype.itemsize),
    )(array)


def attention_kernel(ids_ref, q_ref, g_ref, *refs):
    del ids_ref
    ntiles = len(refs) - 7
    tile_refs = refs[:ntiles]
    live_ref = refs[ntiles]
    dq_ref, own_ref, edge_ref, glob_out, rand_ref, glob_ref = refs[ntiles + 1 :]
    nblocks = own_ref.shape[0]
    block_len, width = q_ref.shape
    group = width // HDIM
    near = 3 + GLOB
    b = pl.program_id(1)
    score_scale = 1.0 / math.sqrt(HDIM)
    query = q_ref[...]
    grad = g_ref[...]
    query_rows = jnp.concatenate(
        [query[:, g * HDIM : (g + 1) * HDIM] for g in range(group)], axis=0
    )
    grad_rows = jnp.concatenate([grad[:, g * HDIM : (g + 1) * HDIM] for g in range(group)], axis=0)
    key_rows = jnp.concatenate([tile_refs[t][:block_len] for t in range(ntiles)], axis=0)
    value_rows = jnp.concatenate([tile_refs[t][block_len:] for t in range(ntiles)], axis=0)
    live = live_ref[...] > 0.5
    contract_last = (((1,), (1,)), ((), ()))
    contract_first = (((0,), (0,)), ((), ()))
    scores = (
        lax.dot_general(key_rows, query_rows, contract_last, preferred_element_type=jnp.float32)
        * score_scale
    )
    scores = jnp.where(live, scores, -1e30)
    row_max = jnp.max(scores, axis=0, keepdims=True)
    shifted = jnp.exp(scores - row_max)
    total = jnp.sum(shifted, axis=0, keepdims=True)
    probs = shifted * (1.0 / total)
    probs_low = probs.astype(jnp.bfloat16)
    output = lax.dot_general(
        value_rows, probs_low, contract_first, preferred_element_type=jnp.float32
    )
    grad_cols = grad_rows.astype(jnp.float32).T
    row_dot = jnp.sum(grad_cols * output, axis=0, keepdims=True)
    prob_grad = lax.dot_general(
        value_rows, grad_rows, contract_last, preferred_element_type=jnp.float32
    )
    score_grad = (probs * (prob_grad - row_dot)).astype(jnp.bfloat16)
    query_grad = (
        lax.dot_general(key_rows, score_grad, contract_first, preferred_element_type=jnp.float32)
        * score_scale
    ).T
    key_grad = jnp.dot(score_grad, query_rows, preferred_element_type=jnp.float32) * score_scale
    value_grad = jnp.dot(probs_low, grad_rows, preferred_element_type=jnp.float32)
    for g in range(group):
        dq_ref[:, g * HDIM : (g + 1) * HDIM] = query_grad[g * block_len : (g + 1) * block_len].astype(
            dq_ref.dtype
        )
    terms = jnp.stack(
        [key_grad.reshape(ntiles, block_len, HDIM), value_grad.reshape(ntiles, block_len, HDIM)],
        axis=1,
    )

    @pl.when(b == 0)
    def _():
        own_ref[...] = jnp.zeros_like(own_ref)
        glob_ref[...] = jnp.zeros_like(glob_ref)
        edge_ref[0] = terms[0].astype(edge_ref.dtype)

    @pl.when(b > 0)
    def _():
        before = jnp.maximum(b - 1, 0)
        own_ref[before] = own_ref[before] + terms[0]

    own_ref[b] = own_ref[b] + terms[1]

    @pl.when(b < nblocks - 1)
    def _():
        after = jnp.minimum(b + 1, nblocks - 1)
        own_ref[after] = own_ref[after] + terms[2]

    @pl.when(b == nblocks - 1)
    def _():
        edge_ref[1] = terms[2].astype(edge_ref.dtype)

    glob_ref[...] = glob_ref[...] + terms[3:near]

    @pl.when(b == nblocks - 1)
    def _():
        glob_out[...] = glob_ref[...].astype(glob_out.dtype)
    rand_ref[...] = terms[near:].astype(rand_ref.dtype)


def block_backward(query_rows, grad_rows, window, global_tiles, received, random_ids, key_live):
    shard_tokens, qwidth = query_rows.shape
    kwidth = window.shape[-1]
    nblocks = window.shape[0] - 2
    block_len = window.shape[1] // 2
    near = 3 + GLOB
    nrand = random_ids.shape[0] // (2 * nblocks)
    ntiles = near + nrand
    heads_kv = kwidth // HDIM
    group_width = qwidth // heads_kv
    pair_rows = 2 * block_len
    live = key_live.reshape(nblocks, ntiles * block_len, 1).astype(jnp.float32)
    row_spec = pl.BlockSpec((block_len, group_width), lambda h, b, ids: (b, h))
    tile_specs = [
        pl.BlockSpec((None, pair_rows, HDIM), lambda h, b, ids, t=t: (b + t, 0, h)) for t in range(3)
    ]
    tile_specs += [
        pl.BlockSpec((None, pair_rows, HDIM), lambda h, b, ids, g=g: (g, 0, h)) for g in range(GLOB)
    ]
    tile_specs += [
        pl.BlockSpec(
            (None, pair_rows, HDIM),
            lambda h, b, ids, r=r: (ids[(b * nrand + r) * 2], ids[(b * nrand + r) * 2 + 1], h),
        )
        for r in range(nrand)
    ]
    live_spec = pl.BlockSpec((None, ntiles * block_len, 1), lambda h, b, ids: (b, 0, 0))
    own_spec = pl.BlockSpec((nblocks, 2, block_len, HDIM), lambda h, b, ids: (0, 0, 0, h))
    edge_spec = pl.BlockSpec((2, 2, block_len, HDIM), lambda h, b, ids: (0, 0, 0, h))
    glob_spec = pl.BlockSpec((GLOB, 2, block_len, HDIM), lambda h, b, ids: (0, 0, 0, h))
    rand_spec = pl.BlockSpec((None, nrand, 2, block_len, HDIM), lambda h, b, ids: (b, 0, 0, 0, h))
    flops = 12 * nblocks * heads_kv * (group_width // HDIM) * block_len * ntiles * block_len * HDIM
    grid_spec = pltpu.PrefetchScalarGridSpec(
        num_scalar_prefetch=1,
        grid=(heads_kv, nblocks),
        in_specs=[row_spec, row_spec, *tile_specs, live_spec],
        out_specs=[row_spec, own_spec, edge_spec, glob_spec, rand_spec],
        scratch_shapes=[pltpu.VMEM((GLOB, 2, block_len, HDIM), jnp.float32)],
    )
    outs = pl.pallas_call(
        attention_kernel,
        grid_spec=grid_spec,
        out_shape=[
            jax.ShapeDtypeStruct((shard_tokens, qwidth), jnp.bfloat16),
            jax.ShapeDtypeStruct((nblocks, 2, block_len, kwidth), jnp.float32),
            jax.ShapeDtypeStruct((2, 2, block_len, kwidth), jnp.bfloat16),
            jax.ShapeDtypeStruct((GLOB, 2, block_len, kwidth), jnp.bfloat16),
            jax.ShapeDtypeStruct((nblocks, nrand, 2, block_len, kwidth), jnp.bfloat16),
        ],
        compiler_params=pltpu.CompilerParams(
            dimension_semantics=("arbitrary", "arbitrary")
        ),
        cost_estimate=pl.CostEstimate(
            flops=flops,
            transcendentals=nblocks * qwidth // HDIM * block_len * ntiles * block_len,
            bytes_accessed=shard_tokens * qwidth * 6 + nblocks * ntiles * block_len * kwidth * 6,
        ),
    )(
        random_ids,
        query_rows,
        grad_rows,
        *([window] * 3),
        *([global_tiles] * GLOB),
        *([received] * nrand),
        live,
    )
    return outs


def request_plan(request_lists, this_shard, query_blocks):
    shards, count = request_lists.shape
    capacity = -(-count // shards)
    owner_ids = request_lists // query_blocks
    local_ids = request_lists % query_blocks
    order = jnp.arange(count, dtype=jnp.int32)
    earlier = order[None, :] < order[:, None]
    same_owner = owner_ids[:, :, None] == owner_ids[:, None, :]
    slot_rank = jnp.sum(same_owner & earlier[None], axis=2)
    slot_ids = jnp.arange(capacity, dtype=jnp.int32)
    chosen = (owner_ids[:, None, :] == this_shard) & (
        slot_rank[:, None, :] == slot_ids[None, :, None]
    )
    serve_block = jnp.sum(jnp.where(chosen, local_ids[:, None, :], 0), axis=2)
    slot_used = jnp.any(chosen, axis=2)
    owner_mine = lax.dynamic_index_in_dim(owner_ids, this_shard, 0, keepdims=False)
    rank_mine = lax.dynamic_index_in_dim(slot_rank, this_shard, 0, keepdims=False)
    return (serve_block, slot_used, owner_mine, rank_mine)


def token_live(tile_ids, pad_sizes, query_blocks, shard_tokens, total_blocks):
    valid = (tile_ids >= 0) & (tile_ids < total_blocks)
    safe_ids = jnp.clip(tile_ids, 0, total_blocks - 1)
    owner_shard = safe_ids // query_blocks
    shards = pad_sizes.shape[0]
    pad_of = jnp.sum(
        jnp.where(owner_shard[..., None] == jnp.arange(shards, dtype=jnp.int32), pad_sizes, 0),
        axis=-1,
    )
    within = (safe_ids % query_blocks)[..., None] * BLK + jnp.arange(BLK, dtype=jnp.int32)
    return valid[..., None] & (within < (shard_tokens - pad_of)[..., None])


def body(queries, keys, values, out_grads, random_blocks, global_blocks, pad_lengths):
    query_rows = queries[0]
    key_rows = keys[0]
    value_rows = values[0]
    grad_rows = out_grads[0]
    random_table = random_blocks[0]
    global_ids = global_blocks[0]
    pad_sizes = pad_lengths[0]
    shards = lax.axis_size("seq")
    this_shard = lax.axis_index("seq")
    shard_tokens, qwidth = query_rows.shape
    kwidth = key_rows.shape[1]
    query_blocks = shard_tokens // BLK
    total_blocks = query_blocks * shards
    own_blocks = jnp.stack(
        [key_rows.reshape(query_blocks, BLK, kwidth), value_rows.reshape(query_blocks, BLK, kwidth)],
        axis=1,
    )
    up = [(i, (i + 1) % shards) for i in range(shards - 1)]
    down = [(j, i) for i, j in up]
    edge_before = lax.ppermute(own_blocks[query_blocks - 1 :], "seq", up)
    edge_after = lax.ppermute(own_blocks[:1], "seq", down)
    requests = random_table.reshape(shards, query_blocks * RAND)
    plan = request_plan(requests, this_shard, query_blocks)
    serve_block, slot_used, owner_mine, rank_mine = plan
    capacity = serve_block.shape[1]
    block_rows = 2 * BLK
    nb = query_blocks
    unit_rows = GLOB * block_rows // shards
    unit_span = block_rows // unit_rows
    own_units = jnp.concatenate(
        [
            own_blocks.reshape(nb * unit_span, unit_rows, kwidth),
            jnp.zeros((1, unit_rows, kwidth), own_blocks.dtype),
        ]
    )
    unit_range = jnp.arange(unit_span, dtype=jnp.int32)
    served_idx = (serve_block[:, :, None] * unit_span + unit_range).reshape(shards, -1)
    global_owned = global_ids // query_blocks == this_shard
    global_idx = jnp.where(
        global_owned[:, None],
        (global_ids % query_blocks)[:, None] * unit_span + unit_range,
        nb * unit_span,
    ).reshape(shards, -1)
    payload_idx = jnp.concatenate([served_idx, global_idx], axis=1)
    payload = jnp.take(own_units, payload_idx.reshape(-1), axis=0, mode="clip").reshape(
        shards, -1, kwidth
    )
    received = lax.all_to_all(payload, "seq", 0, 0, tiled=True)
    global_piece = jnp.sum(received[:, capacity * block_rows :], axis=0, dtype=own_blocks.dtype)
    global_tiles = lax.all_to_all(
        jnp.broadcast_to(global_piece[None], (shards,) + global_piece.shape), "seq", 0, 0, tiled=True
    ).reshape(GLOB, block_rows, kwidth)
    window = jnp.concatenate([edge_before, own_blocks, edge_after], axis=0).reshape(
        nb + 2, block_rows, kwidth
    )
    block_range = jnp.arange(nb, dtype=jnp.int32)
    random_ids = jnp.stack(
        [owner_mine, jnp.clip(rank_mine, 0, capacity - 1)], axis=1
    ).reshape(-1)
    random_three = random_table.reshape(shards, query_blocks, RAND)
    base_ids = this_shard * query_blocks + block_range
    window_ids = base_ids[:, None] + jnp.arange(-1, 2, dtype=jnp.int32)[None, :]
    my_random = lax.dynamic_index_in_dim(random_three, this_shard, 0, keepdims=False)
    tile_ids = jnp.concatenate(
        [window_ids, jnp.broadcast_to(global_ids[None, :], (query_blocks, GLOB)), my_random], axis=1
    )
    key_live = token_live(tile_ids, pad_sizes, query_blocks, shard_tokens, total_blocks)
    query_grad, local_sum, edge_terms, global_part, random_part = block_backward(
        query_rows, grad_rows, window, global_tiles, received, random_ids, key_live
    )
    handed_query = from_behind(query_grad[None], "section", -1)
    edge_low = edge_terms.astype(jnp.bfloat16)
    from_after = lax.ppermute(edge_low[:1], "seq", down)
    from_before = lax.ppermute(edge_low[1:], "seq", up)
    ntile = query_blocks * RAND
    global_low = global_part.astype(jnp.bfloat16).reshape(shards, unit_rows, kwidth)
    term_units = jnp.concatenate(
        [
            random_part.reshape(ntile * unit_span, unit_rows, kwidth),
            global_low,
            jnp.zeros((1, unit_rows, kwidth), random_part.dtype),
        ]
    )
    tile_range = jnp.arange(ntile, dtype=jnp.int32)
    slot_match = (owner_mine[None, None, :] == jnp.arange(shards, dtype=jnp.int32)[:, None, None]) & (
        rank_mine[None, None, :] == jnp.arange(capacity, dtype=jnp.int32)[None, :, None]
    )
    slot_tile = jnp.sum(jnp.where(slot_match, tile_range, 0), axis=2)
    slot_idx = jnp.where(
        jnp.any(slot_match, axis=2)[:, :, None],
        slot_tile[:, :, None] * unit_span + unit_range,
        ntile * unit_span + shards,
    ).reshape(shards, -1)
    back_idx = jnp.concatenate(
        [slot_idx, ntile * unit_span + jnp.arange(shards, dtype=jnp.int32)[:, None]], axis=1
    )
    returned = lax.all_to_all(
        jnp.take(term_units, back_idx.reshape(-1), axis=0, mode="clip").reshape(shards, -1, kwidth),
        "seq",
        0,
        0,
        tiled=True,
    )
    random_back = returned[:, : capacity * block_rows].reshape(shards * capacity, 2, BLK, kwidth)
    global_sum = jnp.sum(returned[:, capacity * block_rows :].astype(jnp.float32), axis=0)
    global_sum = global_sum.astype(jnp.bfloat16)
    global_total = lax.all_to_all(
        jnp.broadcast_to(global_sum[None], (shards,) + global_sum.shape), "seq", 0, 0, tiled=True
    ).reshape(GLOB, 2, BLK, kwidth).astype(jnp.float32)
    onehot = (
        slot_used.reshape(-1)[None, :]
        & (serve_block.reshape(-1)[None, :] == block_range[:, None])
    ).astype(jnp.bfloat16)
    kv_sum = local_sum + jnp.einsum(
        "qf,fxsk->qxsk", onehot, random_back, preferred_element_type=jnp.float32
    )
    kv_sum = kv_sum.at[nb - 1].add(from_after[0].astype(jnp.float32))
    kv_sum = kv_sum.at[0].add(from_before[0].astype(jnp.float32))
    global_pick = (
        (global_ids[:, None] // query_blocks == this_shard)
        & (global_ids[:, None] % query_blocks == block_range[None, :])
    ).astype(jnp.float32)
    kv_sum = kv_sum + jnp.einsum(
        "gq,gxsk->qxsk", global_pick, global_total, precision=lax.Precision.HIGHEST
    )
    kv_grad = kv_sum.astype(jnp.bfloat16)
    handed_query, kv_grad = lax.optimization_barrier((fresh_copy(handed_query), kv_grad))
    handed_kv = from_behind(kv_grad, "section", -1)
    return (
        handed_query,
        handed_kv[:, 0].reshape(1, shard_tokens, kwidth),
        handed_kv[:, 1].reshape(1, shard_tokens, kwidth),
    )


def solution(mesh):
    in_specs = (
        P("section", "seq", None),
        P("section", "seq", None),
        P("section", "seq", None),
        P("section", "seq", None),
        P("section", None, None),
        P("section", None),
        P("section", None),
    )
    out_specs = (P("section", "seq", None), P("section", "seq", None), P("section", "seq", None))
    return jax.shard_map(body, mesh=mesh, in_specs=in_specs, out_specs=out_specs, check_vma=False)
```
